32 devices in a mesh: gx: 8 (over z, x), gy: 4 (over y, core).
Axes of the slice: x: 2, y: 2, z: 4, core: 2. Of those that a mesh axis runs over, the one named last changes fastest.
Arguments:
- positions: float32 [8, 4, 72, 3, 128], P('gx', 'gy'), may hold values from -6 to 6
- strength: float32 [8, 4, 72, 3, 128], P('gx', 'gy'), may hold values from -3 to 3
- core: float32 [8, 4, 72, 128], P('gx', 'gy'), may hold values from 0.2 to 1
- moves: int32 [5, 8, 4], replicated, may hold values from 0 to 8, as said below
- owner: int32 [1024], replicated, may hold values from 0 to 1023, as said below
- near_list: int32 [8, 4, 32, 8], P('gx', 'gy'), may hold values from 0 to 1023, as said below
- far_list: int32 [8, 4, 32, 8], P('gx', 'gy'), may hold values from 0 to 1023
Outputs:
- velocity: float32 [8, 4, 32, 3, 128], P('gx', 'gy')
The draws below stay inside these ranges and needn't reach their ends.
Inputs may be any that keep to these rules, and one draw needn't show every extreme that they name: `moves`: no device sends more live blocks than it holds at a level, no device ever holds more than 72 live blocks, and after the last level every device holds exactly 32. `owner`: A permutation of the locations. `near_list`: every entry names a block whose device differs from the target's device by at most one in gx and in gy; over all near lists of one device, exactly 8 entries name blocks of each existing one of its eight neighbouring devices, and all other entries name blocks of the device itself.
All inputs are finite; a program needn't handle non-finite values.
Results may differ from the reference program's by a relative error of at most 0.00002.
Values sent between devices are 32-bit elements; how exact they have to be, the bound alone decides.
No kernel may reach another device: no remote copies, remote signals or barrier semaphores. Data moves between devices by JAX's collectives and lax.ppermute only.
A program may use at most 64 MiB of HBM per device.

```python
import math
import jax
import jax.numpy as jnp
import numpy as np
from jax import lax

BLK = 128
NBD = 32
NP = 8
NM = 8
MOVE = 8
REQ = 8
LX = 3
LEVELS = 5
CAP = 72
NBLK = 1024
N_GX = 8
N_GY = 4


def owner_table(key):
    return jax.random.permutation(jax.random.fold_in(key, 11), NBLK).astype(jnp.int32)


def draw_owner(key, part):
    return owner_table(key)


def draw_moves(key, part):
    after = jnp.full((N_GX, N_GY), NBD, jnp.int32)
    result = [None] * LEVELS
    for level in reversed(range(LEVELS)):
        random_ask = jax.random.randint(jax.random.fold_in(key, 100 + level), (N_GX, N_GY), 0, MOVE + 1).astype(jnp.int32)
        if level == LEVELS - 1:
            random_ask = random_ask.at[0, 0].set(MOVE)
        if level < LX:
            mate_index = jnp.bitwise_xor(jnp.arange(N_GX, dtype=jnp.int32), 1 << LX - 1 - level)
            sending = jnp.minimum(random_ask, after[mate_index, :])
            mate_sending = sending[mate_index, :]
        else:
            mate_index = jnp.bitwise_xor(jnp.arange(N_GY, dtype=jnp.int32), 1 << LEVELS - 1 - level)
            sending = jnp.minimum(random_ask, after[:, mate_index])
            mate_sending = sending[:, mate_index]
        result[level] = sending
        after = after + sending - mate_sending
    return jnp.stack(result, axis=0).astype(jnp.int32)


def draw_near_list(key, part):
    owner = owner_table(key)
    names_at = jnp.zeros((NBLK,), jnp.int32).at[owner].set(jnp.arange(NBLK, dtype=jnp.int32))
    devices_all = N_GX * N_GY
    entries = NBD * NP
    offsets_x = jnp.array([-1, -1, -1, 0, 0, 1, 1, 1], jnp.int32)
    offsets_y = jnp.array([-1, 0, 1, -1, 1, -1, 0, 1], jnp.int32)
    entry_index = jnp.arange(entries, dtype=jnp.int32)
    remote = entry_index < 8 * REQ
    which = jnp.minimum(entry_index // REQ, 7)
    step_x = jnp.where(remote, offsets_x[which], 0)
    step_y = jnp.where(remote, offsets_y[which], 0)
    linear = jnp.arange(devices_all, dtype=jnp.int32)
    home_x = linear // N_GY
    home_y = linear % N_GY
    goal_x = home_x[:, None] + step_x[None, :]
    goal_y = home_y[:, None] + step_y[None, :]
    inside = (goal_x >= 0) & (goal_x < N_GX) & (goal_y >= 0) & (goal_y < N_GY)
    goal_x = jnp.where(inside, goal_x, home_x[:, None])
    goal_y = jnp.where(inside, goal_y, home_y[:, None])
    slots = jax.random.randint(jax.random.fold_in(key, 12), (devices_all, entries), 0, NBD).astype(jnp.int32)
    where_at = (goal_x * N_GY + goal_y) * NBD + slots
    names = names_at[where_at]
    shuffle_keys = jax.random.split(jax.random.fold_in(key, 13), devices_all)
    orders = jax.vmap(lambda one_key: jax.random.permutation(one_key, entries))(shuffle_keys)
    names = jnp.take_along_axis(names, orders.astype(jnp.int32), axis=1)
    return names.reshape(N_GX, N_GY, NBD, NP).astype(jnp.int32)


def set_ends(values, stream_key, low, top_value):
    extent = values.shape
    index_at = [jax.random.randint(jax.random.fold_in(stream_key, axis), (), 0, extent[axis]) for axis in range(len(extent))]
    values = values.at[tuple(index_at)].set(low)
    longest = extent.index(max(extent))
    index_at[longest] = (index_at[longest] + 1) % extent[longest]
    return values.at[tuple(index_at)].set(top_value)


def block_scale(own_key, dims, cuts, low, high):
    level, own = 1.0, jax.random.fold_in(own_key, 6)
    for position, parts in cuts:
        heights = jnp.exp(jax.random.uniform(jax.random.fold_in(own, position), (parts,), jnp.float32, low / len(cuts), high / len(cuts)))
        level = level * jnp.repeat(heights, dims[position] // parts).reshape([-1 if axis == position else 1 for axis in range(len(dims))])
    return level


def centred(rng, shape, scale, reach, cuts=(), kind=jnp.bfloat16):
    values = scale * jax.random.normal(rng, shape, jnp.float32)
    if cuts:
        values = values * block_scale(rng, shape, cuts, -0.22, 0.18)
    return jnp.clip(values, -reach, reach).astype(kind)


def setup_inputs(seed: int = 0) -> dict:
    splits = jax.random.split(jax.random.key(seed), 8)
    return {
        "positions": centred(splits[0], (N_GX, N_GY, CAP, 3, BLK), 1.0, 6.0, ((0, 8), (1, 4)), jnp.float32),
        "strength": centred(splits[1], (N_GX, N_GY, CAP, 3, BLK), 0.5, 3.0, ((0, 8), (1, 4)), jnp.float32),
        "core": jnp.clip(jnp.exp(math.log(1.0) - 1.609438 * jax.random.uniform(splits[2], (N_GX, N_GY, CAP, BLK), jnp.float32) ** block_scale(splits[2], (N_GX, N_GY, CAP, BLK), ((0, 8), (1, 4)), -0.2, 0.2)), 0.2, 1.0),
        "moves": draw_moves(jax.random.fold_in(splits[7], 71), 0),
        "owner": draw_owner(jax.random.fold_in(splits[7], 71), 0),
        "near_list": draw_near_list(jax.random.fold_in(splits[7], 71), 0),
        "far_list": set_ends(jax.random.randint(splits[6], (N_GX, N_GY, NBD, NM), 0, NBLK), jax.random.fold_in(splits[6], 1), 0, NBLK - 1).astype(jnp.int32),
    }


inv_four_pi = 0.25 / math.pi

def multipoles(blocks):
    centre = lax.optimization_barrier(jnp.mean(blocks[:, 0:3], axis=2))
    total = lax.optimization_barrier(jnp.sum(blocks[:, 3:6], axis=2))
    offset = blocks[:, 0:3] - centre[:, :, None]
    spread = lax.optimization_barrier(jnp.mean(blocks[:, 6] * blocks[:, 6], axis=1)) + lax.optimization_barrier(jnp.mean(lax.optimization_barrier(jnp.sum(offset * offset, axis=1)), axis=1))
    return jnp.concatenate([centre, total, spread[:, None]], axis=1)

def evaluate(target, sources, moments):
    sep_x = target[0][None, :, None] - sources[:, 0][:, None, :]
    sep_y = target[1][None, :, None] - sources[:, 1][:, None, :]
    sep_z = target[2][None, :, None] - sources[:, 2][:, None, :]
    radius_sq = sep_x * sep_x + sep_y * sep_y + sep_z * sep_z + (sources[:, 6] * sources[:, 6])[:, None, :]
    weight = 1.0 / (radius_sq * jnp.sqrt(radius_sq))
    str_x = sources[:, 3][:, None, :] * weight
    str_y = sources[:, 4][:, None, :] * weight
    str_z = sources[:, 5][:, None, :] * weight
    near_x = lax.optimization_barrier(jnp.sum(str_y * sep_z - str_z * sep_y, axis=(0, 2)))
    near_y = lax.optimization_barrier(jnp.sum(str_z * sep_x - str_x * sep_z, axis=(0, 2)))
    near_z = lax.optimization_barrier(jnp.sum(str_x * sep_y - str_y * sep_x, axis=(0, 2)))
    off_x = target[0][None, :] - moments[:, 0][:, None]
    off_y = target[1][None, :] - moments[:, 1][:, None]
    off_z = target[2][None, :] - moments[:, 2][:, None]
    far_sq = off_x * off_x + off_y * off_y + off_z * off_z + moments[:, 6][:, None]
    far_weight = 1.0 / (far_sq * jnp.sqrt(far_sq))
    mom_x = moments[:, 3][:, None] * far_weight
    mom_y = moments[:, 4][:, None] * far_weight
    mom_z = moments[:, 5][:, None] * far_weight
    far_x = lax.optimization_barrier(jnp.sum(mom_y * off_z - mom_z * off_y, axis=0))
    far_y = lax.optimization_barrier(jnp.sum(mom_z * off_x - mom_x * off_z, axis=0))
    far_z = lax.optimization_barrier(jnp.sum(mom_x * off_y - mom_y * off_x, axis=0))
    return jnp.stack([near_x + far_x, near_y + far_y, near_z + far_z], axis=0) * inv_four_pi

def take_slots(buffer_in, begin_at):
    return lax.dynamic_slice_in_dim(buffer_in, begin_at, MOVE, 0)

def put_slots(buffer_in, incoming, begin_at):
    return lax.dynamic_update_slice_in_dim(buffer_in, incoming, begin_at, 0)

def reference(positions, strength, core, moves, owner, near_list, far_list):
    devices_all = N_GX * N_GY
    held = jnp.concatenate([positions, strength, core[:, :, :, None, :]], axis=3)
    held = held.reshape(devices_all, CAP, 7, BLK)
    held = jnp.pad(held, ((0, 0), (0, MOVE), (0, 0), (0, 0)))
    flat_moves = moves.reshape(LEVELS, devices_all)
    linear = np.arange(devices_all)
    grid_x = linear // N_GY
    grid_y = linear % N_GY
    mates = []
    for level in range(LEVELS):
        if level < LX:
            mate_x = grid_x ^ 1 << LX - 1 - level
            mates.append(mate_x * N_GY + grid_y)
        else:
            mate_y = grid_y ^ 1 << LEVELS - 1 - level
            mates.append(grid_x * N_GY + mate_y)
    count = jnp.full((devices_all,), NBD, jnp.int32)
    for level in range(LEVELS):
        count = count + flat_moves[level] - flat_moves[level][mates[level]]
    for level in range(LEVELS):
        sending = flat_moves[level]
        leaving = jax.vmap(take_slots)(held, count - sending)
        arriving = leaving[mates[level]]
        count = count - sending
        held = jax.vmap(put_slots)(held, arriving, count)
        count = count + sending[mates[level]]
    blocks = held[:, :NBD].reshape(NBLK, 7, BLK)
    table = multipoles(blocks)
    near_where = owner[near_list.reshape(NBLK, NP)]
    far_where = owner[far_list.reshape(NBLK, NM)]

    def one_block(bundle):
        return evaluate(bundle[0], blocks[bundle[1]], table[bundle[2]])
    velocity = lax.map(one_block, (blocks[:, 0:3], near_where, far_where))
    return velocity.reshape(N_GX, N_GY, NBD, 3, BLK)
```

```python
import math

import jax
import jax.numpy as jnp
import numpy as np
from jax import lax
from jax.sharding import PartitionSpec as P

MOVE = 8


inv_four_pi = 0.25 / math.pi


def from_partner(shard, axis, apart):
    return lax.ppermute(shard, axis, [(i, i ^ 1 << apart) for i in range(lax.axis_size(axis))])


def padded(shard, sides, width):
    for axis, dim in sides:
        size, length = (lax.axis_size(axis), shard.shape[dim])
        up = [(i, (i + 1) % size) for i in range(size - 1)]
        down = [(j, i) for i, j in up]
        last = lax.slice_in_dim(shard, length - width, length, axis=dim)
        first = lax.slice_in_dim(shard, 0, width, axis=dim)
        before = lax.ppermute(last, axis, up)
        after = lax.ppermute(first, axis, down)
        shard = jnp.concatenate([before, shard, after], axis=dim)
    return shard


def slot_multipoles(pos, stren, core):
    centre = jnp.mean(pos, axis=2)
    total = jnp.sum(stren, axis=2)
    offset = pos - centre[:, :, None]
    spread = jnp.mean(core * core, axis=1) + jnp.mean(jnp.sum(offset * offset, axis=1), axis=1)
    return jnp.concatenate([centre, total, spread[:, None]], axis=1)


def evaluate(target, sources, moments):
    sep_x = target[0][None, :, None] - sources[:, 0][:, None, :]
    sep_y = target[1][None, :, None] - sources[:, 1][:, None, :]
    sep_z = target[2][None, :, None] - sources[:, 2][:, None, :]
    radius_sq = (
        sep_x * sep_x + sep_y * sep_y + sep_z * sep_z + (sources[:, 6] * sources[:, 6])[:, None, :]
    )
    weight = 1.0 / (radius_sq * jnp.sqrt(radius_sq))
    str_x = sources[:, 3][:, None, :] * weight
    str_y = sources[:, 4][:, None, :] * weight
    str_z = sources[:, 5][:, None, :] * weight
    near_x = jnp.sum(str_y * sep_z - str_z * sep_y, axis=(0, 2))
    near_y = jnp.sum(str_z * sep_x - str_x * sep_z, axis=(0, 2))
    near_z = jnp.sum(str_x * sep_y - str_y * sep_x, axis=(0, 2))
    off_x = target[0][None, :] - moments[:, 0][:, None]
    off_y = target[1][None, :] - moments[:, 1][:, None]
    off_z = target[2][None, :] - moments[:, 2][:, None]
    far_sq = off_x * off_x + off_y * off_y + off_z * off_z + moments[:, 6][:, None]
    far_weight = 1.0 / (far_sq * jnp.sqrt(far_sq))
    mom_x = moments[:, 3][:, None] * far_weight
    mom_y = moments[:, 4][:, None] * far_weight
    mom_z = moments[:, 5][:, None] * far_weight
    far_x = jnp.sum(mom_y * off_z - mom_z * off_y, axis=0)
    far_y = jnp.sum(mom_z * off_x - mom_x * off_z, axis=0)
    far_z = jnp.sum(mom_x * off_y - mom_y * off_x, axis=0)
    return jnp.stack([near_x + far_x, near_y + far_y, near_z + far_z], axis=0) * inv_four_pi


def evaluate_all(targets, sources_all, moments):
    block_count = targets.shape[0]
    group_size = math.gcd(block_count, 8)
    groups = block_count // group_size

    def one_group(bundle):
        return jax.vmap(evaluate)(bundle[0], bundle[1], bundle[2])

    grouped = (
        targets.reshape((groups, group_size) + targets.shape[1:]),
        sources_all.reshape((groups, group_size) + sources_all.shape[1:]),
        moments.reshape((groups, group_size) + moments.shape[1:]),
    )
    velocity = lax.map(one_group, grouped)
    return velocity.reshape((block_count,) + velocity.shape[2:])


def trace_back(loc, moves, levels, bits_x, size_x, size_y, nbd):
    devices = size_x * size_y
    linear = np.arange(devices)
    grid_x, grid_y = linear // size_y, linear % size_y
    flat = moves.reshape(levels, devices)
    mates = []
    for level in range(levels):
        if level < bits_x:
            mates.append((grid_x ^ 1 << bits_x - 1 - level) * size_y + grid_y)
        else:
            mates.append(grid_x * size_y + (grid_y ^ 1 << levels - 1 - level))
    count = jnp.full((devices,), nbd, jnp.int32)
    for level in range(levels):
        count = count + flat[level] - flat[level][mates[level]]
    kept = []
    for level in range(levels):
        left = count - flat[level]
        kept.append(left)
        count = left + flat[level][mates[level]]
    device = loc // nbd
    slot = loc % nbd
    for level in reversed(range(levels)):
        if level < bits_x:
            bit = 1 << bits_x - 1 - level
            mate = ((device // size_y) ^ bit) * size_y + device % size_y
        else:
            bit = 1 << levels - 1 - level
            mate = (device // size_y) * size_y + ((device % size_y) ^ bit)
        here = kept[level][device]
        there = kept[level][mate]
        moved = slot >= here
        slot = jnp.where(moved, slot - here + there, slot)
        device = jnp.where(moved, mate, device)
    return device, slot


def table_blocks(table, lanes):
    cap, width = table.shape
    pieces = -(-cap // lanes)
    wide = jnp.pad(table.T, ((0, 0), (0, pieces * lanes - cap)))
    return wide.reshape(width, pieces, lanes).transpose(1, 0, 2)


def local(positions, strength, core, moves, owner, near_list, far_list):
    column_index = lax.axis_index("gx")
    row_index = lax.axis_index("gy")
    size_x = lax.axis_size("gx")
    size_y = lax.axis_size("gy")
    bits_x = size_x.bit_length() - 1
    levels = moves.shape[0]
    cap = positions.shape[2]
    nbd = near_list.shape[2]
    lanes = positions.shape[4]
    me = column_index * size_y + row_index
    slot_table = slot_multipoles(positions[0, 0], strength[0, 0], core[0, 0])
    width = slot_table.shape[1]
    gathered = table_blocks(slot_table, lanes)
    pieces = gathered.shape[0]
    far_where = owner[far_list[0, 0]]
    far_device, far_slot = trace_back(far_where, moves, levels, bits_x, size_x, size_y, nbd)
    held = jnp.concatenate([positions[0, 0], strength[0, 0], core[0, 0][:, None, :]], axis=1)
    held = jnp.pad(held, ((0, MOVE), (0, 0), (0, 0)))
    plans = []
    level_bits = []
    for level in range(levels):
        if level < bits_x:
            bit_at = bits_x - 1 - level
            mate_moves = moves[level, jnp.bitwise_xor(column_index, 1 << bit_at), row_index]
            level_bits.append((1 << bit_at) * size_y)
        else:
            bit_at = levels - 1 - level
            mate_moves = moves[level, column_index, jnp.bitwise_xor(row_index, 1 << bit_at)]
            level_bits.append(1 << bit_at)
        plans.append((bit_at, moves[level, column_index, row_index], mate_moves))
    count = jnp.int32(nbd)
    for plan_item in plans:
        count = count + plan_item[1] - plan_item[2]
    for level in range(levels):
        bit_at, own_moves, mate_moves = plans[level]
        leaving = lax.dynamic_slice_in_dim(held, count - own_moves, MOVE, 0)
        payload = jnp.concatenate([leaving, gathered], axis=0)
        if level < bits_x:
            got = from_partner(payload, "gx", bit_at)
        else:
            got = from_partner(payload, "gy", bit_at)
        arriving = got[:MOVE]
        gathered = jnp.concatenate([gathered, got[MOVE:]], axis=0)
        count = count - own_moves
        held = lax.dynamic_update_slice_in_dim(held, arriving, count, 0)
        count = count + mate_moves
    blocks = held[:nbd]
    relative = jnp.bitwise_xor(far_device, me)
    entry = jnp.zeros_like(relative)
    for level in range(levels):
        entry = entry + ((relative // level_bits[level]) % 2) * (1 << level)
    all_table = gathered.reshape(-1, pieces, width, lanes).transpose(0, 1, 3, 2).reshape(-1, width)
    moments = all_table[entry * (pieces * lanes) + far_slot]
    near_where = owner[near_list[0, 0]]
    source_device = near_where // nbd
    source_slot = near_where % nbd
    delta_x = source_device // size_y - column_index
    delta_y = source_device % size_y - row_index
    direction = (delta_x + 1) * 3 + (delta_y + 1)
    grid_blocks = padded(blocks[None, None], (("gx", 0), ("gy", 1)), 1)
    source_pool = grid_blocks.reshape(9 * nbd, 7, blocks.shape[2])
    pool_index = direction * nbd + source_slot
    sources_all = source_pool[pool_index]
    velocity = evaluate_all(blocks[:, 0:3], sources_all, moments)
    return velocity[None, None]


def solution(mesh):
    placed = (
        P("gx", "gy", None, None, None),
        P("gx", "gy", None, None, None),
        P("gx", "gy", None, None),
        P(),
        P(),
        P("gx", "gy", None, None),
        P("gx", "gy", None, None),
    )
    return jax.shard_map(
        local,
        mesh=mesh,
        in_specs=placed,
        out_specs=P("gx", "gy", None, None, None),
        check_vma=False,
    )
```

```python
import math

import jax
import jax.numpy as jnp
import numpy as np
from jax import lax
from jax.sharding import PartitionSpec as P

MOVE = 8


inv_four_pi = 0.25 / math.pi


def from_partner(shard, axis, apart):
    return lax.ppermute(shard, axis, [(i, i ^ 1 << apart) for i in range(lax.axis_size(axis))])


def padded(shard, sides, width):
    for axis, dim in sides:
        size, length = (lax.axis_size(axis), shard.shape[dim])
        up = [(i, (i + 1) % size) for i in range(size - 1)]
        down = [(j, i) for i, j in up]
        last = lax.slice_in_dim(shard, length - width, length, axis=dim)
        first = lax.slice_in_dim(shard, 0, width, axis=dim)
        before = lax.ppermute(last, axis, up)
        after = lax.ppermute(first, axis, down)
        shard = jnp.concatenate([before, shard, after], axis=dim)
    return shard


def slot_multipoles(pos, stren, core):
    centre = jnp.mean(pos, axis=2)
    total = jnp.sum(stren, axis=2)
    offset = pos - centre[:, :, None]
    spread = jnp.mean(core * core, axis=1) + jnp.mean(jnp.sum(offset * offset, axis=1), axis=1)
    return jnp.concatenate([centre, total, spread[:, None]], axis=1)


def evaluate(target, sources, moments):
    sep_x = target[0][None, :, None] - sources[:, 0][:, None, :]
    sep_y = target[1][None, :, None] - sources[:, 1][:, None, :]
    sep_z = target[2][None, :, None] - sources[:, 2][:, None, :]
    radius_sq = (
        sep_x * sep_x + sep_y * sep_y + sep_z * sep_z + (sources[:, 6] * sources[:, 6])[:, None, :]
    )
    weight = 1.0 / (radius_sq * jnp.sqrt(radius_sq))
    str_x = sources[:, 3][:, None, :] * weight
    str_y = sources[:, 4][:, None, :] * weight
    str_z = sources[:, 5][:, None, :] * weight
    near_x = jnp.sum(str_y * sep_z - str_z * sep_y, axis=(0, 2))
    near_y = jnp.sum(str_z * sep_x - str_x * sep_z, axis=(0, 2))
    near_z = jnp.sum(str_x * sep_y - str_y * sep_x, axis=(0, 2))
    off_x = target[0][None, :] - moments[:, 0][:, None]
    off_y = target[1][None, :] - moments[:, 1][:, None]
    off_z = target[2][None, :] - moments[:, 2][:, None]
    far_sq = off_x * off_x + off_y * off_y + off_z * off_z + moments[:, 6][:, None]
    far_weight = 1.0 / (far_sq * jnp.sqrt(far_sq))
    mom_x = moments[:, 3][:, None] * far_weight
    mom_y = moments[:, 4][:, None] * far_weight
    mom_z = moments[:, 5][:, None] * far_weight
    far_x = jnp.sum(mom_y * off_z - mom_z * off_y, axis=0)
    far_y = jnp.sum(mom_z * off_x - mom_x * off_z, axis=0)
    far_z = jnp.sum(mom_x * off_y - mom_y * off_x, axis=0)
    return jnp.stack([near_x + far_x, near_y + far_y, near_z + far_z], axis=0) * inv_four_pi


def evaluate_all(targets, sources_all, moments):
    block_count = targets.shape[0]
    group_size = math.gcd(block_count, 8)
    groups = block_count // group_size

    def one_group(bundle):
        return jax.vmap(evaluate)(bundle[0], bundle[1], bundle[2])

    grouped = (
        targets.reshape((groups, group_size) + targets.shape[1:]),
        sources_all.reshape((groups, group_size) + sources_all.shape[1:]),
        moments.reshape((groups, group_size) + moments.shape[1:]),
    )
    velocity = lax.map(one_group, grouped)
    return velocity.reshape((block_count,) + velocity.shape[2:])


def partner_values(values, level, bits_x, levels):
    size_x, size_y = values.shape
    if level < bits_x:
        step = 1 << bits_x - 1 - level
        split = values.reshape(size_x // (2 * step), 2, step, size_y)
        return split[:, ::-1].reshape(size_x, size_y)
    step = 1 << levels - 1 - level
    split = values.reshape(size_x, size_y // (2 * step), 2, step)
    return split[:, :, ::-1].reshape(size_x, size_y)


def trace_back(loc, moves, levels, bits_x, nbd):
    size_x, size_y = moves.shape[1], moves.shape[2]
    devices = size_x * size_y
    mate_moves = [partner_values(moves[level], level, bits_x, levels) for level in range(levels)]
    count = jnp.full((size_x, size_y), nbd, jnp.int32)
    for level in range(levels):
        count = count + moves[level] - mate_moves[level]
    kept = []
    for level in range(levels):
        left = count - moves[level]
        kept.append(left)
        count = left + mate_moves[level]
    kept_flat = [k.reshape(1, devices) for k in kept]
    kept_mate = [partner_values(k, level, bits_x, levels).reshape(1, devices) for level, k in enumerate(kept)]
    every = jnp.arange(devices, dtype=jnp.int32)[None, :]
    device = loc.reshape(-1) // nbd
    slot = loc.reshape(-1) % nbd
    for level in reversed(range(levels)):
        if level < bits_x:
            bit = (1 << bits_x - 1 - level) * size_y
        else:
            bit = 1 << levels - 1 - level
        mate = jnp.bitwise_xor(device, bit)
        pick = device[:, None] == every
        here = jnp.sum(jnp.where(pick, kept_flat[level], 0), axis=1)
        there = jnp.sum(jnp.where(pick, kept_mate[level], 0), axis=1)
        moved = slot >= here
        slot = jnp.where(moved, slot - here + there, slot)
        device = jnp.where(moved, mate, device)
    return device.reshape(loc.shape), slot.reshape(loc.shape)


def table_blocks(table, lanes):
    cap, width = table.shape
    pieces = -(-cap // lanes)
    wide = jnp.pad(table.T, ((0, 0), (0, pieces * lanes - cap)))
    return wide.reshape(width, pieces, lanes).transpose(1, 0, 2)


def local(positions, strength, core, moves, owner, near_list, far_list):
    column_index = lax.axis_index("gx")
    row_index = lax.axis_index("gy")
    size_x = lax.axis_size("gx")
    size_y = lax.axis_size("gy")
    bits_x = size_x.bit_length() - 1
    levels = moves.shape[0]
    cap = positions.shape[2]
    nbd = near_list.shape[2]
    lanes = positions.shape[4]
    me = column_index * size_y + row_index
    held = jnp.concatenate([positions[0, 0], strength[0, 0], core[0, 0][:, None, :]], axis=1)
    slot_table = slot_multipoles(held[:, 0:3], held[:, 3:6], held[:, 6])
    width = slot_table.shape[1]
    gathered = table_blocks(slot_table, lanes)
    pieces = gathered.shape[0]
    far_where = owner[far_list[0, 0]]
    far_device, far_slot = trace_back(far_where, moves, levels, bits_x, nbd)
    held = jnp.pad(held, ((0, MOVE), (0, 0), (0, 0)))
    plans = []
    level_bits = []
    for level in range(levels):
        if level < bits_x:
            bit_at = bits_x - 1 - level
            mate_moves = moves[level, jnp.bitwise_xor(column_index, 1 << bit_at), row_index]
            level_bits.append((1 << bit_at) * size_y)
        else:
            bit_at = levels - 1 - level
            mate_moves = moves[level, column_index, jnp.bitwise_xor(row_index, 1 << bit_at)]
            level_bits.append(1 << bit_at)
        plans.append((bit_at, moves[level, column_index, row_index], mate_moves))
    count = jnp.int32(nbd)
    for plan_item in plans:
        count = count + plan_item[1] - plan_item[2]
    for level in range(levels):
        bit_at, own_moves, mate_moves = plans[level]
        leaving = lax.dynamic_slice_in_dim(held, count - own_moves, MOVE, 0)
        payload = jnp.concatenate([leaving, gathered], axis=0)
        if level < bits_x:
            got = from_partner(payload, "gx", bit_at)
        else:
            got = from_partner(payload, "gy", bit_at)
        arriving = got[:MOVE]
        gathered = jnp.concatenate([gathered, got[MOVE:]], axis=0)
        count = count - own_moves
        held = lax.dynamic_update_slice_in_dim(held, arriving, count, 0)
        count = count + mate_moves
    blocks = held[:nbd]
    relative = jnp.bitwise_xor(far_device, me)
    entry = jnp.zeros_like(relative)
    for level in range(levels):
        entry = entry + ((relative // level_bits[level]) % 2) * (1 << level)
    all_table = gathered.reshape(-1, pieces, width, lanes).transpose(0, 1, 3, 2).reshape(-1, width)
    moments = all_table[entry * (pieces * lanes) + far_slot]
    near_where = owner[near_list[0, 0]]
    source_device = near_where // nbd
    source_slot = near_where % nbd
    delta_x = source_device // size_y - column_index
    delta_y = source_device % size_y - row_index
    direction = (delta_x + 1) * 3 + (delta_y + 1)
    grid_blocks = padded(blocks[None, None], (("gx", 0), ("gy", 1)), 1)
    source_pool = grid_blocks.reshape(9 * nbd, 7, blocks.shape[2])
    pool_index = direction * nbd + source_slot
    sources_all = source_pool[pool_index]
    velocity = evaluate_all(blocks[:, 0:3], sources_all, moments)
    return velocity[None, None]


def solution(mesh):
    placed = (
        P("gx", "gy", None, None, None),
        P("gx", "gy", None, None, None),
        P("gx", "gy", None, None),
        P(),
        P(),
        P("gx", "gy", None, None),
        P("gx", "gy", None, None),
    )
    return jax.shard_map(
        local,
        mesh=mesh,
        in_specs=placed,
        out_specs=P("gx", "gy", None, None, None),
        check_vma=False,
    )
```

```python
import math

import jax
import jax.numpy as jnp
import numpy as np
from jax import lax
from jax.sharding import PartitionSpec as P

MOVE = 8


inv_four_pi = 0.25 / math.pi


def from_partner(shard, axis, apart):
    return lax.ppermute(shard, axis, [(i, i ^ 1 << apart) for i in range(lax.axis_size(axis))])


def padded(shard, sides, width):
    for axis, dim in sides:
        size, length = (lax.axis_size(axis), shard.shape[dim])
        up = [(i, (i + 1) % size) for i in range(size - 1)]
        down = [(j, i) for i, j in up]
        last = lax.slice_in_dim(shard, length - width, length, axis=dim)
        first = lax.slice_in_dim(shard, 0, width, axis=dim)
        before = lax.ppermute(last, axis, up)
        after = lax.ppermute(first, axis, down)
        shard = jnp.concatenate([before, shard, after], axis=dim)
    return shard


def slot_multipoles(pos, stren, core):
    centre = jnp.mean(pos, axis=2)
    total = jnp.sum(stren, axis=2)
    offset = pos - centre[:, :, None]
    spread = jnp.mean(core * core, axis=1) + jnp.mean(jnp.sum(offset * offset, axis=1), axis=1)
    return jnp.concatenate([centre, total, spread[:, None]], axis=1)


def evaluate(target, sources, moments):
    sep_x = target[0][None, :, None] - sources[:, 0][:, None, :]
    sep_y = target[1][None, :, None] - sources[:, 1][:, None, :]
    sep_z = target[2][None, :, None] - sources[:, 2][:, None, :]
    radius_sq = (
        sep_x * sep_x + sep_y * sep_y + sep_z * sep_z + (sources[:, 6] * sources[:, 6])[:, None, :]
    )
    inverse = lax.rsqrt(radius_sq)
    weight = inverse * inverse * inverse
    str_x = sources[:, 3][:, None, :] * weight
    str_y = sources[:, 4][:, None, :] * weight
    str_z = sources[:, 5][:, None, :] * weight
    near_x = jnp.sum(str_y * sep_z - str_z * sep_y, axis=(0, 2))
    near_y = jnp.sum(str_z * sep_x - str_x * sep_z, axis=(0, 2))
    near_z = jnp.sum(str_x * sep_y - str_y * sep_x, axis=(0, 2))
    off_x = target[0][None, :] - moments[:, 0][:, None]
    off_y = target[1][None, :] - moments[:, 1][:, None]
    off_z = target[2][None, :] - moments[:, 2][:, None]
    far_sq = off_x * off_x + off_y * off_y + off_z * off_z + moments[:, 6][:, None]
    far_inverse = lax.rsqrt(far_sq)
    far_weight = far_inverse * far_inverse * far_inverse
    mom_x = moments[:, 3][:, None] * far_weight
    mom_y = moments[:, 4][:, None] * far_weight
    mom_z = moments[:, 5][:, None] * far_weight
    far_x = jnp.sum(mom_y * off_z - mom_z * off_y, axis=0)
    far_y = jnp.sum(mom_z * off_x - mom_x * off_z, axis=0)
    far_z = jnp.sum(mom_x * off_y - mom_y * off_x, axis=0)
    return jnp.stack([near_x + far_x, near_y + far_y, near_z + far_z], axis=0) * inv_four_pi


def evaluate_all(targets, sources_all, moments):
    block_count = targets.shape[0]
    group_size = math.gcd(block_count, 8)
    groups = block_count // group_size

    def one_group(bundle):
        return jax.vmap(evaluate)(bundle[0], bundle[1], bundle[2])

    grouped = (
        targets.reshape((groups, group_size) + targets.shape[1:]),
        sources_all.reshape((groups, group_size) + sources_all.shape[1:]),
        moments.reshape((groups, group_size) + moments.shape[1:]),
    )
    velocity = lax.map(one_group, grouped)
    return velocity.reshape((block_count,) + velocity.shape[2:])


def partner_values(values, level, bits_x, levels):
    size_x, size_y = values.shape
    if level < bits_x:
        step = 1 << bits_x - 1 - level
        split = values.reshape(size_x // (2 * step), 2, step, size_y)
        return split[:, ::-1].reshape(size_x, size_y)
    step = 1 << levels - 1 - level
    split = values.reshape(size_x, size_y // (2 * step), 2, step)
    return split[:, :, ::-1].reshape(size_x, size_y)


def trace_back(loc, moves, levels, bits_x, nbd):
    size_x, size_y = moves.shape[1], moves.shape[2]
    devices = size_x * size_y
    mate_moves = [partner_values(moves[level], level, bits_x, levels) for level in range(levels)]
    count = jnp.full((size_x, size_y), nbd, jnp.int32)
    for level in range(levels):
        count = count + moves[level] - mate_moves[level]
    kept = []
    for level in range(levels):
        left = count - moves[level]
        kept.append(left)
        count = left + mate_moves[level]
    kept_flat = [k.reshape(1, devices) for k in kept]
    kept_mate = [partner_values(k, level, bits_x, levels).reshape(1, devices) for level, k in enumerate(kept)]
    every = jnp.arange(devices, dtype=jnp.int32)[None, :]
    device = loc.reshape(-1) // nbd
    slot = loc.reshape(-1) % nbd
    for level in reversed(range(levels)):
        if level < bits_x:
            bit = (1 << bits_x - 1 - level) * size_y
        else:
            bit = 1 << levels - 1 - level
        mate = jnp.bitwise_xor(device, bit)
        pick = device[:, None] == every
        here = jnp.sum(jnp.where(pick, kept_flat[level], 0), axis=1)
        there = jnp.sum(jnp.where(pick, kept_mate[level], 0), axis=1)
        moved = slot >= here
        slot = jnp.where(moved, slot - here + there, slot)
        device = jnp.where(moved, mate, device)
    return device.reshape(loc.shape), slot.reshape(loc.shape)


def table_blocks(table, lanes):
    cap, width = table.shape
    pieces = -(-cap // lanes)
    wide = jnp.pad(table.T, ((0, 0), (0, pieces * lanes - cap)))
    return wide.reshape(width, pieces, lanes).transpose(1, 0, 2)


def local(positions, strength, core, moves, owner, near_list, far_list):
    column_index = lax.axis_index("gx")
    row_index = lax.axis_index("gy")
    size_x = lax.axis_size("gx")
    size_y = lax.axis_size("gy")
    bits_x = size_x.bit_length() - 1
    levels = moves.shape[0]
    cap = positions.shape[2]
    nbd = near_list.shape[2]
    lanes = positions.shape[4]
    me = column_index * size_y + row_index
    held = jnp.concatenate([positions[0, 0], strength[0, 0], core[0, 0][:, None, :]], axis=1)
    slot_table = slot_multipoles(held[:, 0:3], held[:, 3:6], held[:, 6])
    width = slot_table.shape[1]
    gathered = table_blocks(slot_table, lanes)
    pieces = gathered.shape[0]
    far_where = owner[far_list[0, 0]]
    far_device, far_slot = trace_back(far_where, moves, levels, bits_x, nbd)
    held = jnp.pad(held, ((0, MOVE), (0, 0), (0, 0)))
    plans = []
    level_bits = []
    for level in range(levels):
        if level < bits_x:
            bit_at = bits_x - 1 - level
            mate_moves = moves[level, jnp.bitwise_xor(column_index, 1 << bit_at), row_index]
            level_bits.append((1 << bit_at) * size_y)
        else:
            bit_at = levels - 1 - level
            mate_moves = moves[level, column_index, jnp.bitwise_xor(row_index, 1 << bit_at)]
            level_bits.append(1 << bit_at)
        plans.append((bit_at, moves[level, column_index, row_index], mate_moves))
    count = jnp.int32(nbd)
    for plan_item in plans:
        count = count + plan_item[1] - plan_item[2]
    for level in range(levels):
        bit_at, own_moves, mate_moves = plans[level]
        leaving = lax.dynamic_slice_in_dim(held, count - own_moves, MOVE, 0)
        payload = jnp.concatenate([leaving, gathered], axis=0)
        if level < bits_x:
            got = from_partner(payload, "gx", bit_at)
        else:
            got = from_partner(payload, "gy", bit_at)
        arriving = got[:MOVE]
        gathered = jnp.concatenate([gathered, got[MOVE:]], axis=0)
        count = count - own_moves
        held = lax.dynamic_update_slice_in_dim(held, arriving, count, 0)
        count = count + mate_moves
    blocks = held[:nbd]
    relative = jnp.bitwise_xor(far_device, me)
    entry = jnp.zeros_like(relative)
    for level in range(levels):
        entry = entry + ((relative // level_bits[level]) % 2) * (1 << level)
    all_table = gathered.reshape(-1, pieces, width, lanes).transpose(0, 1, 3, 2).reshape(-1, width)
    moments = all_table[entry * (pieces * lanes) + far_slot]
    near_where = owner[near_list[0, 0]]
    source_device = near_where // nbd
    source_slot = near_where % nbd
    delta_x = source_device // size_y - column_index
    delta_y = source_device % size_y - row_index
    direction = (delta_x + 1) * 3 + (delta_y + 1)
    grid_blocks = padded(blocks[None, None], (("gx", 0), ("gy", 1)), 1)
    source_pool = grid_blocks.reshape(9 * nbd, 7, blocks.shape[2])
    pool_index = direction * nbd + source_slot
    sources_all = source_pool[pool_index]
    velocity = jax.vmap(evaluate)(blocks[:, 0:3], sources_all, moments)
    return velocity[None, None]


def solution(mesh):
    placed = (
        P("gx", "gy", None, None, None),
        P("gx", "gy", None, None, None),
        P("gx", "gy", None, None),
        P(),
        P(),
        P("gx", "gy", None, None),
        P("gx", "gy", None, None),
    )
    return jax.shard_map(
        local,
        mesh=mesh,
        in_specs=placed,
        out_specs=P("gx", "gy", None, None, None),
        check_vma=False,
    )
```

```python
import math

import jax
import jax.numpy as jnp
import numpy as np
from jax import lax
from jax.sharding import PartitionSpec as P

MOVE = 8


inv_four_pi = 0.25 / math.pi


def from_partner(shard, axis, apart):
    return lax.ppermute(shard, axis, [(i, i ^ 1 << apart) for i in range(lax.axis_size(axis))])


def padded(shard, sides, width):
    for axis, dim in sides:
        size, length = (lax.axis_size(axis), shard.shape[dim])
        up = [(i, (i + 1) % size) for i in range(size - 1)]
        down = [(j, i) for i, j in up]
        last = lax.slice_in_dim(shard, length - width, length, axis=dim)
        first = lax.slice_in_dim(shard, 0, width, axis=dim)
        before = lax.ppermute(last, axis, up)
        after = lax.ppermute(first, axis, down)
        shard = jnp.concatenate([before, shard, after], axis=dim)
    return shard


def slot_multipoles(pos, stren, core):
    centre = jnp.mean(pos, axis=2)
    total = jnp.sum(stren, axis=2)
    offset = pos - centre[:, :, None]
    spread = jnp.mean(core * core, axis=1) + jnp.mean(jnp.sum(offset * offset, axis=1), axis=1)
    return jnp.concatenate([centre, total, spread[:, None]], axis=1)


def evaluate(target, sources, moments):
    sep_x = target[0][None, :, None] - sources[:, 0][:, None, :]
    sep_y = target[1][None, :, None] - sources[:, 1][:, None, :]
    sep_z = target[2][None, :, None] - sources[:, 2][:, None, :]
    radius_sq = (
        sep_x * sep_x + sep_y * sep_y + sep_z * sep_z + (sources[:, 6] * sources[:, 6])[:, None, :]
    )
    inverse = lax.rsqrt(radius_sq)
    weight = inverse * inverse * inverse
    str_x = sources[:, 3][:, None, :] * weight
    str_y = sources[:, 4][:, None, :] * weight
    str_z = sources[:, 5][:, None, :] * weight
    near_x = jnp.sum(str_y * sep_z - str_z * sep_y, axis=(0, 2))
    near_y = jnp.sum(str_z * sep_x - str_x * sep_z, axis=(0, 2))
    near_z = jnp.sum(str_x * sep_y - str_y * sep_x, axis=(0, 2))
    off_x = target[0][None, :] - moments[:, 0][:, None]
    off_y = target[1][None, :] - moments[:, 1][:, None]
    off_z = target[2][None, :] - moments[:, 2][:, None]
    far_sq = off_x * off_x + off_y * off_y + off_z * off_z + moments[:, 6][:, None]
    far_inverse = lax.rsqrt(far_sq)
    far_weight = far_inverse * far_inverse * far_inverse
    mom_x = moments[:, 3][:, None] * far_weight
    mom_y = moments[:, 4][:, None] * far_weight
    mom_z = moments[:, 5][:, None] * far_weight
    far_x = jnp.sum(mom_y * off_z - mom_z * off_y, axis=0)
    far_y = jnp.sum(mom_z * off_x - mom_x * off_z, axis=0)
    far_z = jnp.sum(mom_x * off_y - mom_y * off_x, axis=0)
    return jnp.stack([near_x + far_x, near_y + far_y, near_z + far_z], axis=0) * inv_four_pi


def evaluate_all(targets, sources_all, moments):
    block_count = targets.shape[0]
    group_size = math.gcd(block_count, 8)
    groups = block_count // group_size

    def one_group(bundle):
        return jax.vmap(evaluate)(bundle[0], bundle[1], bundle[2])

    grouped = (
        targets.reshape((groups, group_size) + targets.shape[1:]),
        sources_all.reshape((groups, group_size) + sources_all.shape[1:]),
        moments.reshape((groups, group_size) + moments.shape[1:]),
    )
    velocity = lax.map(one_group, grouped)
    return velocity.reshape((block_count,) + velocity.shape[2:])


def trace_back(loc, moves, levels, bits_x, nbd):
    size_x, size_y = moves.shape[1], moves.shape[2]
    devices = size_x * size_y
    level_bit = np.array(
        [(1 << bits_x - 1 - level) * size_y if level < bits_x else 1 << levels - 1 - level for level in range(levels)],
        np.int32,
    )
    flat = moves.reshape(levels, devices)
    every = jnp.arange(devices, dtype=jnp.int32)
    swap = jnp.bitwise_xor(every[None, :, None], level_bit[:, None, None]) == every[None, None, :]
    mate_moves = jnp.sum(jnp.where(swap, flat[:, None, :], 0), axis=2)
    delta = flat - mate_moves
    before = nbd + jnp.sum(delta, axis=0)
    kept = []
    for level in range(levels):
        kept.append(before - flat[level])
        before = before - delta[level]
    kept = jnp.stack(kept, axis=0)
    kept_mate = jnp.sum(jnp.where(swap, kept[:, None, :], 0), axis=2)
    device = loc.reshape(-1) // nbd
    slot = loc.reshape(-1) % nbd
    for level in reversed(range(levels)):
        pick = device[:, None] == every[None, :]
        here = jnp.sum(jnp.where(pick, kept[level][None, :], 0), axis=1)
        there = jnp.sum(jnp.where(pick, kept_mate[level][None, :], 0), axis=1)
        moved = slot >= here
        slot = jnp.where(moved, slot - here + there, slot)
        device = jnp.where(moved, jnp.bitwise_xor(device, level_bit[level]), device)
    return device.reshape(loc.shape), slot.reshape(loc.shape)


def table_blocks(table, lanes):
    cap, width = table.shape
    pieces = -(-cap // lanes)
    wide = jnp.pad(table.T, ((0, 0), (0, pieces * lanes - cap)))
    return wide.reshape(width, pieces, lanes).transpose(1, 0, 2)


def local(positions, strength, core, moves, owner, near_list, far_list):
    column_index = lax.axis_index("gx")
    row_index = lax.axis_index("gy")
    size_x = lax.axis_size("gx")
    size_y = lax.axis_size("gy")
    bits_x = size_x.bit_length() - 1
    levels = moves.shape[0]
    cap = positions.shape[2]
    nbd = near_list.shape[2]
    lanes = positions.shape[4]
    me = column_index * size_y + row_index
    held = jnp.concatenate([positions[0, 0], strength[0, 0], core[0, 0][:, None, :]], axis=1)
    slot_table = slot_multipoles(held[:, 0:3], held[:, 3:6], held[:, 6])
    width = slot_table.shape[1]
    gathered = table_blocks(slot_table, lanes)
    pieces = gathered.shape[0]
    far_where = owner[far_list[0, 0]]
    far_device, far_slot = trace_back(far_where, moves, levels, bits_x, nbd)
    held = jnp.pad(held, ((0, MOVE), (0, 0), (0, 0)))
    plans = []
    level_bits = []
    for level in range(levels):
        if level < bits_x:
            bit_at = bits_x - 1 - level
            mate_moves = moves[level, jnp.bitwise_xor(column_index, 1 << bit_at), row_index]
            level_bits.append((1 << bit_at) * size_y)
        else:
            bit_at = levels - 1 - level
            mate_moves = moves[level, column_index, jnp.bitwise_xor(row_index, 1 << bit_at)]
            level_bits.append(1 << bit_at)
        plans.append((bit_at, moves[level, column_index, row_index], mate_moves))
    count = jnp.int32(nbd)
    for plan_item in plans:
        count = count + plan_item[1] - plan_item[2]
    for level in range(levels):
        bit_at, own_moves, mate_moves = plans[level]
        leaving = lax.dynamic_slice_in_dim(held, count - own_moves, MOVE, 0)
        payload = jnp.concatenate([leaving, gathered], axis=0)
        if level < bits_x:
            got = from_partner(payload, "gx", bit_at)
        else:
            got = from_partner(payload, "gy", bit_at)
        arriving = got[:MOVE]
        gathered = jnp.concatenate([gathered, got[MOVE:]], axis=0)
        count = count - own_moves
        held = lax.dynamic_update_slice_in_dim(held, arriving, count, 0)
        count = count + mate_moves
    blocks = held[:nbd]
    relative = jnp.bitwise_xor(far_device, me)
    entry = jnp.zeros_like(relative)
    for level in range(levels):
        entry = entry + ((relative // level_bits[level]) % 2) * (1 << level)
    all_table = gathered.reshape(-1, pieces, width, lanes).transpose(0, 1, 3, 2).reshape(-1, width)
    moments = all_table[entry * (pieces * lanes) + far_slot]
    near_where = owner[near_list[0, 0]]
    source_device = near_where // nbd
    source_slot = near_where % nbd
    delta_x = source_device // size_y - column_index
    delta_y = source_device % size_y - row_index
    direction = (delta_x + 1) * 3 + (delta_y + 1)
    grid_blocks = padded(blocks[None, None], (("gx", 0), ("gy", 1)), 1)
    source_pool = grid_blocks.reshape(9 * nbd, 7, blocks.shape[2])
    pool_index = direction * nbd + source_slot
    sources_all = source_pool[pool_index]
    velocity = jax.vmap(evaluate)(blocks[:, 0:3], sources_all, moments)
    return velocity[None, None]


def solution(mesh):
    placed = (
        P("gx", "gy", None, None, None),
        P("gx", "gy", None, None, None),
        P("gx", "gy", None, None),
        P(),
        P(),
        P("gx", "gy", None, None),
        P("gx", "gy", None, None),
    )
    return jax.shard_map(
        local,
        mesh=mesh,
        in_specs=placed,
        out_specs=P("gx", "gy", None, None, None),
        check_vma=False,
    )
```

```python
import math

import jax
import jax.numpy as jnp
import numpy as np
from jax import lax
from jax.sharding import PartitionSpec as P

MOVE = 8


inv_four_pi = 0.25 / math.pi


def from_partner(shard, axis, apart):
    return lax.ppermute(shard, axis, [(i, i ^ 1 << apart) for i in range(lax.axis_size(axis))])


def padded(shard, sides, width):
    for axis, dim in sides:
        size, length = (lax.axis_size(axis), shard.shape[dim])
        up = [(i, (i + 1) % size) for i in range(size - 1)]
        down = [(j, i) for i, j in up]
        last = lax.slice_in_dim(shard, length - width, length, axis=dim)
        first = lax.slice_in_dim(shard, 0, width, axis=dim)
        before = lax.ppermute(last, axis, up)
        after = lax.ppermute(first, axis, down)
        shard = jnp.concatenate([before, shard, after], axis=dim)
    return shard


def slot_multipoles(pos, stren, core):
    centre = jnp.mean(pos, axis=2)
    total = jnp.sum(stren, axis=2)
    offset = pos - centre[:, :, None]
    spread = jnp.mean(core * core, axis=1) + jnp.mean(jnp.sum(offset * offset, axis=1), axis=1)
    return jnp.concatenate([centre, total, spread[:, None]], axis=1)


def evaluate(target, sources, moments):
    sep_x = target[0][None, :, None] - sources[:, 0][:, None, :]
    sep_y = target[1][None, :, None] - sources[:, 1][:, None, :]
    sep_z = target[2][None, :, None] - sources[:, 2][:, None, :]
    radius_sq = (
        sep_x * sep_x + sep_y * sep_y + sep_z * sep_z + (sources[:, 6] * sources[:, 6])[:, None, :]
    )
    inverse = lax.rsqrt(radius_sq)
    weight = inverse * inverse * inverse
    str_x = sources[:, 3][:, None, :] * weight
    str_y = sources[:, 4][:, None, :] * weight
    str_z = sources[:, 5][:, None, :] * weight
    near_x = jnp.sum(str_y * sep_z - str_z * sep_y, axis=(0, 2))
    near_y = jnp.sum(str_z * sep_x - str_x * sep_z, axis=(0, 2))
    near_z = jnp.sum(str_x * sep_y - str_y * sep_x, axis=(0, 2))
    off_x = target[0][None, :] - moments[:, 0][:, None]
    off_y = target[1][None, :] - moments[:, 1][:, None]
    off_z = target[2][None, :] - moments[:, 2][:, None]
    far_sq = off_x * off_x + off_y * off_y + off_z * off_z + moments[:, 6][:, None]
    far_inverse = lax.rsqrt(far_sq)
    far_weight = far_inverse * far_inverse * far_inverse
    mom_x = moments[:, 3][:, None] * far_weight
    mom_y = moments[:, 4][:, None] * far_weight
    mom_z = moments[:, 5][:, None] * far_weight
    far_x = jnp.sum(mom_y * off_z - mom_z * off_y, axis=0)
    far_y = jnp.sum(mom_z * off_x - mom_x * off_z, axis=0)
    far_z = jnp.sum(mom_x * off_y - mom_y * off_x, axis=0)
    return jnp.stack([near_x + far_x, near_y + far_y, near_z + far_z], axis=0) * inv_four_pi


def evaluate_all(targets, sources_all, moments):
    block_count = targets.shape[0]
    group_size = math.gcd(block_count, 8)
    groups = block_count // group_size

    def one_group(bundle):
        return jax.vmap(evaluate)(bundle[0], bundle[1], bundle[2])

    grouped = (
        targets.reshape((groups, group_size) + targets.shape[1:]),
        sources_all.reshape((groups, group_size) + sources_all.shape[1:]),
        moments.reshape((groups, group_size) + moments.shape[1:]),
    )
    velocity = lax.map(one_group, grouped)
    return velocity.reshape((block_count,) + velocity.shape[2:])


def trace_back(loc, moves, levels, bits_x, nbd):
    size_x, size_y = moves.shape[1], moves.shape[2]
    devices = size_x * size_y
    level_bit = np.array(
        [(1 << bits_x - 1 - level) * size_y if level < bits_x else 1 << levels - 1 - level for level in range(levels)],
        np.int32,
    )
    flat = moves.reshape(levels, devices)
    every = jnp.arange(devices, dtype=jnp.int32)
    swap = jnp.bitwise_xor(every[None, :, None], level_bit[:, None, None]) == every[None, None, :]
    mate_moves = jnp.sum(jnp.where(swap, flat[:, None, :], 0), axis=2)
    delta = flat - mate_moves
    before = nbd + jnp.sum(delta, axis=0)
    kept = []
    for level in range(levels):
        kept.append(before - flat[level])
        before = before - delta[level]
    kept = jnp.stack(kept, axis=0)
    kept_mate = jnp.sum(jnp.where(swap, kept[:, None, :], 0), axis=2)
    device = loc.reshape(-1) // nbd
    slot = loc.reshape(-1) % nbd
    for level in reversed(range(levels)):
        pick = device[:, None] == every[None, :]
        here = jnp.sum(jnp.where(pick, kept[level][None, :], 0), axis=1)
        there = jnp.sum(jnp.where(pick, kept_mate[level][None, :], 0), axis=1)
        moved = slot >= here
        slot = jnp.where(moved, slot - here + there, slot)
        device = jnp.where(moved, jnp.bitwise_xor(device, level_bit[level]), device)
    return device.reshape(loc.shape), slot.reshape(loc.shape)


def table_blocks(table, lanes):
    cap, width = table.shape
    pieces = -(-cap // lanes)
    wide = jnp.pad(table.T, ((0, 0), (0, pieces * lanes - cap)))
    return wide.reshape(width, pieces, lanes).transpose(1, 0, 2)


def local(positions, strength, core, moves, owner, near_list, far_list):
    column_index = lax.axis_index("gx")
    row_index = lax.axis_index("gy")
    size_x = lax.axis_size("gx")
    size_y = lax.axis_size("gy")
    bits_x = size_x.bit_length() - 1
    levels = moves.shape[0]
    cap = positions.shape[2]
    nbd = near_list.shape[2]
    lanes = positions.shape[4]
    me = column_index * size_y + row_index
    held = jnp.concatenate([positions[0, 0], strength[0, 0], core[0, 0][:, None, :]], axis=1)
    slot_table = slot_multipoles(held[:, 0:3], held[:, 3:6], held[:, 6])
    width = slot_table.shape[1]
    gathered = table_blocks(slot_table, lanes)
    pieces = gathered.shape[0]
    far_where = owner[far_list[0, 0]]
    far_device, far_slot = trace_back(far_where, moves, levels, bits_x, nbd)
    held = jnp.pad(held, ((0, MOVE), (0, 0), (0, 0)))
    plans = []
    level_bits = []
    for level in range(levels):
        if level < bits_x:
            bit_at = bits_x - 1 - level
            mate_moves = moves[level, jnp.bitwise_xor(column_index, 1 << bit_at), row_index]
            level_bits.append((1 << bit_at) * size_y)
        else:
            bit_at = levels - 1 - level
            mate_moves = moves[level, column_index, jnp.bitwise_xor(row_index, 1 << bit_at)]
            level_bits.append(1 << bit_at)
        plans.append((bit_at, moves[level, column_index, row_index], mate_moves))
    count = jnp.int32(nbd)
    for plan_item in plans:
        count = count + plan_item[1] - plan_item[2]
    slot_ids = jnp.arange(held.shape[0], dtype=jnp.int32)
    move_ids = jnp.arange(MOVE, dtype=jnp.int32)
    for level in range(levels):
        bit_at, own_moves, mate_moves = plans[level]
        take = slot_ids[None, :] == (count - own_moves + move_ids)[:, None]
        leaving = jnp.sum(jnp.where(take[:, :, None, None], held[None], 0.0), axis=1)
        payload = jnp.concatenate([leaving, gathered], axis=0)
        if level < bits_x:
            got = from_partner(payload, "gx", bit_at)
        else:
            got = from_partner(payload, "gy", bit_at)
        arriving = got[:MOVE]
        gathered = jnp.concatenate([gathered, got[MOVE:]], axis=0)
        count = count - own_moves
        put = slot_ids[:, None] == (count + move_ids)[None, :]
        placed = jnp.sum(jnp.where(put[:, :, None, None], arriving[None], 0.0), axis=1)
        held = jnp.where(jnp.any(put, axis=1)[:, None, None], placed, held)
        count = count + mate_moves
    blocks = held[:nbd]
    relative = jnp.bitwise_xor(far_device, me)
    entry = jnp.zeros_like(relative)
    for level in range(levels):
        entry = entry + ((relative // level_bits[level]) % 2) * (1 << level)
    all_table = gathered.reshape(-1, pieces, width, lanes).transpose(0, 1, 3, 2).reshape(-1, width)
    moments = all_table[entry * (pieces * lanes) + far_slot]
    near_where = owner[near_list[0, 0]]
    source_device = near_where // nbd
    source_slot = near_where % nbd
    delta_x = source_device // size_y - column_index
    delta_y = source_device % size_y - row_index
    direction = (delta_x + 1) * 3 + (delta_y + 1)
    grid_blocks = padded(blocks[None, None], (("gx", 0), ("gy", 1)), 1)
    source_pool = grid_blocks.reshape(9 * nbd, 7, blocks.shape[2])
    pool_index = direction * nbd + source_slot
    sources_all = source_pool[pool_index]
    velocity = jax.vmap(evaluate)(blocks[:, 0:3], sources_all, moments)
    return velocity[None, None]


def solution(mesh):
    placed = (
        P("gx", "gy", None, None, None),
        P("gx", "gy", None, None, None),
        P("gx", "gy", None, None),
        P(),
        P(),
        P("gx", "gy", None, None),
        P("gx", "gy", None, None),
    )
    return jax.shard_map(
        local,
        mesh=mesh,
        in_specs=placed,
        out_specs=P("gx", "gy", None, None, None),
        check_vma=False,
    )
```

```python
import math

import jax
import jax.numpy as jnp
import numpy as np
from jax import lax
from jax.sharding import PartitionSpec as P

MOVE = 8


inv_four_pi = 0.25 / math.pi


def from_partner(shard, axis, apart):
    return lax.ppermute(shard, axis, [(i, i ^ 1 << apart) for i in range(lax.axis_size(axis))])


def padded(shard, sides, width):
    for axis, dim in sides:
        size, length = (lax.axis_size(axis), shard.shape[dim])
        up = [(i, (i + 1) % size) for i in range(size - 1)]
        down = [(j, i) for i, j in up]
        last = lax.slice_in_dim(shard, length - width, length, axis=dim)
        first = lax.slice_in_dim(shard, 0, width, axis=dim)
        before = lax.ppermute(last, axis, up)
        after = lax.ppermute(first, axis, down)
        shard = jnp.concatenate([before, shard, after], axis=dim)
    return shard


def slot_multipoles(pos, stren, core):
    centre = jnp.mean(pos, axis=2)
    total = jnp.sum(stren, axis=2)
    offset = pos - centre[:, :, None]
    spread = jnp.mean(core * core, axis=1) + jnp.mean(jnp.sum(offset * offset, axis=1), axis=1)
    return jnp.concatenate([centre, total, spread[:, None]], axis=1)


def evaluate(target, centre, sources, extra, moments):
    sep_x = target[0][None, :, None] - sources[:, 0][:, None, :]
    sep_y = target[1][None, :, None] - sources[:, 1][:, None, :]
    sep_z = target[2][None, :, None] - sources[:, 2][:, None, :]
    radius_sq = sep_x * sep_x + sep_y * sep_y + sep_z * sep_z + extra[:, 0][:, None, :]
    inverse = lax.rsqrt(radius_sq)
    weight = inverse * inverse * inverse
    sum_x = jnp.sum(sources[:, 3][:, None, :] * weight, axis=(0, 2))
    sum_y = jnp.sum(sources[:, 4][:, None, :] * weight, axis=(0, 2))
    sum_z = jnp.sum(sources[:, 5][:, None, :] * weight, axis=(0, 2))
    arm_x = jnp.sum(extra[:, 1][:, None, :] * weight, axis=(0, 2))
    arm_y = jnp.sum(extra[:, 2][:, None, :] * weight, axis=(0, 2))
    arm_z = jnp.sum(extra[:, 3][:, None, :] * weight, axis=(0, 2))
    rel_x = target[0] - centre[0]
    rel_y = target[1] - centre[1]
    rel_z = target[2] - centre[2]
    near_x = sum_y * rel_z - sum_z * rel_y - arm_x
    near_y = sum_z * rel_x - sum_x * rel_z - arm_y
    near_z = sum_x * rel_y - sum_y * rel_x - arm_z
    off_x = target[0][None, :] - moments[:, 0][:, None]
    off_y = target[1][None, :] - moments[:, 1][:, None]
    off_z = target[2][None, :] - moments[:, 2][:, None]
    far_sq = off_x * off_x + off_y * off_y + off_z * off_z + moments[:, 6][:, None]
    far_inverse = lax.rsqrt(far_sq)
    far_weight = far_inverse * far_inverse * far_inverse
    mom_x = moments[:, 3][:, None] * far_weight
    mom_y = moments[:, 4][:, None] * far_weight
    mom_z = moments[:, 5][:, None] * far_weight
    far_x = jnp.sum(mom_y * off_z - mom_z * off_y, axis=0)
    far_y = jnp.sum(mom_z * off_x - mom_x * off_z, axis=0)
    far_z = jnp.sum(mom_x * off_y - mom_y * off_x, axis=0)
    return jnp.stack([near_x + far_x, near_y + far_y, near_z + far_z], axis=0) * inv_four_pi


def source_terms(sources_all, centre):
    px = sources_all[:, :, 0] - centre[:, 0][:, None, None]
    py = sources_all[:, :, 1] - centre[:, 1][:, None, None]
    pz = sources_all[:, :, 2] - centre[:, 2][:, None, None]
    sx, sy, sz = sources_all[:, :, 3], sources_all[:, :, 4], sources_all[:, :, 5]
    core_sq = sources_all[:, :, 6] * sources_all[:, :, 6]
    extra = jnp.stack([core_sq, sy * pz - sz * py, sz * px - sx * pz, sx * py - sy * px], axis=2)
    return lax.optimization_barrier(extra)


def trace_back(loc, moves, levels, bits_x, nbd):
    size_x, size_y = moves.shape[1], moves.shape[2]
    devices = size_x * size_y
    level_bit = np.array(
        [(1 << bits_x - 1 - level) * size_y if level < bits_x else 1 << levels - 1 - level for level in range(levels)],
        np.int32,
    )
    flat = moves.reshape(levels, devices)
    every = jnp.arange(devices, dtype=jnp.int32)
    swap = jnp.bitwise_xor(every[None, :, None], level_bit[:, None, None]) == every[None, None, :]
    mate_moves = jnp.sum(jnp.where(swap, flat[:, None, :], 0), axis=2)
    delta = flat - mate_moves
    before = nbd + jnp.sum(delta, axis=0)
    kept = []
    for level in range(levels):
        kept.append(before - flat[level])
        before = before - delta[level]
    kept = jnp.stack(kept, axis=0)
    kept_mate = jnp.sum(jnp.where(swap, kept[:, None, :], 0), axis=2)
    device = loc.reshape(-1) // nbd
    slot = loc.reshape(-1) % nbd
    for level in reversed(range(levels)):
        pick = device[:, None] == every[None, :]
        here = jnp.sum(jnp.where(pick, kept[level][None, :], 0), axis=1)
        there = jnp.sum(jnp.where(pick, kept_mate[level][None, :], 0), axis=1)
        moved = slot >= here
        slot = jnp.where(moved, slot - here + there, slot)
        device = jnp.where(moved, jnp.bitwise_xor(device, level_bit[level]), device)
    return device.reshape(loc.shape), slot.reshape(loc.shape)


def table_blocks(table, lanes):
    cap, width = table.shape
    pieces = -(-cap // lanes)
    wide = jnp.pad(table.T, ((0, 0), (0, pieces * lanes - cap)))
    return wide.reshape(width, pieces, lanes).transpose(1, 0, 2)


def local(positions, strength, core, moves, owner, near_list, far_list):
    column_index = lax.axis_index("gx")
    row_index = lax.axis_index("gy")
    size_x = lax.axis_size("gx")
    size_y = lax.axis_size("gy")
    bits_x = size_x.bit_length() - 1
    levels = moves.shape[0]
    cap = positions.shape[2]
    nbd = near_list.shape[2]
    lanes = positions.shape[4]
    me = column_index * size_y + row_index
    held = jnp.concatenate([positions[0, 0], strength[0, 0], core[0, 0][:, None, :]], axis=1)
    slot_table = slot_multipoles(held[:, 0:3], held[:, 3:6], held[:, 6])
    width = slot_table.shape[1]
    gathered = table_blocks(slot_table, lanes)
    pieces = gathered.shape[0]
    far_where = owner[far_list[0, 0]]
    far_device, far_slot = trace_back(far_where, moves, levels, bits_x, nbd)
    held = jnp.pad(held, ((0, MOVE), (0, 0), (0, 0)))
    plans = []
    level_bits = []
    for level in range(levels):
        if level < bits_x:
            bit_at = bits_x - 1 - level
            mate_moves = moves[level, jnp.bitwise_xor(column_index, 1 << bit_at), row_index]
            level_bits.append((1 << bit_at) * size_y)
        else:
            bit_at = levels - 1 - level
            mate_moves = moves[level, column_index, jnp.bitwise_xor(row_index, 1 << bit_at)]
            level_bits.append(1 << bit_at)
        plans.append((bit_at, moves[level, column_index, row_index], mate_moves))
    count = jnp.int32(nbd)
    for plan_item in plans:
        count = count + plan_item[1] - plan_item[2]
    for level in range(levels):
        bit_at, own_moves, mate_moves = plans[level]
        leaving = lax.dynamic_slice_in_dim(held, count - own_moves, MOVE, 0)
        payload = jnp.concatenate([leaving, gathered], axis=0)
        if level < bits_x:
            got = from_partner(payload, "gx", bit_at)
        else:
            got = from_partner(payload, "gy", bit_at)
        arriving = got[:MOVE]
        gathered = jnp.concatenate([gathered, got[MOVE:]], axis=0)
        count = count - own_moves
        held = lax.dynamic_update_slice_in_dim(held, arriving, count, 0)
        count = count + mate_moves
    blocks = held[:nbd]
    relative = jnp.bitwise_xor(far_device, me)
    entry = jnp.zeros_like(relative)
    for level in range(levels):
        entry = entry + ((relative // level_bits[level]) % 2) * (1 << level)
    all_table = gathered.reshape(-1, pieces, width, lanes).transpose(0, 1, 3, 2).reshape(-1, width)
    moments = all_table[entry * (pieces * lanes) + far_slot]
    near_where = owner[near_list[0, 0]]
    source_device = near_where // nbd
    source_slot = near_where % nbd
    delta_x = source_device // size_y - column_index
    delta_y = source_device % size_y - row_index
    direction = (delta_x + 1) * 3 + (delta_y + 1)
    grid_blocks = padded(blocks[None, None], (("gx", 0), ("gy", 1)), 1)
    source_pool = grid_blocks.reshape(9 * nbd, 7, blocks.shape[2])
    pool_index = direction * nbd + source_slot
    sources_all = source_pool[pool_index]
    targets = blocks[:, 0:3]
    centre = jnp.mean(targets, axis=2)
    extra = source_terms(sources_all, centre)
    velocity = jax.vmap(evaluate)(targets, centre, sources_all, extra, moments)
    return velocity[None, None]


def solution(mesh):
    placed = (
        P("gx", "gy", None, None, None),
        P("gx", "gy", None, None, None),
        P("gx", "gy", None, None),
        P(),
        P(),
        P("gx", "gy", None, None),
        P("gx", "gy", None, None),
    )
    return jax.shard_map(
        local,
        mesh=mesh,
        in_specs=placed,
        out_specs=P("gx", "gy", None, None, None),
        check_vma=False,
    )
```

```python
import math

import jax
import jax.numpy as jnp
import numpy as np
from jax import lax
from jax.sharding import PartitionSpec as P

MOVE = 8


inv_four_pi = 0.25 / math.pi


def from_partner(shard, axis, apart):
    return lax.ppermute(shard, axis, [(i, i ^ 1 << apart) for i in range(lax.axis_size(axis))])


def shifted(shard, axis, step):
    size = lax.axis_size(axis)
    return lax.ppermute(shard, axis, [(i, i + step) for i in range(size) if 0 <= i + step < size])


def halo_sources(blocks, near_where, column_index, row_index, size_y, nbd):
    column = jnp.concatenate([shifted(blocks, "gx", 1), blocks, shifted(blocks, "gx", -1)], axis=0)
    pool = jnp.concatenate([shifted(column, "gy", 1), column, shifted(column, "gy", -1)], axis=0)
    source_device = near_where // nbd
    delta_x = source_device // size_y - column_index
    delta_y = source_device % size_y - row_index
    pool_index = ((delta_y + 1) * 3 + (delta_x + 1)) * nbd + near_where % nbd
    return pool[pool_index]


def slot_multipoles(pos, stren, core):
    centre = jnp.mean(pos, axis=2)
    total = jnp.sum(stren, axis=2)
    offset = pos - centre[:, :, None]
    spread = jnp.mean(core * core, axis=1) + jnp.mean(jnp.sum(offset * offset, axis=1), axis=1)
    return jnp.concatenate([centre, total, spread[:, None]], axis=1)


def evaluate(target, centre, sources, extra, moments):
    sep_x = target[0][None, :, None] - sources[:, 0][:, None, :]
    sep_y = target[1][None, :, None] - sources[:, 1][:, None, :]
    sep_z = target[2][None, :, None] - sources[:, 2][:, None, :]
    radius_sq = sep_x * sep_x + sep_y * sep_y + sep_z * sep_z + extra[:, 0][:, None, :]
    inverse = lax.rsqrt(radius_sq)
    weight = inverse * inverse * inverse
    sum_x = jnp.sum(sources[:, 3][:, None, :] * weight, axis=(0, 2))
    sum_y = jnp.sum(sources[:, 4][:, None, :] * weight, axis=(0, 2))
    sum_z = jnp.sum(sources[:, 5][:, None, :] * weight, axis=(0, 2))
    arm_x = jnp.sum(extra[:, 1][:, None, :] * weight, axis=(0, 2))
    arm_y = jnp.sum(extra[:, 2][:, None, :] * weight, axis=(0, 2))
    arm_z = jnp.sum(extra[:, 3][:, None, :] * weight, axis=(0, 2))
    rel_x = target[0] - centre[0]
    rel_y = target[1] - centre[1]
    rel_z = target[2] - centre[2]
    near_x = sum_y * rel_z - sum_z * rel_y - arm_x
    near_y = sum_z * rel_x - sum_x * rel_z - arm_y
    near_z = sum_x * rel_y - sum_y * rel_x - arm_z
    off_x = target[0][None, :] - moments[:, 0][:, None]
    off_y = target[1][None, :] - moments[:, 1][:, None]
    off_z = target[2][None, :] - moments[:, 2][:, None]
    far_sq = off_x * off_x + off_y * off_y + off_z * off_z + moments[:, 6][:, None]
    far_inverse = lax.rsqrt(far_sq)
    far_weight = far_inverse * far_inverse * far_inverse
    mom_x = moments[:, 3][:, None] * far_weight
    mom_y = moments[:, 4][:, None] * far_weight
    mom_z = moments[:, 5][:, None] * far_weight
    far_x = jnp.sum(mom_y * off_z - mom_z * off_y, axis=0)
    far_y = jnp.sum(mom_z * off_x - mom_x * off_z, axis=0)
    far_z = jnp.sum(mom_x * off_y - mom_y * off_x, axis=0)
    return jnp.stack([near_x + far_x, near_y + far_y, near_z + far_z], axis=0) * inv_four_pi


def source_terms(sources_all, centre):
    px = sources_all[:, :, 0] - centre[:, 0][:, None, None]
    py = sources_all[:, :, 1] - centre[:, 1][:, None, None]
    pz = sources_all[:, :, 2] - centre[:, 2][:, None, None]
    sx, sy, sz = sources_all[:, :, 3], sources_all[:, :, 4], sources_all[:, :, 5]
    core_sq = sources_all[:, :, 6] * sources_all[:, :, 6]
    extra = jnp.stack([core_sq, sy * pz - sz * py, sz * px - sx * pz, sx * py - sy * px], axis=2)
    return lax.optimization_barrier(extra)


def trace_back(loc, moves, levels, bits_x, nbd):
    size_x, size_y = moves.shape[1], moves.shape[2]
    devices = size_x * size_y
    level_bit = np.array(
        [(1 << bits_x - 1 - level) * size_y if level < bits_x else 1 << levels - 1 - level for level in range(levels)],
        np.int32,
    )
    flat = moves.reshape(levels, devices)
    every = jnp.arange(devices, dtype=jnp.int32)
    swap = jnp.bitwise_xor(every[None, :, None], level_bit[:, None, None]) == every[None, None, :]
    mate_moves = jnp.sum(jnp.where(swap, flat[:, None, :], 0), axis=2)
    delta = flat - mate_moves
    before = nbd + jnp.sum(delta, axis=0)
    kept = []
    for level in range(levels):
        kept.append(before - flat[level])
        before = before - delta[level]
    kept = jnp.stack(kept, axis=0)
    kept_mate = jnp.sum(jnp.where(swap, kept[:, None, :], 0), axis=2)
    device = loc.reshape(-1) // nbd
    slot = loc.reshape(-1) % nbd
    for level in reversed(range(levels)):
        pick = device[:, None] == every[None, :]
        here = jnp.sum(jnp.where(pick, kept[level][None, :], 0), axis=1)
        there = jnp.sum(jnp.where(pick, kept_mate[level][None, :], 0), axis=1)
        moved = slot >= here
        slot = jnp.where(moved, slot - here + there, slot)
        device = jnp.where(moved, jnp.bitwise_xor(device, level_bit[level]), device)
    return device.reshape(loc.shape), slot.reshape(loc.shape)


def table_blocks(table, lanes):
    cap, width = table.shape
    pieces = -(-cap // lanes)
    wide = jnp.pad(table.T, ((0, 0), (0, pieces * lanes - cap)))
    return wide.reshape(width, pieces, lanes).transpose(1, 0, 2)


def local(positions, strength, core, moves, owner, near_list, far_list):
    column_index = lax.axis_index("gx")
    row_index = lax.axis_index("gy")
    size_x = lax.axis_size("gx")
    size_y = lax.axis_size("gy")
    bits_x = size_x.bit_length() - 1
    levels = moves.shape[0]
    cap = positions.shape[2]
    nbd = near_list.shape[2]
    lanes = positions.shape[4]
    me = column_index * size_y + row_index
    held = jnp.concatenate([positions[0, 0], strength[0, 0], core[0, 0][:, None, :]], axis=1)
    slot_table = slot_multipoles(held[:, 0:3], held[:, 3:6], held[:, 6])
    width = slot_table.shape[1]
    gathered = table_blocks(slot_table, lanes)
    pieces = gathered.shape[0]
    both_where = owner[jnp.concatenate([near_list[0, 0], far_list[0, 0]], axis=1)]
    near_where = both_where[:, : near_list.shape[3]]
    far_where = both_where[:, near_list.shape[3] :]
    far_device, far_slot = trace_back(far_where, moves, levels, bits_x, nbd)
    held = jnp.pad(held, ((0, MOVE), (0, 0), (0, 0)))
    plans = []
    level_bits = []
    for level in range(levels):
        if level < bits_x:
            bit_at = bits_x - 1 - level
            mate_moves = moves[level, jnp.bitwise_xor(column_index, 1 << bit_at), row_index]
            level_bits.append((1 << bit_at) * size_y)
        else:
            bit_at = levels - 1 - level
            mate_moves = moves[level, column_index, jnp.bitwise_xor(row_index, 1 << bit_at)]
            level_bits.append(1 << bit_at)
        plans.append((bit_at, moves[level, column_index, row_index], mate_moves))
    count = jnp.int32(nbd)
    for plan_item in plans:
        count = count + plan_item[1] - plan_item[2]
    for level in range(levels):
        bit_at, own_moves, mate_moves = plans[level]
        leaving = lax.dynamic_slice_in_dim(held, count - own_moves, MOVE, 0)
        payload = jnp.concatenate([leaving, gathered], axis=0)
        if level < bits_x:
            got = from_partner(payload, "gx", bit_at)
        else:
            got = from_partner(payload, "gy", bit_at)
        arriving = got[:MOVE]
        gathered = jnp.concatenate([gathered, got[MOVE:]], axis=0)
        count = count - own_moves
        held = lax.dynamic_update_slice_in_dim(held, arriving, count, 0)
        count = count + mate_moves
    blocks = held[:nbd]
    relative = jnp.bitwise_xor(far_device, me)
    entry = jnp.zeros_like(relative)
    for level in range(levels):
        entry = entry + ((relative // level_bits[level]) % 2) * (1 << level)
    all_table = gathered.reshape(-1, pieces, width, lanes).transpose(0, 1, 3, 2).reshape(-1, width)
    moments = all_table[entry * (pieces * lanes) + far_slot]
    sources_all = halo_sources(blocks, near_where, column_index, row_index, size_y, nbd)
    targets = blocks[:, 0:3]
    centre = jnp.mean(targets, axis=2)
    extra = source_terms(sources_all, centre)
    velocity = jax.vmap(evaluate)(targets, centre, sources_all, extra, moments)
    return velocity[None, None]


def solution(mesh):
    placed = (
        P("gx", "gy", None, None, None),
        P("gx", "gy", None, None, None),
        P("gx", "gy", None, None),
        P(),
        P(),
        P("gx", "gy", None, None),
        P("gx", "gy", None, None),
    )
    return jax.shard_map(
        local,
        mesh=mesh,
        in_specs=placed,
        out_specs=P("gx", "gy", None, None, None),
        check_vma=False,
    )
```

```python
import math

import jax
import jax.numpy as jnp
import numpy as np
from jax import lax
from jax.sharding import PartitionSpec as P

MOVE = 8


inv_four_pi = 0.25 / math.pi


def from_partner(shard, axis, apart):
    return lax.ppermute(shard, axis, [(i, i ^ 1 << apart) for i in range(lax.axis_size(axis))])


def padded(shard, sides, width):
    for axis, dim in sides:
        size, length = (lax.axis_size(axis), shard.shape[dim])
        up = [(i, (i + 1) % size) for i in range(size - 1)]
        down = [(j, i) for i, j in up]
        last = lax.slice_in_dim(shard, length - width, length, axis=dim)
        first = lax.slice_in_dim(shard, 0, width, axis=dim)
        before = lax.ppermute(last, axis, up)
        after = lax.ppermute(first, axis, down)
        shard = jnp.concatenate([before, shard, after], axis=dim)
    return shard


def slot_multipoles(pos, stren, core):
    centre = jnp.mean(pos, axis=2)
    total = jnp.sum(stren, axis=2)
    offset = pos - centre[:, :, None]
    spread = jnp.mean(core * core, axis=1) + jnp.mean(jnp.sum(offset * offset, axis=1), axis=1)
    return jnp.concatenate([centre, total, spread[:, None]], axis=1)


def evaluate(target, centre, sources, extra, moments):
    sep_x = target[0][None, :, None] - sources[:, 0][:, None, :]
    sep_y = target[1][None, :, None] - sources[:, 1][:, None, :]
    sep_z = target[2][None, :, None] - sources[:, 2][:, None, :]
    radius_sq = sep_x * sep_x + sep_y * sep_y + sep_z * sep_z + extra[:, 0][:, None, :]
    inverse = lax.rsqrt(radius_sq)
    weight = inverse * inverse * inverse
    sum_x = jnp.sum(sources[:, 3][:, None, :] * weight, axis=(0, 2))
    sum_y = jnp.sum(sources[:, 4][:, None, :] * weight, axis=(0, 2))
    sum_z = jnp.sum(sources[:, 5][:, None, :] * weight, axis=(0, 2))
    arm_x = jnp.sum(extra[:, 1][:, None, :] * weight, axis=(0, 2))
    arm_y = jnp.sum(extra[:, 2][:, None, :] * weight, axis=(0, 2))
    arm_z = jnp.sum(extra[:, 3][:, None, :] * weight, axis=(0, 2))
    rel_x = target[0] - centre[0]
    rel_y = target[1] - centre[1]
    rel_z = target[2] - centre[2]
    near_x = sum_y * rel_z - sum_z * rel_y - arm_x
    near_y = sum_z * rel_x - sum_x * rel_z - arm_y
    near_z = sum_x * rel_y - sum_y * rel_x - arm_z
    off_x = target[0][None, :] - moments[:, 0][:, None]
    off_y = target[1][None, :] - moments[:, 1][:, None]
    off_z = target[2][None, :] - moments[:, 2][:, None]
    far_sq = off_x * off_x + off_y * off_y + off_z * off_z + moments[:, 6][:, None]
    far_inverse = lax.rsqrt(far_sq)
    far_weight = far_inverse * far_inverse * far_inverse
    mom_x = moments[:, 3][:, None] * far_weight
    mom_y = moments[:, 4][:, None] * far_weight
    mom_z = moments[:, 5][:, None] * far_weight
    far_x = jnp.sum(mom_y * off_z - mom_z * off_y, axis=0)
    far_y = jnp.sum(mom_z * off_x - mom_x * off_z, axis=0)
    far_z = jnp.sum(mom_x * off_y - mom_y * off_x, axis=0)
    return jnp.stack([near_x + far_x, near_y + far_y, near_z + far_z], axis=0) * inv_four_pi


def source_terms(sources_all, centre):
    px = sources_all[:, :, 0] - centre[:, 0][:, None, None]
    py = sources_all[:, :, 1] - centre[:, 1][:, None, None]
    pz = sources_all[:, :, 2] - centre[:, 2][:, None, None]
    sx, sy, sz = sources_all[:, :, 3], sources_all[:, :, 4], sources_all[:, :, 5]
    core_sq = sources_all[:, :, 6] * sources_all[:, :, 6]
    extra = jnp.stack([core_sq, sy * pz - sz * py, sz * px - sx * pz, sx * py - sy * px], axis=2)
    return lax.optimization_barrier(extra)


def level_tables(moves, levels, bits_x, nbd):
    size_x, size_y = moves.shape[1], moves.shape[2]
    devices = size_x * size_y
    level_bit = np.array(
        [(1 << bits_x - 1 - level) * size_y if level < bits_x else 1 << levels - 1 - level for level in range(levels)],
        np.int32,
    )
    flat = moves.reshape(levels, devices)
    every = jnp.arange(devices, dtype=jnp.int32)
    swap = jnp.bitwise_xor(every[None, :, None], level_bit[:, None, None]) == every[None, None, :]
    mate_moves = jnp.sum(jnp.where(swap, flat[:, None, :], 0), axis=2)
    delta = flat - mate_moves
    before = nbd + jnp.sum(delta, axis=0)
    kept = []
    for level in range(levels):
        kept.append(before - flat[level])
        before = before - delta[level]
    kept = jnp.stack(kept, axis=0)
    kept_mate = jnp.sum(jnp.where(swap, kept[:, None, :], 0), axis=2)
    return kept, kept_mate, level_bit


def trace_back(loc, kept, kept_mate, level_bit, nbd):
    levels, devices = kept.shape
    every = jnp.arange(devices, dtype=jnp.int32)
    device = loc.reshape(-1) // nbd
    slot = loc.reshape(-1) % nbd
    for level in reversed(range(levels)):
        pick = device[:, None] == every[None, :]
        here = jnp.sum(jnp.where(pick, kept[level][None, :], 0), axis=1)
        there = jnp.sum(jnp.where(pick, kept_mate[level][None, :], 0), axis=1)
        moved = slot >= here
        slot = jnp.where(moved, slot - here + there, slot)
        device = jnp.where(moved, jnp.bitwise_xor(device, level_bit[level]), device)
    return device.reshape(loc.shape), slot.reshape(loc.shape)


def table_blocks(table, lanes):
    cap, width = table.shape
    pieces = -(-cap // lanes)
    wide = jnp.pad(table.T, ((0, 0), (0, pieces * lanes - cap)))
    return wide.reshape(width, pieces, lanes).transpose(1, 0, 2)


def local(positions, strength, core, moves, owner, near_list, far_list):
    column_index = lax.axis_index("gx")
    row_index = lax.axis_index("gy")
    size_x = lax.axis_size("gx")
    size_y = lax.axis_size("gy")
    bits_x = size_x.bit_length() - 1
    levels = moves.shape[0]
    cap = positions.shape[2]
    nbd = near_list.shape[2]
    lanes = positions.shape[4]
    me = column_index * size_y + row_index
    held = jnp.concatenate([positions[0, 0], strength[0, 0], core[0, 0][:, None, :]], axis=1)
    slot_table = slot_multipoles(held[:, 0:3], held[:, 3:6], held[:, 6])
    width = slot_table.shape[1]
    gathered = table_blocks(slot_table, lanes)
    pieces = gathered.shape[0]
    held = jnp.pad(held, ((0, MOVE), (0, 0), (0, 0)))
    plans = []
    level_bits = []
    for level in range(levels):
        if level < bits_x:
            bit_at = bits_x - 1 - level
            mate_moves = moves[level, jnp.bitwise_xor(column_index, 1 << bit_at), row_index]
            level_bits.append((1 << bit_at) * size_y)
        else:
            bit_at = levels - 1 - level
            mate_moves = moves[level, column_index, jnp.bitwise_xor(row_index, 1 << bit_at)]
            level_bits.append(1 << bit_at)
        plans.append((bit_at, moves[level, column_index, row_index], mate_moves))
    count = jnp.int32(nbd)
    for plan_item in plans:
        count = count + plan_item[1] - plan_item[2]
    for level in range(levels):
        bit_at, own_moves, mate_moves = plans[level]
        leaving = lax.dynamic_slice_in_dim(held, count - own_moves, MOVE, 0)
        payload = jnp.concatenate([leaving, gathered], axis=0)
        if level < bits_x:
            got = from_partner(payload, "gx", bit_at)
        else:
            got = from_partner(payload, "gy", bit_at)
        arriving = got[:MOVE]
        gathered = jnp.concatenate([gathered, got[MOVE:]], axis=0)
        count = count - own_moves
        held = lax.dynamic_update_slice_in_dim(held, arriving, count, 0)
        count = count + mate_moves
        if level == 0:
            moves_late, _ = lax.optimization_barrier((moves, held))
            kept, kept_mate, level_bit = level_tables(moves_late, levels, bits_x, nbd)
        if level == min(1, levels - 1):
            near_late, _ = lax.optimization_barrier((near_list[0, 0], held))
            near_where = owner[near_late]
        if level == min(2, levels - 1):
            far_late, _ = lax.optimization_barrier((far_list[0, 0], held))
            far_where = owner[far_late]
            far_device, far_slot = trace_back(far_where, kept, kept_mate, level_bit, nbd)
    blocks = held[:nbd]
    relative = jnp.bitwise_xor(far_device, me)
    entry = jnp.zeros_like(relative)
    for level in range(levels):
        entry = entry + ((relative // level_bits[level]) % 2) * (1 << level)
    all_table = gathered.reshape(-1, pieces, width, lanes).transpose(0, 1, 3, 2).reshape(-1, width)
    moments = all_table[entry * (pieces * lanes) + far_slot]
    source_device = near_where // nbd
    source_slot = near_where % nbd
    delta_x = source_device // size_y - column_index
    delta_y = source_device % size_y - row_index
    direction = (delta_x + 1) * 3 + (delta_y + 1)
    grid_blocks = padded(blocks[None, None], (("gx", 0), ("gy", 1)), 1)
    source_pool = grid_blocks.reshape(9 * nbd, 7, blocks.shape[2])
    pool_index = direction * nbd + source_slot
    sources_all = source_pool[pool_index]
    targets = blocks[:, 0:3]
    centre = jnp.mean(targets, axis=2)
    extra = source_terms(sources_all, centre)
    velocity = jax.vmap(evaluate)(targets, centre, sources_all, extra, moments)
    return velocity[None, None]


def solution(mesh):
    placed = (
        P("gx", "gy", None, None, None),
        P("gx", "gy", None, None, None),
        P("gx", "gy", None, None),
        P(),
        P(),
        P("gx", "gy", None, None),
        P("gx", "gy", None, None),
    )
    return jax.shard_map(
        local,
        mesh=mesh,
        in_specs=placed,
        out_specs=P("gx", "gy", None, None, None),
        check_vma=False,
    )
```

```python
import math

import jax
import jax.numpy as jnp
import numpy as np
from jax import lax
from jax.sharding import PartitionSpec as P

MOVE = 8


inv_four_pi = 0.25 / math.pi


def from_partner(shard, axis, apart):
    return lax.ppermute(shard, axis, [(i, i ^ 1 << apart) for i in range(lax.axis_size(axis))])


def padded(shard, sides, width):
    for axis, dim in sides:
        size, length = (lax.axis_size(axis), shard.shape[dim])
        up = [(i, (i + 1) % size) for i in range(size - 1)]
        down = [(j, i) for i, j in up]
        last = lax.slice_in_dim(shard, length - width, length, axis=dim)
        first = lax.slice_in_dim(shard, 0, width, axis=dim)
        before = lax.ppermute(last, axis, up)
        after = lax.ppermute(first, axis, down)
        shard = jnp.concatenate([before, shard, after], axis=dim)
    return shard


def slot_multipoles(pos, stren, core):
    centre = jnp.mean(pos, axis=2)
    total = jnp.sum(stren, axis=2)
    offset = pos - centre[:, :, None]
    spread = jnp.mean(core * core, axis=1) + jnp.mean(jnp.sum(offset * offset, axis=1), axis=1)
    return jnp.concatenate([centre, total, spread[:, None]], axis=1)


def evaluate(target, centre, sources, extra, moments):
    sep_x = target[0][None, :, None] - sources[:, 0][:, None, :]
    sep_y = target[1][None, :, None] - sources[:, 1][:, None, :]
    sep_z = target[2][None, :, None] - sources[:, 2][:, None, :]
    radius_sq = sep_x * sep_x + sep_y * sep_y + sep_z * sep_z + extra[:, 0][:, None, :]
    inverse = lax.rsqrt(radius_sq)
    weight = inverse * inverse * inverse
    sum_x = jnp.sum(sources[:, 3][:, None, :] * weight, axis=(0, 2))
    sum_y = jnp.sum(sources[:, 4][:, None, :] * weight, axis=(0, 2))
    sum_z = jnp.sum(sources[:, 5][:, None, :] * weight, axis=(0, 2))
    arm_x = jnp.sum(extra[:, 1][:, None, :] * weight, axis=(0, 2))
    arm_y = jnp.sum(extra[:, 2][:, None, :] * weight, axis=(0, 2))
    arm_z = jnp.sum(extra[:, 3][:, None, :] * weight, axis=(0, 2))
    rel_x = target[0] - centre[0]
    rel_y = target[1] - centre[1]
    rel_z = target[2] - centre[2]
    near_x = sum_y * rel_z - sum_z * rel_y - arm_x
    near_y = sum_z * rel_x - sum_x * rel_z - arm_y
    near_z = sum_x * rel_y - sum_y * rel_x - arm_z
    off_x = target[0][None, :] - moments[:, 0][:, None]
    off_y = target[1][None, :] - moments[:, 1][:, None]
    off_z = target[2][None, :] - moments[:, 2][:, None]
    far_sq = off_x * off_x + off_y * off_y + off_z * off_z + moments[:, 6][:, None]
    far_inverse = lax.rsqrt(far_sq)
    far_weight = far_inverse * far_inverse * far_inverse
    mom_x = moments[:, 3][:, None] * far_weight
    mom_y = moments[:, 4][:, None] * far_weight
    mom_z = moments[:, 5][:, None] * far_weight
    far_x = jnp.sum(mom_y * off_z - mom_z * off_y, axis=0)
    far_y = jnp.sum(mom_z * off_x - mom_x * off_z, axis=0)
    far_z = jnp.sum(mom_x * off_y - mom_y * off_x, axis=0)
    return jnp.stack([near_x + far_x, near_y + far_y, near_z + far_z], axis=0) * inv_four_pi


def source_terms(sources_all, centre):
    px = sources_all[:, :, 0] - centre[:, 0][:, None, None]
    py = sources_all[:, :, 1] - centre[:, 1][:, None, None]
    pz = sources_all[:, :, 2] - centre[:, 2][:, None, None]
    sx, sy, sz = sources_all[:, :, 3], sources_all[:, :, 4], sources_all[:, :, 5]
    core_sq = sources_all[:, :, 6] * sources_all[:, :, 6]
    extra = jnp.stack([core_sq, sy * pz - sz * py, sz * px - sx * pz, sx * py - sy * px], axis=2)
    return lax.optimization_barrier(extra)


def level_tables(moves, levels, bits_x, nbd):
    size_x, size_y = moves.shape[1], moves.shape[2]
    devices = size_x * size_y
    level_bit = np.array(
        [(1 << bits_x - 1 - level) * size_y if level < bits_x else 1 << levels - 1 - level for level in range(levels)],
        np.int32,
    )
    flat = moves.reshape(levels, devices)
    every = jnp.arange(devices, dtype=jnp.int32)
    swap = jnp.bitwise_xor(every[None, :, None], level_bit[:, None, None]) == every[None, None, :]
    mate_moves = jnp.sum(jnp.where(swap, flat[:, None, :], 0), axis=2)
    delta = flat - mate_moves
    before = nbd + jnp.sum(delta, axis=0)
    kept = []
    for level in range(levels):
        kept.append(before - flat[level])
        before = before - delta[level]
    kept = jnp.stack(kept, axis=0)
    kept_mate = jnp.sum(jnp.where(swap, kept[:, None, :], 0), axis=2)
    return kept, kept_mate, level_bit


def trace_back(loc, kept, kept_mate, level_bit, nbd):
    levels, devices = kept.shape
    every = jnp.arange(devices, dtype=jnp.int32)
    device = loc.reshape(-1) // nbd
    slot = loc.reshape(-1) % nbd
    for level in reversed(range(levels)):
        pick = device[:, None] == every[None, :]
        here = jnp.sum(jnp.where(pick, kept[level][None, :], 0), axis=1)
        there = jnp.sum(jnp.where(pick, kept_mate[level][None, :], 0), axis=1)
        moved = slot >= here
        slot = jnp.where(moved, slot - here + there, slot)
        device = jnp.where(moved, jnp.bitwise_xor(device, level_bit[level]), device)
    return device.reshape(loc.shape), slot.reshape(loc.shape)


def table_blocks(table, lanes):
    cap, width = table.shape
    pieces = -(-cap // lanes)
    wide = jnp.pad(table.T, ((0, 0), (0, pieces * lanes - cap)))
    return wide.reshape(width, pieces, lanes).transpose(1, 0, 2)


def local(positions, strength, core, moves, owner, near_list, far_list):
    column_index = lax.axis_index("gx")
    row_index = lax.axis_index("gy")
    size_x = lax.axis_size("gx")
    size_y = lax.axis_size("gy")
    bits_x = size_x.bit_length() - 1
    levels = moves.shape[0]
    cap = positions.shape[2]
    nbd = near_list.shape[2]
    lanes = positions.shape[4]
    me = column_index * size_y + row_index
    held = jnp.concatenate([positions[0, 0], strength[0, 0], core[0, 0][:, None, :]], axis=1)
    slot_table = slot_multipoles(held[:, 0:3], held[:, 3:6], held[:, 6])
    width = slot_table.shape[1]
    gathered = table_blocks(slot_table, lanes)
    pieces = gathered.shape[0]
    held = jnp.pad(held, ((0, MOVE), (0, 0), (0, 0)))
    plans = []
    level_bits = []
    for level in range(levels):
        if level < bits_x:
            bit_at = bits_x - 1 - level
            mate_moves = moves[level, jnp.bitwise_xor(column_index, 1 << bit_at), row_index]
            level_bits.append((1 << bit_at) * size_y)
        else:
            bit_at = levels - 1 - level
            mate_moves = moves[level, column_index, jnp.bitwise_xor(row_index, 1 << bit_at)]
            level_bits.append(1 << bit_at)
        plans.append((bit_at, moves[level, column_index, row_index], mate_moves))
    count = jnp.int32(nbd)
    for plan_item in plans:
        count = count + plan_item[1] - plan_item[2]
    devices = size_x * size_y
    flat_moves = moves.reshape(levels, devices)
    every = jnp.arange(devices, dtype=jnp.int32)
    weights = [(every == me).astype(jnp.int32) - (every == jnp.bitwise_xor(me, level_bit)).astype(jnp.int32) for level_bit in level_bits]
    start_all = nbd + sum(jnp.sum(weights[level] * flat_moves[level]) for level in range(levels))
    first_out = start_all - jnp.sum((every == me).astype(jnp.int32) * flat_moves[0])
    slot_ids = jnp.arange(held.shape[0], dtype=jnp.int32)
    take = slot_ids[None, :] == (first_out + jnp.arange(MOVE, dtype=jnp.int32))[:, None]
    first_leaving = jnp.sum(jnp.where(take[:, :, None, None], held[None], 0.0), axis=1)
    for level in range(levels):
        bit_at, own_moves, mate_moves = plans[level]
        if level == 0:
            leaving = first_leaving
        else:
            leaving = lax.dynamic_slice_in_dim(held, count - own_moves, MOVE, 0)
        payload = jnp.concatenate([leaving, gathered], axis=0)
        if level < bits_x:
            got = from_partner(payload, "gx", bit_at)
        else:
            got = from_partner(payload, "gy", bit_at)
        arriving = got[:MOVE]
        gathered = jnp.concatenate([gathered, got[MOVE:]], axis=0)
        count = count - own_moves
        held = lax.dynamic_update_slice_in_dim(held, arriving, count, 0)
        count = count + mate_moves
        if level == 0:
            moves_late, _ = lax.optimization_barrier((moves, held))
            kept, kept_mate, level_bit = level_tables(moves_late, levels, bits_x, nbd)
        if level == min(1, levels - 1):
            near_late, _ = lax.optimization_barrier((near_list[0, 0], held))
            near_where = owner[near_late]
        if level == min(2, levels - 1):
            far_late, _ = lax.optimization_barrier((far_list[0, 0], held))
            far_where = owner[far_late]
            far_device, far_slot = trace_back(far_where, kept, kept_mate, level_bit, nbd)
    blocks = held[:nbd]
    relative = jnp.bitwise_xor(far_device, me)
    entry = jnp.zeros_like(relative)
    for level in range(levels):
        entry = entry + ((relative // level_bits[level]) % 2) * (1 << level)
    all_table = gathered.reshape(-1, pieces, width, lanes).transpose(0, 1, 3, 2).reshape(-1, width)
    moments = all_table[entry * (pieces * lanes) + far_slot]
    source_device = near_where // nbd
    source_slot = near_where % nbd
    delta_x = source_device // size_y - column_index
    delta_y = source_device % size_y - row_index
    direction = (delta_x + 1) * 3 + (delta_y + 1)
    grid_blocks = padded(blocks[None, None], (("gx", 0), ("gy", 1)), 1)
    source_pool = grid_blocks.reshape(9 * nbd, 7, blocks.shape[2])
    pool_index = direction * nbd + source_slot
    sources_all = source_pool[pool_index]
    targets = blocks[:, 0:3]
    centre = jnp.mean(targets, axis=2)
    extra = source_terms(sources_all, centre)
    velocity = jax.vmap(evaluate)(targets, centre, sources_all, extra, moments)
    return velocity[None, None]


def solution(mesh):
    placed = (
        P("gx", "gy", None, None, None),
        P("gx", "gy", None, None, None),
        P("gx", "gy", None, None),
        P(),
        P(),
        P("gx", "gy", None, None),
        P("gx", "gy", None, None),
    )
    return jax.shard_map(
        local,
        mesh=mesh,
        in_specs=placed,
        out_specs=P("gx", "gy", None, None, None),
        check_vma=False,
    )
```

```python
import math

import jax
import jax.numpy as jnp
import numpy as np
from jax import lax
from jax.sharding import PartitionSpec as P

MOVE = 8


inv_four_pi = 0.25 / math.pi


def from_partner(shard, axis, apart):
    return lax.ppermute(shard, axis, [(i, i ^ 1 << apart) for i in range(lax.axis_size(axis))])


def padded(shard, sides, width):
    for axis, dim in sides:
        size, length = (lax.axis_size(axis), shard.shape[dim])
        up = [(i, (i + 1) % size) for i in range(size - 1)]
        down = [(j, i) for i, j in up]
        last = lax.slice_in_dim(shard, length - width, length, axis=dim)
        first = lax.slice_in_dim(shard, 0, width, axis=dim)
        before = lax.ppermute(last, axis, up)
        after = lax.ppermute(first, axis, down)
        shard = jnp.concatenate([before, shard, after], axis=dim)
    return shard


def slot_multipoles(pos, stren, core):
    centre = jnp.mean(pos, axis=2)
    total = jnp.sum(stren, axis=2)
    offset = pos - centre[:, :, None]
    spread = jnp.mean(core * core, axis=1) + jnp.mean(jnp.sum(offset * offset, axis=1), axis=1)
    return jnp.concatenate([centre, total, spread[:, None]], axis=1)


def evaluate(target, centre, sources, extra, moments):
    sep_x = target[0][None, :, None] - sources[:, 0][:, None, :]
    sep_y = target[1][None, :, None] - sources[:, 1][:, None, :]
    sep_z = target[2][None, :, None] - sources[:, 2][:, None, :]
    radius_sq = sep_x * sep_x + sep_y * sep_y + sep_z * sep_z + extra[:, 0][:, None, :]
    inverse = lax.rsqrt(radius_sq)
    weight = inverse * inverse * inverse
    sum_x = jnp.sum(sources[:, 3][:, None, :] * weight, axis=(0, 2))
    sum_y = jnp.sum(sources[:, 4][:, None, :] * weight, axis=(0, 2))
    sum_z = jnp.sum(sources[:, 5][:, None, :] * weight, axis=(0, 2))
    arm_x = jnp.sum(extra[:, 1][:, None, :] * weight, axis=(0, 2))
    arm_y = jnp.sum(extra[:, 2][:, None, :] * weight, axis=(0, 2))
    arm_z = jnp.sum(extra[:, 3][:, None, :] * weight, axis=(0, 2))
    rel_x = target[0] - centre[0]
    rel_y = target[1] - centre[1]
    rel_z = target[2] - centre[2]
    near_x = sum_y * rel_z - sum_z * rel_y - arm_x
    near_y = sum_z * rel_x - sum_x * rel_z - arm_y
    near_z = sum_x * rel_y - sum_y * rel_x - arm_z
    off_x = target[0][None, :] - moments[:, 0][:, None]
    off_y = target[1][None, :] - moments[:, 1][:, None]
    off_z = target[2][None, :] - moments[:, 2][:, None]
    far_sq = off_x * off_x + off_y * off_y + off_z * off_z + moments[:, 6][:, None]
    far_inverse = lax.rsqrt(far_sq)
    far_weight = far_inverse * far_inverse * far_inverse
    mom_x = moments[:, 3][:, None] * far_weight
    mom_y = moments[:, 4][:, None] * far_weight
    mom_z = moments[:, 5][:, None] * far_weight
    far_x = jnp.sum(mom_y * off_z - mom_z * off_y, axis=0)
    far_y = jnp.sum(mom_z * off_x - mom_x * off_z, axis=0)
    far_z = jnp.sum(mom_x * off_y - mom_y * off_x, axis=0)
    return jnp.stack([near_x + far_x, near_y + far_y, near_z + far_z], axis=0) * inv_four_pi


def source_terms(sources_all, centre):
    px = sources_all[:, :, 0] - centre[:, 0][:, None, None]
    py = sources_all[:, :, 1] - centre[:, 1][:, None, None]
    pz = sources_all[:, :, 2] - centre[:, 2][:, None, None]
    sx, sy, sz = sources_all[:, :, 3], sources_all[:, :, 4], sources_all[:, :, 5]
    core_sq = sources_all[:, :, 6] * sources_all[:, :, 6]
    extra = jnp.stack([core_sq, sy * pz - sz * py, sz * px - sx * pz, sx * py - sy * px], axis=2)
    return lax.optimization_barrier(extra)


def level_tables(moves, levels, bits_x, nbd):
    size_x, size_y = moves.shape[1], moves.shape[2]
    devices = size_x * size_y
    level_bit = np.array(
        [(1 << bits_x - 1 - level) * size_y if level < bits_x else 1 << levels - 1 - level for level in range(levels)],
        np.int32,
    )
    flat = moves.reshape(levels, devices)
    every = jnp.arange(devices, dtype=jnp.int32)
    swap = jnp.bitwise_xor(every[None, :, None], level_bit[:, None, None]) == every[None, None, :]
    mate_moves = jnp.sum(jnp.where(swap, flat[:, None, :], 0), axis=2)
    delta = flat - mate_moves
    before = nbd + jnp.sum(delta, axis=0)
    kept = []
    for level in range(levels):
        kept.append(before - flat[level])
        before = before - delta[level]
    kept = jnp.stack(kept, axis=0)
    kept_mate = jnp.sum(jnp.where(swap, kept[:, None, :], 0), axis=2)
    return kept, kept_mate, level_bit


def trace_back(loc, kept, kept_mate, level_bit, nbd):
    levels, devices = kept.shape
    every = jnp.arange(devices, dtype=jnp.int32)
    device = loc.reshape(-1) // nbd
    slot = loc.reshape(-1) % nbd
    for level in reversed(range(levels)):
        pick = device[:, None] == every[None, :]
        here = jnp.sum(jnp.where(pick, kept[level][None, :], 0), axis=1)
        there = jnp.sum(jnp.where(pick, kept_mate[level][None, :], 0), axis=1)
        moved = slot >= here
        slot = jnp.where(moved, slot - here + there, slot)
        device = jnp.where(moved, jnp.bitwise_xor(device, level_bit[level]), device)
    return device.reshape(loc.shape), slot.reshape(loc.shape)


def table_blocks(table, lanes):
    cap, width = table.shape
    pieces = -(-cap // lanes)
    wide = jnp.pad(table.T, ((0, 0), (0, pieces * lanes - cap)))
    return wide.reshape(width, pieces, lanes).transpose(1, 0, 2)


def local(positions, strength, core, moves, owner, near_list, far_list):
    column_index = lax.axis_index("gx")
    row_index = lax.axis_index("gy")
    size_x = lax.axis_size("gx")
    size_y = lax.axis_size("gy")
    bits_x = size_x.bit_length() - 1
    levels = moves.shape[0]
    cap = positions.shape[2]
    nbd = near_list.shape[2]
    lanes = positions.shape[4]
    me = column_index * size_y + row_index
    held = jnp.concatenate([positions[0, 0], strength[0, 0], core[0, 0][:, None, :]], axis=1)
    slot_table = slot_multipoles(held[:, 0:3], held[:, 3:6], held[:, 6])
    width = slot_table.shape[1]
    gathered = table_blocks(slot_table, lanes)
    pieces = gathered.shape[0]
    held = jnp.pad(held, ((0, MOVE), (0, 0), (0, 0)))
    level_bits = []
    for level in range(levels):
        if level < bits_x:
            level_bits.append((1 << bits_x - 1 - level) * size_y)
        else:
            level_bits.append(1 << levels - 1 - level)
    devices = size_x * size_y
    flat_moves = moves.reshape(levels, devices)
    every = jnp.arange(devices, dtype=jnp.int32)
    mates = jnp.bitwise_xor(me, jnp.array(level_bits, jnp.int32))
    own = jnp.sum(jnp.where(every[None, :] == me, flat_moves, 0), axis=1)
    mate_own = jnp.sum(jnp.where(every[None, :] == mates[:, None], flat_moves, 0), axis=1)
    count = nbd + jnp.sum(own - mate_own, keepdims=True)
    slot_ids = jnp.arange(held.shape[0], dtype=jnp.int32)
    move_ids = jnp.arange(MOVE, dtype=jnp.int32)
    for level in range(levels):
        if level < bits_x:
            axis_name, bit_at = "gx", bits_x - 1 - level
        else:
            axis_name, bit_at = "gy", levels - 1 - level
        count = count - own[level : level + 1]
        take = slot_ids[None, :] == (count + move_ids)[:, None]
        leaving = jnp.sum(jnp.where(take[:, :, None, None], held[None], 0.0), axis=1)
        payload = jnp.concatenate([leaving, gathered], axis=0)
        got = from_partner(payload, axis_name, bit_at)
        arriving = got[:MOVE]
        gathered = jnp.concatenate([gathered, got[MOVE:]], axis=0)
        put = slot_ids[:, None] == (count + move_ids)[None, :]
        placed = jnp.sum(jnp.where(put[:, :, None, None], arriving[None], 0.0), axis=1)
        held = jnp.where(jnp.any(put, axis=1)[:, None, None], placed, held)
        count = count + mate_own[level : level + 1]
        if level == 0:
            moves_late, _ = lax.optimization_barrier((moves, held))
            kept, kept_mate, level_bit = level_tables(moves_late, levels, bits_x, nbd)
        if level == min(1, levels - 1):
            near_late, _ = lax.optimization_barrier((near_list[0, 0], held))
            near_where = owner[near_late]
        if level == min(2, levels - 1):
            far_late, _ = lax.optimization_barrier((far_list[0, 0], held))
            far_where = owner[far_late]
            far_device, far_slot = trace_back(far_where, kept, kept_mate, level_bit, nbd)
    blocks = held[:nbd]
    relative = jnp.bitwise_xor(far_device, me)
    entry = jnp.zeros_like(relative)
    for level in range(levels):
        entry = entry + ((relative // level_bits[level]) % 2) * (1 << level)
    all_table = gathered.reshape(-1, pieces, width, lanes).transpose(0, 1, 3, 2).reshape(-1, width)
    moments = all_table[entry * (pieces * lanes) + far_slot]
    source_device = near_where // nbd
    source_slot = near_where % nbd
    delta_x = source_device // size_y - column_index
    delta_y = source_device % size_y - row_index
    direction = (delta_x + 1) * 3 + (delta_y + 1)
    grid_blocks = padded(blocks[None, None], (("gx", 0), ("gy", 1)), 1)
    source_pool = grid_blocks.reshape(9 * nbd, 7, blocks.shape[2])
    pool_index = direction * nbd + source_slot
    sources_all = source_pool[pool_index]
    targets = blocks[:, 0:3]
    centre = jnp.mean(targets, axis=2)
    extra = source_terms(sources_all, centre)
    velocity = jax.vmap(evaluate)(targets, centre, sources_all, extra, moments)
    return velocity[None, None]


def solution(mesh):
    placed = (
        P("gx", "gy", None, None, None),
        P("gx", "gy", None, None, None),
        P("gx", "gy", None, None),
        P(),
        P(),
        P("gx", "gy", None, None),
        P("gx", "gy", None, None),
    )
    return jax.shard_map(
        local,
        mesh=mesh,
        in_specs=placed,
        out_specs=P("gx", "gy", None, None, None),
        check_vma=False,
    )
```

```python
import math

import jax
import jax.numpy as jnp
import numpy as np
from jax import lax
from jax.sharding import PartitionSpec as P

MOVE = 8


inv_four_pi = 0.25 / math.pi


def from_partner(shard, axis, apart):
    return lax.ppermute(shard, axis, [(i, i ^ 1 << apart) for i in range(lax.axis_size(axis))])


def swapped(shard, axis):
    size = lax.axis_size(axis)
    first = [(i, i ^ 1) for i in range(size)]
    second = [(i, i + 1 - 2 * (i % 2 == 0)) for i in range(1, size - 1)]
    return jnp.concatenate([lax.ppermute(shard, axis, first), shard, lax.ppermute(shard, axis, second)], axis=0)


def slot_multipoles(pos, stren, core):
    centre = jnp.mean(pos, axis=2)
    total = jnp.sum(stren, axis=2)
    offset = pos - centre[:, :, None]
    spread = jnp.mean(core * core, axis=1) + jnp.mean(jnp.sum(offset * offset, axis=1), axis=1)
    return jnp.concatenate([centre, total, spread[:, None]], axis=1)


def evaluate(target, centre, sources, extra, moments):
    sep_x = target[0][None, :, None] - sources[:, 0][:, None, :]
    sep_y = target[1][None, :, None] - sources[:, 1][:, None, :]
    sep_z = target[2][None, :, None] - sources[:, 2][:, None, :]
    radius_sq = sep_x * sep_x + sep_y * sep_y + sep_z * sep_z + extra[:, 0][:, None, :]
    inverse = lax.rsqrt(radius_sq)
    weight = inverse * inverse * inverse
    sum_x = jnp.sum(sources[:, 3][:, None, :] * weight, axis=(0, 2))
    sum_y = jnp.sum(sources[:, 4][:, None, :] * weight, axis=(0, 2))
    sum_z = jnp.sum(sources[:, 5][:, None, :] * weight, axis=(0, 2))
    arm_x = jnp.sum(extra[:, 1][:, None, :] * weight, axis=(0, 2))
    arm_y = jnp.sum(extra[:, 2][:, None, :] * weight, axis=(0, 2))
    arm_z = jnp.sum(extra[:, 3][:, None, :] * weight, axis=(0, 2))
    rel_x = target[0] - centre[0]
    rel_y = target[1] - centre[1]
    rel_z = target[2] - centre[2]
    near_x = sum_y * rel_z - sum_z * rel_y - arm_x
    near_y = sum_z * rel_x - sum_x * rel_z - arm_y
    near_z = sum_x * rel_y - sum_y * rel_x - arm_z
    off_x = target[0][None, :] - moments[:, 0][:, None]
    off_y = target[1][None, :] - moments[:, 1][:, None]
    off_z = target[2][None, :] - moments[:, 2][:, None]
    far_sq = off_x * off_x + off_y * off_y + off_z * off_z + moments[:, 6][:, None]
    far_inverse = lax.rsqrt(far_sq)
    far_weight = far_inverse * far_inverse * far_inverse
    mom_x = moments[:, 3][:, None] * far_weight
    mom_y = moments[:, 4][:, None] * far_weight
    mom_z = moments[:, 5][:, None] * far_weight
    far_x = jnp.sum(mom_y * off_z - mom_z * off_y, axis=0)
    far_y = jnp.sum(mom_z * off_x - mom_x * off_z, axis=0)
    far_z = jnp.sum(mom_x * off_y - mom_y * off_x, axis=0)
    return jnp.stack([near_x + far_x, near_y + far_y, near_z + far_z], axis=0) * inv_four_pi


def source_terms(sources_all, centre):
    px = sources_all[:, :, 0] - centre[:, 0][:, None, None]
    py = sources_all[:, :, 1] - centre[:, 1][:, None, None]
    pz = sources_all[:, :, 2] - centre[:, 2][:, None, None]
    sx, sy, sz = sources_all[:, :, 3], sources_all[:, :, 4], sources_all[:, :, 5]
    core_sq = sources_all[:, :, 6] * sources_all[:, :, 6]
    extra = jnp.stack([core_sq, sy * pz - sz * py, sz * px - sx * pz, sx * py - sy * px], axis=2)
    return lax.optimization_barrier(extra)


def trace_back(loc, moves, levels, bits_x, nbd):
    size_x, size_y = moves.shape[1], moves.shape[2]
    devices = size_x * size_y
    level_bit = np.array(
        [(1 << bits_x - 1 - level) * size_y if level < bits_x else 1 << levels - 1 - level for level in range(levels)],
        np.int32,
    )
    flat = moves.reshape(levels, devices)
    every = jnp.arange(devices, dtype=jnp.int32)
    swap = jnp.bitwise_xor(every[None, :, None], level_bit[:, None, None]) == every[None, None, :]
    mate_moves = jnp.sum(jnp.where(swap, flat[:, None, :], 0), axis=2)
    delta = flat - mate_moves
    before = nbd + jnp.sum(delta, axis=0)
    kept = []
    for level in range(levels):
        kept.append(before - flat[level])
        before = before - delta[level]
    kept = jnp.stack(kept, axis=0)
    kept_mate = jnp.sum(jnp.where(swap, kept[:, None, :], 0), axis=2)
    device = loc.reshape(-1) // nbd
    slot = loc.reshape(-1) % nbd
    for level in reversed(range(levels)):
        pick = device[:, None] == every[None, :]
        here = jnp.sum(jnp.where(pick, kept[level][None, :], 0), axis=1)
        there = jnp.sum(jnp.where(pick, kept_mate[level][None, :], 0), axis=1)
        moved = slot >= here
        slot = jnp.where(moved, slot - here + there, slot)
        device = jnp.where(moved, jnp.bitwise_xor(device, level_bit[level]), device)
    return device.reshape(loc.shape), slot.reshape(loc.shape)


def table_blocks(table, lanes):
    cap, width = table.shape
    pieces = -(-cap // lanes)
    wide = jnp.pad(table.T, ((0, 0), (0, pieces * lanes - cap)))
    return wide.reshape(width, pieces, lanes).transpose(1, 0, 2)


def local(positions, strength, core, moves, owner, near_list, far_list):
    column_index = lax.axis_index("gx")
    row_index = lax.axis_index("gy")
    size_x = lax.axis_size("gx")
    size_y = lax.axis_size("gy")
    bits_x = size_x.bit_length() - 1
    levels = moves.shape[0]
    cap = positions.shape[2]
    nbd = near_list.shape[2]
    lanes = positions.shape[4]
    me = column_index * size_y + row_index
    held = jnp.concatenate([positions[0, 0], strength[0, 0], core[0, 0][:, None, :]], axis=1)
    slot_table = slot_multipoles(held[:, 0:3], held[:, 3:6], held[:, 6])
    width = slot_table.shape[1]
    gathered = table_blocks(slot_table, lanes)
    pieces = gathered.shape[0]
    far_where = owner[far_list[0, 0]]
    far_device, far_slot = trace_back(far_where, moves, levels, bits_x, nbd)
    held = jnp.pad(held, ((0, MOVE), (0, 0), (0, 0)))
    plans = []
    level_bits = []
    for level in range(levels):
        if level < bits_x:
            bit_at = bits_x - 1 - level
            mate_moves = moves[level, jnp.bitwise_xor(column_index, 1 << bit_at), row_index]
            level_bits.append((1 << bit_at) * size_y)
        else:
            bit_at = levels - 1 - level
            mate_moves = moves[level, column_index, jnp.bitwise_xor(row_index, 1 << bit_at)]
            level_bits.append(1 << bit_at)
        plans.append((bit_at, moves[level, column_index, row_index], mate_moves))
    count = jnp.int32(nbd)
    for plan_item in plans:
        count = count + plan_item[1] - plan_item[2]
    for level in range(levels):
        bit_at, own_moves, mate_moves = plans[level]
        leaving = lax.dynamic_slice_in_dim(held, count - own_moves, MOVE, 0)
        payload = jnp.concatenate([leaving, gathered], axis=0)
        if level < bits_x:
            got = from_partner(payload, "gx", bit_at)
        else:
            got = from_partner(payload, "gy", bit_at)
        arriving = got[:MOVE]
        gathered = jnp.concatenate([gathered, got[MOVE:]], axis=0)
        count = count - own_moves
        held = lax.dynamic_update_slice_in_dim(held, arriving, count, 0)
        count = count + mate_moves
    blocks = held[:nbd]
    relative = jnp.bitwise_xor(far_device, me)
    entry = jnp.zeros_like(relative)
    for level in range(levels):
        entry = entry + ((relative // level_bits[level]) % 2) * (1 << level)
    all_table = gathered.reshape(-1, pieces, width, lanes).transpose(0, 1, 3, 2).reshape(-1, width)
    moments = all_table[entry * (pieces * lanes) + far_slot]
    near_where = owner[near_list[0, 0]]
    source_device = near_where // nbd
    source_slot = near_where % nbd
    delta_x = source_device // size_y - column_index
    delta_y = source_device % size_y - row_index
    sign_x = 2 * (column_index % 2) - 1
    sign_y = 2 * (row_index % 2) - 1
    source_pool = swapped(swapped(blocks, "gx"), "gy")
    pool_index = ((1 + delta_y * sign_y) * 3 + (1 + delta_x * sign_x)) * nbd + source_slot
    sources_all = source_pool[pool_index]
    targets = blocks[:, 0:3]
    centre = jnp.mean(targets, axis=2)
    extra = source_terms(sources_all, centre)
    velocity = jax.vmap(evaluate)(targets, centre, sources_all, extra, moments)
    return velocity[None, None]


def solution(mesh):
    placed = (
        P("gx", "gy", None, None, None),
        P("gx", "gy", None, None, None),
        P("gx", "gy", None, None),
        P(),
        P(),
        P("gx", "gy", None, None),
        P("gx", "gy", None, None),
    )
    return jax.shard_map(
        local,
        mesh=mesh,
        in_specs=placed,
        out_specs=P("gx", "gy", None, None, None),
        check_vma=False,
    )
```

```python
import math

import jax
import jax.numpy as jnp
import numpy as np
from jax import lax
from jax.sharding import PartitionSpec as P

MOVE = 8


inv_four_pi = 0.25 / math.pi


def from_partner(shard, axis, apart):
    return lax.ppermute(shard, axis, [(i, i ^ 1 << apart) for i in range(lax.axis_size(axis))])


def swapped(shard, axis):
    size = lax.axis_size(axis)
    first = [(i, i ^ 1) for i in range(size)]
    second = [(i, i + 1 - 2 * (i % 2 == 0)) for i in range(1, size - 1)]
    return jnp.concatenate([lax.ppermute(shard, axis, first), shard, lax.ppermute(shard, axis, second)], axis=0)


def routed(shard, axis):
    size = lax.axis_size(axis)
    step = [(i, i + 2 if i % 2 else i - 2) for i in range(size) if 0 <= (i + 2 if i % 2 else i - 2) < size]
    relayed = lax.ppermute(shard, axis, step)
    pair = lax.ppermute(jnp.concatenate([shard, relayed], axis=0), axis, [(i, i ^ 1) for i in range(size)])
    count = shard.shape[0]
    return jnp.concatenate([pair[:count], shard, pair[count:]], axis=0)


def slot_multipoles(pos, stren, core):
    centre = jnp.mean(pos, axis=2)
    total = jnp.sum(stren, axis=2)
    offset = pos - centre[:, :, None]
    spread = jnp.mean(core * core, axis=1) + jnp.mean(jnp.sum(offset * offset, axis=1), axis=1)
    return jnp.concatenate([centre, total, spread[:, None]], axis=1)


def evaluate(target, centre, sources, extra, moments):
    sep_x = target[0][None, :, None] - sources[:, 0][:, None, :]
    sep_y = target[1][None, :, None] - sources[:, 1][:, None, :]
    sep_z = target[2][None, :, None] - sources[:, 2][:, None, :]
    radius_sq = sep_x * sep_x + sep_y * sep_y + sep_z * sep_z + extra[:, 0][:, None, :]
    inverse = lax.rsqrt(radius_sq)
    weight = inverse * inverse * inverse
    sum_x = jnp.sum(sources[:, 3][:, None, :] * weight, axis=(0, 2))
    sum_y = jnp.sum(sources[:, 4][:, None, :] * weight, axis=(0, 2))
    sum_z = jnp.sum(sources[:, 5][:, None, :] * weight, axis=(0, 2))
    arm_x = jnp.sum(extra[:, 1][:, None, :] * weight, axis=(0, 2))
    arm_y = jnp.sum(extra[:, 2][:, None, :] * weight, axis=(0, 2))
    arm_z = jnp.sum(extra[:, 3][:, None, :] * weight, axis=(0, 2))
    rel_x = target[0] - centre[0]
    rel_y = target[1] - centre[1]
    rel_z = target[2] - centre[2]
    near_x = sum_y * rel_z - sum_z * rel_y - arm_x
    near_y = sum_z * rel_x - sum_x * rel_z - arm_y
    near_z = sum_x * rel_y - sum_y * rel_x - arm_z
    off_x = target[0][None, :] - moments[:, 0][:, None]
    off_y = target[1][None, :] - moments[:, 1][:, None]
    off_z = target[2][None, :] - moments[:, 2][:, None]
    far_sq = off_x * off_x + off_y * off_y + off_z * off_z + moments[:, 6][:, None]
    far_inverse = lax.rsqrt(far_sq)
    far_weight = far_inverse * far_inverse * far_inverse
    mom_x = moments[:, 3][:, None] * far_weight
    mom_y = moments[:, 4][:, None] * far_weight
    mom_z = moments[:, 5][:, None] * far_weight
    far_x = jnp.sum(mom_y * off_z - mom_z * off_y, axis=0)
    far_y = jnp.sum(mom_z * off_x - mom_x * off_z, axis=0)
    far_z = jnp.sum(mom_x * off_y - mom_y * off_x, axis=0)
    return jnp.stack([near_x + far_x, near_y + far_y, near_z + far_z], axis=0) * inv_four_pi


def source_terms(sources_all, centre):
    px = sources_all[:, :, 0] - centre[:, 0][:, None, None]
    py = sources_all[:, :, 1] - centre[:, 1][:, None, None]
    pz = sources_all[:, :, 2] - centre[:, 2][:, None, None]
    sx, sy, sz = sources_all[:, :, 3], sources_all[:, :, 4], sources_all[:, :, 5]
    core_sq = sources_all[:, :, 6] * sources_all[:, :, 6]
    extra = jnp.stack([core_sq, sy * pz - sz * py, sz * px - sx * pz, sx * py - sy * px], axis=2)
    return lax.optimization_barrier(extra)


def trace_back(loc, moves, levels, bits_x, nbd):
    size_x, size_y = moves.shape[1], moves.shape[2]
    devices = size_x * size_y
    level_bit = np.array(
        [(1 << bits_x - 1 - level) * size_y if level < bits_x else 1 << levels - 1 - level for level in range(levels)],
        np.int32,
    )
    flat = moves.reshape(levels, devices)
    every = jnp.arange(devices, dtype=jnp.int32)
    swap = jnp.bitwise_xor(every[None, :, None], level_bit[:, None, None]) == every[None, None, :]
    mate_moves = jnp.sum(jnp.where(swap, flat[:, None, :], 0), axis=2)
    delta = flat - mate_moves
    before = nbd + jnp.sum(delta, axis=0)
    kept = []
    for level in range(levels):
        kept.append(before - flat[level])
        before = before - delta[level]
    kept = jnp.stack(kept, axis=0)
    kept_mate = jnp.sum(jnp.where(swap, kept[:, None, :], 0), axis=2)
    device = loc.reshape(-1) // nbd
    slot = loc.reshape(-1) % nbd
    for level in reversed(range(levels)):
        pick = device[:, None] == every[None, :]
        here = jnp.sum(jnp.where(pick, kept[level][None, :], 0), axis=1)
        there = jnp.sum(jnp.where(pick, kept_mate[level][None, :], 0), axis=1)
        moved = slot >= here
        slot = jnp.where(moved, slot - here + there, slot)
        device = jnp.where(moved, jnp.bitwise_xor(device, level_bit[level]), device)
    return device.reshape(loc.shape), slot.reshape(loc.shape)


def table_blocks(table, lanes):
    cap, width = table.shape
    pieces = -(-cap // lanes)
    wide = jnp.pad(table.T, ((0, 0), (0, pieces * lanes - cap)))
    return wide.reshape(width, pieces, lanes).transpose(1, 0, 2)


def local(positions, strength, core, moves, owner, near_list, far_list):
    column_index = lax.axis_index("gx")
    row_index = lax.axis_index("gy")
    size_x = lax.axis_size("gx")
    size_y = lax.axis_size("gy")
    bits_x = size_x.bit_length() - 1
    levels = moves.shape[0]
    cap = positions.shape[2]
    nbd = near_list.shape[2]
    lanes = positions.shape[4]
    me = column_index * size_y + row_index
    held = jnp.concatenate([positions[0, 0], strength[0, 0], core[0, 0][:, None, :]], axis=1)
    slot_table = slot_multipoles(held[:, 0:3], held[:, 3:6], held[:, 6])
    width = slot_table.shape[1]
    gathered = table_blocks(slot_table, lanes)
    pieces = gathered.shape[0]
    far_where = owner[far_list[0, 0]]
    far_device, far_slot = trace_back(far_where, moves, levels, bits_x, nbd)
    held = jnp.pad(held, ((0, MOVE), (0, 0), (0, 0)))
    plans = []
    level_bits = []
    for level in range(levels):
        if level < bits_x:
            bit_at = bits_x - 1 - level
            mate_moves = moves[level, jnp.bitwise_xor(column_index, 1 << bit_at), row_index]
            level_bits.append((1 << bit_at) * size_y)
        else:
            bit_at = levels - 1 - level
            mate_moves = moves[level, column_index, jnp.bitwise_xor(row_index, 1 << bit_at)]
            level_bits.append(1 << bit_at)
        plans.append((bit_at, moves[level, column_index, row_index], mate_moves))
    count = jnp.int32(nbd)
    for plan_item in plans:
        count = count + plan_item[1] - plan_item[2]
    for level in range(levels):
        bit_at, own_moves, mate_moves = plans[level]
        leaving = lax.dynamic_slice_in_dim(held, count - own_moves, MOVE, 0)
        payload = jnp.concatenate([leaving, gathered], axis=0)
        if level < bits_x:
            got = from_partner(payload, "gx", bit_at)
        else:
            got = from_partner(payload, "gy", bit_at)
        arriving = got[:MOVE]
        gathered = jnp.concatenate([gathered, got[MOVE:]], axis=0)
        count = count - own_moves
        held = lax.dynamic_update_slice_in_dim(held, arriving, count, 0)
        count = count + mate_moves
    blocks = held[:nbd]
    relative = jnp.bitwise_xor(far_device, me)
    entry = jnp.zeros_like(relative)
    for level in range(levels):
        entry = entry + ((relative // level_bits[level]) % 2) * (1 << level)
    all_table = gathered.reshape(-1, pieces, width, lanes).transpose(0, 1, 3, 2).reshape(-1, width)
    moments = all_table[entry * (pieces * lanes) + far_slot]
    near_where = owner[near_list[0, 0]]
    source_device = near_where // nbd
    source_slot = near_where % nbd
    delta_x = source_device // size_y - column_index
    delta_y = source_device % size_y - row_index
    sign_x = 2 * (column_index % 2) - 1
    sign_y = 2 * (row_index % 2) - 1
    source_pool = swapped(routed(blocks, "gx"), "gy")
    pool_index = ((1 + delta_y * sign_y) * 3 + (1 + delta_x * sign_x)) * nbd + source_slot
    sources_all = source_pool[pool_index]
    targets = blocks[:, 0:3]
    centre = jnp.mean(targets, axis=2)
    extra = source_terms(sources_all, centre)
    velocity = jax.vmap(evaluate)(targets, centre, sources_all, extra, moments)
    return velocity[None, None]


def solution(mesh):
    placed = (
        P("gx", "gy", None, None, None),
        P("gx", "gy", None, None, None),
        P("gx", "gy", None, None),
        P(),
        P(),
        P("gx", "gy", None, None),
        P("gx", "gy", None, None),
    )
    return jax.shard_map(
        local,
        mesh=mesh,
        in_specs=placed,
        out_specs=P("gx", "gy", None, None, None),
        check_vma=False,
    )
```

```python
import math

import jax
import jax.numpy as jnp
import numpy as np
from jax import lax
from jax.sharding import PartitionSpec as P

MOVE = 8


inv_four_pi = 0.25 / math.pi


def from_partner(shard, axis, apart):
    return lax.ppermute(shard, axis, [(i, i ^ 1 << apart) for i in range(lax.axis_size(axis))])


def swapped(shard, axis):
    size = lax.axis_size(axis)
    first = [(i, i ^ 1) for i in range(size)]
    second = [(i, i + 1 - 2 * (i % 2 == 0)) for i in range(1, size - 1)]
    return jnp.concatenate([lax.ppermute(shard, axis, first), shard, lax.ppermute(shard, axis, second)], axis=0)


def slot_multipoles(pos, stren, core):
    lanes = pos.shape[-1]
    ones = jnp.ones((lanes,), jnp.float32)
    exact = lax.Precision.HIGHEST
    centre = jnp.einsum("scl,l->sc", pos, ones, precision=exact) / lanes
    total = jnp.einsum("scl,l->sc", stren, ones, precision=exact)
    offset = pos - centre[:, :, None]
    spread = (
        jnp.einsum("sl,l->s", core * core, ones, precision=exact) / lanes
        + jnp.einsum("scl,l->s", offset * offset, ones, precision=exact) / lanes
    )
    return jnp.concatenate([centre, total, spread[:, None]], axis=1)


def evaluate(target, centre, sources, extra, moments):
    sep_x = target[0][None, :, None] - sources[:, 0][:, None, :]
    sep_y = target[1][None, :, None] - sources[:, 1][:, None, :]
    sep_z = target[2][None, :, None] - sources[:, 2][:, None, :]
    radius_sq = sep_x * sep_x + sep_y * sep_y + sep_z * sep_z + extra[:, 0][:, None, :]
    inverse = lax.rsqrt(radius_sq)
    weight = inverse * inverse * inverse
    sum_x = jnp.sum(sources[:, 3][:, None, :] * weight, axis=(0, 2))
    sum_y = jnp.sum(sources[:, 4][:, None, :] * weight, axis=(0, 2))
    sum_z = jnp.sum(sources[:, 5][:, None, :] * weight, axis=(0, 2))
    arm_x = jnp.sum(extra[:, 1][:, None, :] * weight, axis=(0, 2))
    arm_y = jnp.sum(extra[:, 2][:, None, :] * weight, axis=(0, 2))
    arm_z = jnp.sum(extra[:, 3][:, None, :] * weight, axis=(0, 2))
    rel_x = target[0] - centre[0]
    rel_y = target[1] - centre[1]
    rel_z = target[2] - centre[2]
    near_x = sum_y * rel_z - sum_z * rel_y - arm_x
    near_y = sum_z * rel_x - sum_x * rel_z - arm_y
    near_z = sum_x * rel_y - sum_y * rel_x - arm_z
    off_x = target[0][None, :] - moments[:, 0][:, None]
    off_y = target[1][None, :] - moments[:, 1][:, None]
    off_z = target[2][None, :] - moments[:, 2][:, None]
    far_sq = off_x * off_x + off_y * off_y + off_z * off_z + moments[:, 6][:, None]
    far_inverse = lax.rsqrt(far_sq)
    far_weight = far_inverse * far_inverse * far_inverse
    mom_x = moments[:, 3][:, None] * far_weight
    mom_y = moments[:, 4][:, None] * far_weight
    mom_z = moments[:, 5][:, None] * far_weight
    far_x = jnp.sum(mom_y * off_z - mom_z * off_y, axis=0)
    far_y = jnp.sum(mom_z * off_x - mom_x * off_z, axis=0)
    far_z = jnp.sum(mom_x * off_y - mom_y * off_x, axis=0)
    return jnp.stack([near_x + far_x, near_y + far_y, near_z + far_z], axis=0) * inv_four_pi


def source_terms(sources_all, centre):
    px = sources_all[:, :, 0] - centre[:, 0][:, None, None]
    py = sources_all[:, :, 1] - centre[:, 1][:, None, None]
    pz = sources_all[:, :, 2] - centre[:, 2][:, None, None]
    sx, sy, sz = sources_all[:, :, 3], sources_all[:, :, 4], sources_all[:, :, 5]
    core_sq = sources_all[:, :, 6] * sources_all[:, :, 6]
    extra = jnp.stack([core_sq, sy * pz - sz * py, sz * px - sx * pz, sx * py - sy * px], axis=2)
    return lax.optimization_barrier(extra)


def trace_back(loc, moves, levels, bits_x, nbd):
    size_x, size_y = moves.shape[1], moves.shape[2]
    devices = size_x * size_y
    level_bit = np.array(
        [(1 << bits_x - 1 - level) * size_y if level < bits_x else 1 << levels - 1 - level for level in range(levels)],
        np.int32,
    )
    flat = moves.reshape(levels, devices)
    every = jnp.arange(devices, dtype=jnp.int32)
    swap = jnp.bitwise_xor(every[None, :, None], level_bit[:, None, None]) == every[None, None, :]
    mate_moves = jnp.sum(jnp.where(swap, flat[:, None, :], 0), axis=2)
    delta = flat - mate_moves
    before = nbd + jnp.sum(delta, axis=0)
    kept = []
    for level in range(levels):
        kept.append(before - flat[level])
        before = before - delta[level]
    kept = jnp.stack(kept, axis=0)
    kept_mate = jnp.sum(jnp.where(swap, kept[:, None, :], 0), axis=2)
    device = loc.reshape(-1) // nbd
    slot = loc.reshape(-1) % nbd
    for level in reversed(range(levels)):
        pick = device[:, None] == every[None, :]
        here = jnp.sum(jnp.where(pick, kept[level][None, :], 0), axis=1)
        there = jnp.sum(jnp.where(pick, kept_mate[level][None, :], 0), axis=1)
        moved = slot >= here
        slot = jnp.where(moved, slot - here + there, slot)
        device = jnp.where(moved, jnp.bitwise_xor(device, level_bit[level]), device)
    return device.reshape(loc.shape), slot.reshape(loc.shape)


def table_blocks(table, lanes):
    cap, width = table.shape
    pieces = -(-cap // lanes)
    wide = jnp.pad(table.T, ((0, 0), (0, pieces * lanes - cap)))
    return wide.reshape(width, pieces, lanes).transpose(1, 0, 2)


def local(positions, strength, core, moves, owner, near_list, far_list):
    column_index = lax.axis_index("gx")
    row_index = lax.axis_index("gy")
    size_x = lax.axis_size("gx")
    size_y = lax.axis_size("gy")
    bits_x = size_x.bit_length() - 1
    levels = moves.shape[0]
    cap = positions.shape[2]
    nbd = near_list.shape[2]
    lanes = positions.shape[4]
    me = column_index * size_y + row_index
    held = jnp.concatenate([positions[0, 0], strength[0, 0], core[0, 0][:, None, :]], axis=1)
    slot_table = slot_multipoles(held[:, 0:3], held[:, 3:6], held[:, 6])
    width = slot_table.shape[1]
    gathered = table_blocks(slot_table, lanes)
    pieces = gathered.shape[0]
    far_where = owner[far_list[0, 0]]
    far_device, far_slot = trace_back(far_where, moves, levels, bits_x, nbd)
    held = jnp.pad(held, ((0, MOVE), (0, 0), (0, 0)))
    plans = []
    level_bits = []
    for level in range(levels):
        if level < bits_x:
            bit_at = bits_x - 1 - level
            mate_moves = moves[level, jnp.bitwise_xor(column_index, 1 << bit_at), row_index]
            level_bits.append((1 << bit_at) * size_y)
        else:
            bit_at = levels - 1 - level
            mate_moves = moves[level, column_index, jnp.bitwise_xor(row_index, 1 << bit_at)]
            level_bits.append(1 << bit_at)
        plans.append((bit_at, moves[level, column_index, row_index], mate_moves))
    count = jnp.int32(nbd)
    for plan_item in plans:
        count = count + plan_item[1] - plan_item[2]
    for level in range(levels):
        bit_at, own_moves, mate_moves = plans[level]
        leaving = lax.dynamic_slice_in_dim(held, count - own_moves, MOVE, 0)
        payload = jnp.concatenate([leaving, gathered], axis=0)
        if level < bits_x:
            got = from_partner(payload, "gx", bit_at)
        else:
            got = from_partner(payload, "gy", bit_at)
        arriving = got[:MOVE]
        gathered = jnp.concatenate([gathered, got[MOVE:]], axis=0)
        count = count - own_moves
        held = lax.dynamic_update_slice_in_dim(held, arriving, count, 0)
        count = count + mate_moves
    blocks = held[:nbd]
    relative = jnp.bitwise_xor(far_device, me)
    entry = jnp.zeros_like(relative)
    for level in range(levels):
        entry = entry + ((relative // level_bits[level]) % 2) * (1 << level)
    all_table = gathered.reshape(-1, pieces, width, lanes).transpose(0, 1, 3, 2).reshape(-1, width)
    moments = all_table[entry * (pieces * lanes) + far_slot]
    near_where = owner[near_list[0, 0]]
    source_device = near_where // nbd
    source_slot = near_where % nbd
    delta_x = source_device // size_y - column_index
    delta_y = source_device % size_y - row_index
    sign_x = 2 * (column_index % 2) - 1
    sign_y = 2 * (row_index % 2) - 1
    source_pool = swapped(swapped(blocks, "gx"), "gy")
    pool_index = ((1 + delta_y * sign_y) * 3 + (1 + delta_x * sign_x)) * nbd + source_slot
    sources_all = source_pool[pool_index]
    targets = blocks[:, 0:3]
    centre = jnp.mean(targets, axis=2)
    extra = source_terms(sources_all, centre)
    velocity = jax.vmap(evaluate)(targets, centre, sources_all, extra, moments)
    return velocity[None, None]


def solution(mesh):
    placed = (
        P("gx", "gy", None, None, None),
        P("gx", "gy", None, None, None),
        P("gx", "gy", None, None),
        P(),
        P(),
        P("gx", "gy", None, None),
        P("gx", "gy", None, None),
    )
    return jax.shard_map(
        local,
        mesh=mesh,
        in_specs=placed,
        out_specs=P("gx", "gy", None, None, None),
        check_vma=False,
    )
```

```python
import math

import jax
import jax.numpy as jnp
import numpy as np
from jax import lax
from jax.sharding import PartitionSpec as P

MOVE = 8


inv_four_pi = 0.25 / math.pi


def from_partner(shard, axis, apart):
    return lax.ppermute(shard, axis, [(i, i ^ 1 << apart) for i in range(lax.axis_size(axis))])


def swapped(shard, axis):
    size = lax.axis_size(axis)
    first = [(i, i ^ 1) for i in range(size)]
    second = [(i, i + 1 - 2 * (i % 2 == 0)) for i in range(1, size - 1)]
    return jnp.concatenate([lax.ppermute(shard, axis, first), shard, lax.ppermute(shard, axis, second)], axis=0)


def slot_multipoles(pos, stren, core):
    lanes = pos.shape[-1]
    ones = jnp.ones((lanes,), jnp.float32)
    exact = lax.Precision.HIGHEST
    centre = jnp.einsum("scl,l->sc", pos, ones, precision=exact) / lanes
    total = jnp.einsum("scl,l->sc", stren, ones, precision=exact)
    offset = pos - centre[:, :, None]
    spread = (
        jnp.einsum("sl,l->s", core * core, ones, precision=exact) / lanes
        + jnp.sum(jnp.einsum("scl,l->sc", offset * offset, ones, precision=exact), axis=1) / lanes
    )
    return jnp.concatenate([centre, total, spread[:, None]], axis=1)


def evaluate(target, centre, sources, extra, moments):
    sep_x = target[0][None, :, None] - sources[:, 0][:, None, :]
    sep_y = target[1][None, :, None] - sources[:, 1][:, None, :]
    sep_z = target[2][None, :, None] - sources[:, 2][:, None, :]
    radius_sq = sep_x * sep_x + sep_y * sep_y + sep_z * sep_z + extra[:, 0][:, None, :]
    inverse = lax.rsqrt(radius_sq)
    weight = inverse * inverse * inverse
    sum_x = jnp.sum(sources[:, 3][:, None, :] * weight, axis=(0, 2))
    sum_y = jnp.sum(sources[:, 4][:, None, :] * weight, axis=(0, 2))
    sum_z = jnp.sum(sources[:, 5][:, None, :] * weight, axis=(0, 2))
    arm_x = jnp.sum(extra[:, 1][:, None, :] * weight, axis=(0, 2))
    arm_y = jnp.sum(extra[:, 2][:, None, :] * weight, axis=(0, 2))
    arm_z = jnp.sum(extra[:, 3][:, None, :] * weight, axis=(0, 2))
    rel_x = target[0] - centre[0]
    rel_y = target[1] - centre[1]
    rel_z = target[2] - centre[2]
    near_x = sum_y * rel_z - sum_z * rel_y - arm_x
    near_y = sum_z * rel_x - sum_x * rel_z - arm_y
    near_z = sum_x * rel_y - sum_y * rel_x - arm_z
    off_x = target[0][None, :] - moments[:, 0][:, None]
    off_y = target[1][None, :] - moments[:, 1][:, None]
    off_z = target[2][None, :] - moments[:, 2][:, None]
    far_sq = off_x * off_x + off_y * off_y + off_z * off_z + moments[:, 6][:, None]
    far_inverse = lax.rsqrt(far_sq)
    far_weight = far_inverse * far_inverse * far_inverse
    mom_x = moments[:, 3][:, None] * far_weight
    mom_y = moments[:, 4][:, None] * far_weight
    mom_z = moments[:, 5][:, None] * far_weight
    far_x = jnp.sum(mom_y * off_z - mom_z * off_y, axis=0)
    far_y = jnp.sum(mom_z * off_x - mom_x * off_z, axis=0)
    far_z = jnp.sum(mom_x * off_y - mom_y * off_x, axis=0)
    return jnp.stack([near_x + far_x, near_y + far_y, near_z + far_z], axis=0) * inv_four_pi


def source_terms(sources_all, centre):
    px = sources_all[:, :, 0] - centre[:, 0][:, None, None]
    py = sources_all[:, :, 1] - centre[:, 1][:, None, None]
    pz = sources_all[:, :, 2] - centre[:, 2][:, None, None]
    sx, sy, sz = sources_all[:, :, 3], sources_all[:, :, 4], sources_all[:, :, 5]
    core_sq = sources_all[:, :, 6] * sources_all[:, :, 6]
    extra = jnp.stack([core_sq, sy * pz - sz * py, sz * px - sx * pz, sx * py - sy * px], axis=2)
    return lax.optimization_barrier(extra)


def trace_back(loc, moves, levels, bits_x, nbd):
    size_x, size_y = moves.shape[1], moves.shape[2]
    devices = size_x * size_y
    level_bit = np.array(
        [(1 << bits_x - 1 - level) * size_y if level < bits_x else 1 << levels - 1 - level for level in range(levels)],
        np.int32,
    )
    flat = moves.reshape(levels, devices)
    every = jnp.arange(devices, dtype=jnp.int32)
    swap = jnp.bitwise_xor(every[None, :, None], level_bit[:, None, None]) == every[None, None, :]
    mate_moves = jnp.sum(jnp.where(swap, flat[:, None, :], 0), axis=2)
    delta = flat - mate_moves
    before = nbd + jnp.sum(delta, axis=0)
    kept = []
    for level in range(levels):
        kept.append(before - flat[level])
        before = before - delta[level]
    kept = jnp.stack(kept, axis=0)
    kept_mate = jnp.sum(jnp.where(swap, kept[:, None, :], 0), axis=2)
    device = loc.reshape(-1) // nbd
    slot = loc.reshape(-1) % nbd
    for level in reversed(range(levels)):
        pick = device[:, None] == every[None, :]
        here = jnp.sum(jnp.where(pick, kept[level][None, :], 0), axis=1)
        there = jnp.sum(jnp.where(pick, kept_mate[level][None, :], 0), axis=1)
        moved = slot >= here
        slot = jnp.where(moved, slot - here + there, slot)
        device = jnp.where(moved, jnp.bitwise_xor(device, level_bit[level]), device)
    return device.reshape(loc.shape), slot.reshape(loc.shape)


def table_blocks(table, lanes):
    cap, width = table.shape
    pieces = -(-cap // lanes)
    wide = jnp.pad(table.T, ((0, 0), (0, pieces * lanes - cap)))
    return wide.reshape(width, pieces, lanes).transpose(1, 0, 2)


def local(positions, strength, core, moves, owner, near_list, far_list):
    column_index = lax.axis_index("gx")
    row_index = lax.axis_index("gy")
    size_x = lax.axis_size("gx")
    size_y = lax.axis_size("gy")
    bits_x = size_x.bit_length() - 1
    levels = moves.shape[0]
    cap = positions.shape[2]
    nbd = near_list.shape[2]
    lanes = positions.shape[4]
    me = column_index * size_y + row_index
    held = jnp.concatenate([positions[0, 0], strength[0, 0], core[0, 0][:, None, :]], axis=1)
    slot_table = slot_multipoles(held[:, 0:3], held[:, 3:6], held[:, 6])
    width = slot_table.shape[1]
    gathered = table_blocks(slot_table, lanes)
    pieces = gathered.shape[0]
    far_where = owner[far_list[0, 0]]
    far_device, far_slot = trace_back(far_where, moves, levels, bits_x, nbd)
    held = jnp.pad(held, ((0, MOVE), (0, 0), (0, 0)))
    plans = []
    level_bits = []
    for level in range(levels):
        if level < bits_x:
            bit_at = bits_x - 1 - level
            mate_moves = moves[level, jnp.bitwise_xor(column_index, 1 << bit_at), row_index]
            level_bits.append((1 << bit_at) * size_y)
        else:
            bit_at = levels - 1 - level
            mate_moves = moves[level, column_index, jnp.bitwise_xor(row_index, 1 << bit_at)]
            level_bits.append(1 << bit_at)
        plans.append((bit_at, moves[level, column_index, row_index], mate_moves))
    count = jnp.int32(nbd)
    for plan_item in plans:
        count = count + plan_item[1] - plan_item[2]
    for level in range(levels):
        bit_at, own_moves, mate_moves = plans[level]
        leaving = lax.dynamic_slice_in_dim(held, count - own_moves, MOVE, 0)
        payload = jnp.concatenate([leaving, gathered], axis=0)
        if level < bits_x:
            got = from_partner(payload, "gx", bit_at)
        else:
            got = from_partner(payload, "gy", bit_at)
        arriving = got[:MOVE]
        gathered = jnp.concatenate([gathered, got[MOVE:]], axis=0)
        count = count - own_moves
        held = lax.dynamic_update_slice_in_dim(held, arriving, count, 0)
        count = count + mate_moves
    blocks = held[:nbd]
    relative = jnp.bitwise_xor(far_device, me)
    entry = jnp.zeros_like(relative)
    for level in range(levels):
        entry = entry + ((relative // level_bits[level]) % 2) * (1 << level)
    all_table = gathered.reshape(-1, pieces, width, lanes).transpose(0, 1, 3, 2).reshape(-1, width)
    moments = all_table[entry * (pieces * lanes) + far_slot]
    near_where = owner[near_list[0, 0]]
    source_device = near_where // nbd
    source_slot = near_where % nbd
    delta_x = source_device // size_y - column_index
    delta_y = source_device % size_y - row_index
    sign_x = 2 * (column_index % 2) - 1
    sign_y = 2 * (row_index % 2) - 1
    source_pool = swapped(swapped(blocks, "gx"), "gy")
    pool_index = ((1 + delta_y * sign_y) * 3 + (1 + delta_x * sign_x)) * nbd + source_slot
    sources_all = source_pool[pool_index]
    targets = blocks[:, 0:3]
    centre = jnp.mean(targets, axis=2)
    extra = source_terms(sources_all, centre)
    velocity = jax.vmap(evaluate)(targets, centre, sources_all, extra, moments)
    return velocity[None, None]


def solution(mesh):
    placed = (
        P("gx", "gy", None, None, None),
        P("gx", "gy", None, None, None),
        P("gx", "gy", None, None),
        P(),
        P(),
        P("gx", "gy", None, None),
        P("gx", "gy", None, None),
    )
    return jax.shard_map(
        local,
        mesh=mesh,
        in_specs=placed,
        out_specs=P("gx", "gy", None, None, None),
        check_vma=False,
    )
```

```python
import math

import jax
import jax.numpy as jnp
import numpy as np
from jax import lax
from jax.sharding import PartitionSpec as P

MOVE = 8


inv_four_pi = 0.25 / math.pi


def from_partner(shard, axis, apart):
    return lax.ppermute(shard, axis, [(i, i ^ 1 << apart) for i in range(lax.axis_size(axis))])


def swapped(shard, axis):
    size = lax.axis_size(axis)
    first = [(i, i ^ 1) for i in range(size)]
    second = [(i, i + 1 - 2 * (i % 2 == 0)) for i in range(1, size - 1)]
    return jnp.concatenate([lax.ppermute(shard, axis, first), shard, lax.ppermute(shard, axis, second)], axis=0)


def slot_multipoles(pos, stren, core):
    lanes = pos.shape[-1]
    ones = jnp.ones((lanes,), jnp.float32)
    exact = lax.Precision.HIGHEST
    rough = jnp.einsum("scl,l->sc", pos, ones, precision=exact) / lanes
    centre = rough + jnp.einsum("scl,l->sc", pos - rough[:, :, None], ones, precision=exact) / lanes
    total = jnp.einsum("scl,l->sc", stren, ones, precision=exact)
    offset = pos - centre[:, :, None]
    spread = (
        jnp.einsum("sl,l->s", core * core, ones, precision=exact) / lanes
        + jnp.sum(jnp.einsum("scl,l->sc", offset * offset, ones, precision=exact), axis=1) / lanes
    )
    return jnp.concatenate([centre, total, spread[:, None]], axis=1)


def evaluate(target, centre, sources, extra, moments):
    sep_x = target[0][None, :, None] - sources[:, 0][:, None, :]
    sep_y = target[1][None, :, None] - sources[:, 1][:, None, :]
    sep_z = target[2][None, :, None] - sources[:, 2][:, None, :]
    radius_sq = sep_x * sep_x + sep_y * sep_y + sep_z * sep_z + extra[:, 0][:, None, :]
    inverse = lax.rsqrt(radius_sq)
    weight = inverse * inverse * inverse
    sum_x = jnp.sum(sources[:, 3][:, None, :] * weight, axis=(0, 2))
    sum_y = jnp.sum(sources[:, 4][:, None, :] * weight, axis=(0, 2))
    sum_z = jnp.sum(sources[:, 5][:, None, :] * weight, axis=(0, 2))
    arm_x = jnp.sum(extra[:, 1][:, None, :] * weight, axis=(0, 2))
    arm_y = jnp.sum(extra[:, 2][:, None, :] * weight, axis=(0, 2))
    arm_z = jnp.sum(extra[:, 3][:, None, :] * weight, axis=(0, 2))
    rel_x = target[0] - centre[0]
    rel_y = target[1] - centre[1]
    rel_z = target[2] - centre[2]
    near_x = sum_y * rel_z - sum_z * rel_y - arm_x
    near_y = sum_z * rel_x - sum_x * rel_z - arm_y
    near_z = sum_x * rel_y - sum_y * rel_x - arm_z
    off_x = target[0][None, :] - moments[:, 0][:, None]
    off_y = target[1][None, :] - moments[:, 1][:, None]
    off_z = target[2][None, :] - moments[:, 2][:, None]
    far_sq = off_x * off_x + off_y * off_y + off_z * off_z + moments[:, 6][:, None]
    far_inverse = lax.rsqrt(far_sq)
    far_weight = far_inverse * far_inverse * far_inverse
    mom_x = moments[:, 3][:, None] * far_weight
    mom_y = moments[:, 4][:, None] * far_weight
    mom_z = moments[:, 5][:, None] * far_weight
    far_x = jnp.sum(mom_y * off_z - mom_z * off_y, axis=0)
    far_y = jnp.sum(mom_z * off_x - mom_x * off_z, axis=0)
    far_z = jnp.sum(mom_x * off_y - mom_y * off_x, axis=0)
    return jnp.stack([near_x + far_x, near_y + far_y, near_z + far_z], axis=0) * inv_four_pi


def source_terms(sources_all, centre):
    px = sources_all[:, :, 0] - centre[:, 0][:, None, None]
    py = sources_all[:, :, 1] - centre[:, 1][:, None, None]
    pz = sources_all[:, :, 2] - centre[:, 2][:, None, None]
    sx, sy, sz = sources_all[:, :, 3], sources_all[:, :, 4], sources_all[:, :, 5]
    core_sq = sources_all[:, :, 6] * sources_all[:, :, 6]
    extra = jnp.stack([core_sq, sy * pz - sz * py, sz * px - sx * pz, sx * py - sy * px], axis=2)
    return lax.optimization_barrier(extra)


def trace_back(loc, moves, levels, bits_x, nbd):
    size_x, size_y = moves.shape[1], moves.shape[2]
    devices = size_x * size_y
    level_bit = np.array(
        [(1 << bits_x - 1 - level) * size_y if level < bits_x else 1 << levels - 1 - level for level in range(levels)],
        np.int32,
    )
    flat = moves.reshape(levels, devices)
    every = jnp.arange(devices, dtype=jnp.int32)
    swap = jnp.bitwise_xor(every[None, :, None], level_bit[:, None, None]) == every[None, None, :]
    mate_moves = jnp.sum(jnp.where(swap, flat[:, None, :], 0), axis=2)
    delta = flat - mate_moves
    before = nbd + jnp.sum(delta, axis=0)
    kept = []
    for level in range(levels):
        kept.append(before - flat[level])
        before = before - delta[level]
    kept = jnp.stack(kept, axis=0)
    kept_mate = jnp.sum(jnp.where(swap, kept[:, None, :], 0), axis=2)
    device = loc.reshape(-1) // nbd
    slot = loc.reshape(-1) % nbd
    for level in reversed(range(levels)):
        pick = device[:, None] == every[None, :]
        here = jnp.sum(jnp.where(pick, kept[level][None, :], 0), axis=1)
        there = jnp.sum(jnp.where(pick, kept_mate[level][None, :], 0), axis=1)
        moved = slot >= here
        slot = jnp.where(moved, slot - here + there, slot)
        device = jnp.where(moved, jnp.bitwise_xor(device, level_bit[level]), device)
    return device.reshape(loc.shape), slot.reshape(loc.shape)


def table_blocks(table, lanes):
    cap, width = table.shape
    pieces = -(-cap // lanes)
    wide = jnp.pad(table.T, ((0, 0), (0, pieces * lanes - cap)))
    return wide.reshape(width, pieces, lanes).transpose(1, 0, 2)


def local(positions, strength, core, moves, owner, near_list, far_list):
    column_index = lax.axis_index("gx")
    row_index = lax.axis_index("gy")
    size_x = lax.axis_size("gx")
    size_y = lax.axis_size("gy")
    bits_x = size_x.bit_length() - 1
    levels = moves.shape[0]
    cap = positions.shape[2]
    nbd = near_list.shape[2]
    lanes = positions.shape[4]
    me = column_index * size_y + row_index
    held = jnp.concatenate([positions[0, 0], strength[0, 0], core[0, 0][:, None, :]], axis=1)
    slot_table = slot_multipoles(held[:, 0:3], held[:, 3:6], held[:, 6])
    width = slot_table.shape[1]
    gathered = table_blocks(slot_table, lanes)
    pieces = gathered.shape[0]
    far_where = owner[far_list[0, 0]]
    far_device, far_slot = trace_back(far_where, moves, levels, bits_x, nbd)
    held = jnp.pad(held, ((0, MOVE), (0, 0), (0, 0)))
    plans = []
    level_bits = []
    for level in range(levels):
        if level < bits_x:
            bit_at = bits_x - 1 - level
            mate_moves = moves[level, jnp.bitwise_xor(column_index, 1 << bit_at), row_index]
            level_bits.append((1 << bit_at) * size_y)
        else:
            bit_at = levels - 1 - level
            mate_moves = moves[level, column_index, jnp.bitwise_xor(row_index, 1 << bit_at)]
            level_bits.append(1 << bit_at)
        plans.append((bit_at, moves[level, column_index, row_index], mate_moves))
    count = jnp.int32(nbd)
    for plan_item in plans:
        count = count + plan_item[1] - plan_item[2]
    for level in range(levels):
        bit_at, own_moves, mate_moves = plans[level]
        leaving = lax.dynamic_slice_in_dim(held, count - own_moves, MOVE, 0)
        payload = jnp.concatenate([leaving, gathered], axis=0)
        if level < bits_x:
            got = from_partner(payload, "gx", bit_at)
        else:
            got = from_partner(payload, "gy", bit_at)
        arriving = got[:MOVE]
        gathered = jnp.concatenate([gathered, got[MOVE:]], axis=0)
        count = count - own_moves
        held = lax.dynamic_update_slice_in_dim(held, arriving, count, 0)
        count = count + mate_moves
    blocks = held[:nbd]
    relative = jnp.bitwise_xor(far_device, me)
    entry = jnp.zeros_like(relative)
    for level in range(levels):
        entry = entry + ((relative // level_bits[level]) % 2) * (1 << level)
    all_table = gathered.reshape(-1, pieces, width, lanes).transpose(0, 1, 3, 2).reshape(-1, width)
    moments = all_table[entry * (pieces * lanes) + far_slot]
    near_where = owner[near_list[0, 0]]
    source_device = near_where // nbd
    source_slot = near_where % nbd
    delta_x = source_device // size_y - column_index
    delta_y = source_device % size_y - row_index
    sign_x = 2 * (column_index % 2) - 1
    sign_y = 2 * (row_index % 2) - 1
    source_pool = swapped(swapped(blocks, "gx"), "gy")
    pool_index = ((1 + delta_y * sign_y) * 3 + (1 + delta_x * sign_x)) * nbd + source_slot
    sources_all = source_pool[pool_index]
    targets = blocks[:, 0:3]
    centre = jnp.mean(targets, axis=2)
    extra = source_terms(sources_all, centre)
    velocity = jax.vmap(evaluate)(targets, centre, sources_all, extra, moments)
    return velocity[None, None]


def solution(mesh):
    placed = (
        P("gx", "gy", None, None, None),
        P("gx", "gy", None, None, None),
        P("gx", "gy", None, None),
        P(),
        P(),
        P("gx", "gy", None, None),
        P("gx", "gy", None, None),
    )
    return jax.shard_map(
        local,
        mesh=mesh,
        in_specs=placed,
        out_specs=P("gx", "gy", None, None, None),
        check_vma=False,
    )
```

```python
import math

import jax
import jax.numpy as jnp
import numpy as np
from jax import lax
from jax.sharding import PartitionSpec as P

MOVE = 8


inv_four_pi = 0.25 / math.pi


def from_partner(shard, axis, apart):
    return lax.ppermute(shard, axis, [(i, i ^ 1 << apart) for i in range(lax.axis_size(axis))])


def swapped(shard, axis):
    size = lax.axis_size(axis)
    first = [(i, i ^ 1) for i in range(size)]
    second = [(i, i + 1 - 2 * (i % 2 == 0)) for i in range(1, size - 1)]
    return jnp.concatenate([lax.ppermute(shard, axis, first), shard, lax.ppermute(shard, axis, second)], axis=0)


def slot_multipoles(pos, stren, core):
    lanes = pos.shape[-1]
    ones = jnp.ones((lanes,), jnp.float32)
    exact = lax.Precision.HIGHEST
    rough = jnp.einsum("scl,l->sc", pos, ones, precision=exact) / lanes
    centre = rough + jnp.einsum("scl,l->sc", pos - rough[:, :, None], ones, precision=exact) / lanes
    total = jnp.einsum("scl,l->sc", stren, ones, precision=exact)
    offset = pos - centre[:, :, None]
    spread = (
        jnp.einsum("sl,l->s", core * core, ones, precision=exact) / lanes
        + jnp.sum(jnp.einsum("scl,l->sc", offset * offset, ones, precision=exact), axis=1) / lanes
    )
    return jnp.concatenate([centre, total, spread[:, None]], axis=1)


def evaluate(target, centre, sources, extra, moments):
    sep_x = target[0][None, :, None] - sources[:, 0][:, None, :]
    sep_y = target[1][None, :, None] - sources[:, 1][:, None, :]
    sep_z = target[2][None, :, None] - sources[:, 2][:, None, :]
    radius_sq = sep_x * sep_x + sep_y * sep_y + sep_z * sep_z + extra[:, 0][:, None, :]
    inverse = lax.rsqrt(radius_sq)
    weight = inverse * inverse * inverse
    sum_x = jnp.sum(sources[:, 3][:, None, :] * weight, axis=(0, 2))
    sum_y = jnp.sum(sources[:, 4][:, None, :] * weight, axis=(0, 2))
    sum_z = jnp.sum(sources[:, 5][:, None, :] * weight, axis=(0, 2))
    arm_x = jnp.sum(extra[:, 1][:, None, :] * weight, axis=(0, 2))
    arm_y = jnp.sum(extra[:, 2][:, None, :] * weight, axis=(0, 2))
    arm_z = jnp.sum(extra[:, 3][:, None, :] * weight, axis=(0, 2))
    rel_x = target[0] - centre[0]
    rel_y = target[1] - centre[1]
    rel_z = target[2] - centre[2]
    near_x = sum_y * rel_z - sum_z * rel_y - arm_x
    near_y = sum_z * rel_x - sum_x * rel_z - arm_y
    near_z = sum_x * rel_y - sum_y * rel_x - arm_z
    off_x = target[0][None, :] - moments[:, 0][:, None]
    off_y = target[1][None, :] - moments[:, 1][:, None]
    off_z = target[2][None, :] - moments[:, 2][:, None]
    far_sq = off_x * off_x + off_y * off_y + off_z * off_z + moments[:, 6][:, None]
    far_inverse = lax.rsqrt(far_sq)
    far_weight = far_inverse * far_inverse * far_inverse
    mom_x = moments[:, 3][:, None] * far_weight
    mom_y = moments[:, 4][:, None] * far_weight
    mom_z = moments[:, 5][:, None] * far_weight
    far_x = jnp.sum(mom_y * off_z - mom_z * off_y, axis=0)
    far_y = jnp.sum(mom_z * off_x - mom_x * off_z, axis=0)
    far_z = jnp.sum(mom_x * off_y - mom_y * off_x, axis=0)
    return jnp.stack([near_x + far_x, near_y + far_y, near_z + far_z], axis=0) * inv_four_pi


def source_terms(sources_all, centre):
    px = sources_all[:, :, 0] - centre[:, 0][:, None, None]
    py = sources_all[:, :, 1] - centre[:, 1][:, None, None]
    pz = sources_all[:, :, 2] - centre[:, 2][:, None, None]
    sx, sy, sz = sources_all[:, :, 3], sources_all[:, :, 4], sources_all[:, :, 5]
    core_sq = sources_all[:, :, 6] * sources_all[:, :, 6]
    extra = jnp.stack([core_sq, sy * pz - sz * py, sz * px - sx * pz, sx * py - sy * px], axis=2)
    return lax.optimization_barrier(extra)


def level_tables(moves, levels, bits_x, nbd):
    size_x, size_y = moves.shape[1], moves.shape[2]
    devices = size_x * size_y
    level_bit = np.array(
        [(1 << bits_x - 1 - level) * size_y if level < bits_x else 1 << levels - 1 - level for level in range(levels)],
        np.int32,
    )
    flat = moves.reshape(levels, devices)
    every = jnp.arange(devices, dtype=jnp.int32)
    swap = jnp.bitwise_xor(every[None, :, None], level_bit[:, None, None]) == every[None, None, :]
    mate_moves = jnp.sum(jnp.where(swap, flat[:, None, :], 0), axis=2)
    delta = flat - mate_moves
    before = nbd + jnp.sum(delta, axis=0)
    kept = []
    for level in range(levels):
        kept.append(before - flat[level])
        before = before - delta[level]
    kept = jnp.stack(kept, axis=0)
    kept_mate = jnp.sum(jnp.where(swap, kept[:, None, :], 0), axis=2)
    return kept, kept_mate, level_bit


def trace_back(loc, kept, kept_mate, level_bit, nbd):
    levels, devices = kept.shape
    every = jnp.arange(devices, dtype=jnp.int32)
    device = loc.reshape(-1) // nbd
    slot = loc.reshape(-1) % nbd
    for level in reversed(range(levels)):
        pick = device[:, None] == every[None, :]
        here = jnp.sum(jnp.where(pick, kept[level][None, :], 0), axis=1)
        there = jnp.sum(jnp.where(pick, kept_mate[level][None, :], 0), axis=1)
        moved = slot >= here
        slot = jnp.where(moved, slot - here + there, slot)
        device = jnp.where(moved, jnp.bitwise_xor(device, level_bit[level]), device)
    return device.reshape(loc.shape), slot.reshape(loc.shape)


def table_blocks(table, lanes):
    cap, width = table.shape
    pieces = -(-cap // lanes)
    wide = jnp.pad(table.T, ((0, 0), (0, pieces * lanes - cap)))
    return wide.reshape(width, pieces, lanes).transpose(1, 0, 2)


def local(positions, strength, core, moves, owner, near_list, far_list):
    column_index = lax.axis_index("gx")
    row_index = lax.axis_index("gy")
    size_x = lax.axis_size("gx")
    size_y = lax.axis_size("gy")
    bits_x = size_x.bit_length() - 1
    levels = moves.shape[0]
    cap = positions.shape[2]
    nbd = near_list.shape[2]
    lanes = positions.shape[4]
    me = column_index * size_y + row_index
    held = jnp.concatenate([positions[0, 0], strength[0, 0], core[0, 0][:, None, :]], axis=1)
    slot_table = slot_multipoles(held[:, 0:3], held[:, 3:6], held[:, 6])
    width = slot_table.shape[1]
    gathered = table_blocks(slot_table, lanes)
    pieces = gathered.shape[0]
    held = jnp.pad(held, ((0, MOVE), (0, 0), (0, 0)))
    level_bits = []
    for level in range(levels):
        if level < bits_x:
            level_bits.append((1 << bits_x - 1 - level) * size_y)
        else:
            level_bits.append(1 << levels - 1 - level)
    devices = size_x * size_y
    flat_moves = moves.reshape(levels, devices)
    every = jnp.arange(devices, dtype=jnp.int32)
    mates = jnp.bitwise_xor(me, jnp.array(level_bits, jnp.int32))
    own = jnp.sum(jnp.where(every[None, :] == me, flat_moves, 0), axis=1)
    mate_own = jnp.sum(jnp.where(every[None, :] == mates[:, None], flat_moves, 0), axis=1)
    count = nbd + jnp.sum(own - mate_own, keepdims=True)
    slot_ids = jnp.arange(held.shape[0], dtype=jnp.int32)
    move_ids = jnp.arange(MOVE, dtype=jnp.int32)
    exact = lax.Precision.HIGHEST
    for level in range(levels):
        if level < bits_x:
            axis_name, bit_at = "gx", bits_x - 1 - level
        else:
            axis_name, bit_at = "gy", levels - 1 - level
        count = count - own[level : level + 1]
        take = (slot_ids[None, :] == (count + move_ids)[:, None]).astype(jnp.float32)
        leaving = jnp.einsum("ms,scl->mcl", take, held, precision=exact)
        payload = jnp.concatenate([leaving, gathered], axis=0)
        got = from_partner(payload, axis_name, bit_at)
        arriving = got[:MOVE]
        gathered = jnp.concatenate([gathered, got[MOVE:]], axis=0)
        put = slot_ids[:, None] == (count + move_ids)[None, :]
        placed = jnp.einsum("sm,mcl->scl", put.astype(jnp.float32), arriving, precision=exact)
        held = jnp.where(jnp.any(put, axis=1)[:, None, None], placed, held)
        count = count + mate_own[level : level + 1]
    far_where = owner[far_list[0, 0]]
    kept, kept_mate, level_bit = level_tables(moves, levels, bits_x, nbd)
    far_device, far_slot = trace_back(far_where, kept, kept_mate, level_bit, nbd)
    blocks = held[:nbd]
    relative = jnp.bitwise_xor(far_device, me)
    entry = jnp.zeros_like(relative)
    for level in range(levels):
        entry = entry + ((relative // level_bits[level]) % 2) * (1 << level)
    all_table = gathered.reshape(-1, pieces, width, lanes).transpose(0, 1, 3, 2).reshape(-1, width)
    moments = all_table[entry * (pieces * lanes) + far_slot]
    near_where = owner[near_list[0, 0]]
    source_device = near_where // nbd
    source_slot = near_where % nbd
    delta_x = source_device // size_y - column_index
    delta_y = source_device % size_y - row_index
    sign_x = 2 * (column_index % 2) - 1
    sign_y = 2 * (row_index % 2) - 1
    source_pool = swapped(swapped(blocks, "gx"), "gy")
    pool_index = ((1 + delta_y * sign_y) * 3 + (1 + delta_x * sign_x)) * nbd + source_slot
    sources_all = source_pool[pool_index]
    targets = blocks[:, 0:3]
    centre = jnp.mean(targets, axis=2)
    extra = source_terms(sources_all, centre)
    velocity = jax.vmap(evaluate)(targets, centre, sources_all, extra, moments)
    return velocity[None, None]


def solution(mesh):
    placed = (
        P("gx", "gy", None, None, None),
        P("gx", "gy", None, None, None),
        P("gx", "gy", None, None),
        P(),
        P(),
        P("gx", "gy", None, None),
        P("gx", "gy", None, None),
    )
    return jax.shard_map(
        local,
        mesh=mesh,
        in_specs=placed,
        out_specs=P("gx", "gy", None, None, None),
        check_vma=False,
    )
```

```python
import math

import jax
import jax.numpy as jnp
import numpy as np
from jax import lax
from jax.sharding import PartitionSpec as P

MOVE = 8


inv_four_pi = 0.25 / math.pi


def from_partner(shard, axis, apart):
    return lax.ppermute(shard, axis, [(i, i ^ 1 << apart) for i in range(lax.axis_size(axis))])


def swapped(shard, axis):
    size = lax.axis_size(axis)
    first = [(i, i ^ 1) for i in range(size)]
    second = [(i, i + 1 - 2 * (i % 2 == 0)) for i in range(1, size - 1)]
    return jnp.concatenate([lax.ppermute(shard, axis, first), shard, lax.ppermute(shard, axis, second)], axis=0)


def slot_multipoles(pos, stren, core):
    lanes = pos.shape[-1]
    ones = jnp.ones((lanes,), jnp.float32)
    exact = lax.Precision.HIGHEST
    rough = jnp.einsum("scl,l->sc", pos, ones, precision=exact) / lanes
    centre = rough + jnp.einsum("scl,l->sc", pos - rough[:, :, None], ones, precision=exact) / lanes
    total = jnp.einsum("scl,l->sc", stren, ones, precision=exact)
    offset = pos - centre[:, :, None]
    spread = (
        jnp.einsum("sl,l->s", core * core, ones, precision=exact) / lanes
        + jnp.sum(jnp.einsum("scl,l->sc", offset * offset, ones, precision=exact), axis=1) / lanes
    )
    return jnp.concatenate([centre, total, spread[:, None]], axis=1)


def evaluate(target, centre, sources, extra, moments):
    sep_x = target[0][None, :, None] - sources[:, 0][:, None, :]
    sep_y = target[1][None, :, None] - sources[:, 1][:, None, :]
    sep_z = target[2][None, :, None] - sources[:, 2][:, None, :]
    radius_sq = sep_x * sep_x + sep_y * sep_y + sep_z * sep_z + extra[:, 0][:, None, :]
    inverse = lax.rsqrt(radius_sq)
    weight = inverse * inverse * inverse
    sum_x = jnp.sum(sources[:, 3][:, None, :] * weight, axis=(0, 2))
    sum_y = jnp.sum(sources[:, 4][:, None, :] * weight, axis=(0, 2))
    sum_z = jnp.sum(sources[:, 5][:, None, :] * weight, axis=(0, 2))
    arm_x = jnp.sum(extra[:, 1][:, None, :] * weight, axis=(0, 2))
    arm_y = jnp.sum(extra[:, 2][:, None, :] * weight, axis=(0, 2))
    arm_z = jnp.sum(extra[:, 3][:, None, :] * weight, axis=(0, 2))
    rel_x = target[0] - centre[0]
    rel_y = target[1] - centre[1]
    rel_z = target[2] - centre[2]
    near_x = sum_y * rel_z - sum_z * rel_y - arm_x
    near_y = sum_z * rel_x - sum_x * rel_z - arm_y
    near_z = sum_x * rel_y - sum_y * rel_x - arm_z
    off_x = target[0][None, :] - moments[:, 0][:, None]
    off_y = target[1][None, :] - moments[:, 1][:, None]
    off_z = target[2][None, :] - moments[:, 2][:, None]
    far_sq = off_x * off_x + off_y * off_y + off_z * off_z + moments[:, 6][:, None]
    far_inverse = lax.rsqrt(far_sq)
    far_weight = far_inverse * far_inverse * far_inverse
    mom_x = moments[:, 3][:, None] * far_weight
    mom_y = moments[:, 4][:, None] * far_weight
    mom_z = moments[:, 5][:, None] * far_weight
    far_x = jnp.sum(mom_y * off_z - mom_z * off_y, axis=0)
    far_y = jnp.sum(mom_z * off_x - mom_x * off_z, axis=0)
    far_z = jnp.sum(mom_x * off_y - mom_y * off_x, axis=0)
    return jnp.stack([near_x + far_x, near_y + far_y, near_z + far_z], axis=0) * inv_four_pi


def source_terms(sources_all, centre):
    px = sources_all[:, :, 0] - centre[:, 0][:, None, None]
    py = sources_all[:, :, 1] - centre[:, 1][:, None, None]
    pz = sources_all[:, :, 2] - centre[:, 2][:, None, None]
    sx, sy, sz = sources_all[:, :, 3], sources_all[:, :, 4], sources_all[:, :, 5]
    core_sq = sources_all[:, :, 6] * sources_all[:, :, 6]
    extra = jnp.stack([core_sq, sy * pz - sz * py, sz * px - sx * pz, sx * py - sy * px], axis=2)
    return lax.optimization_barrier(extra)


def level_tables(moves, levels, bits_x, nbd):
    size_x, size_y = moves.shape[1], moves.shape[2]
    devices = size_x * size_y
    level_bit = np.array(
        [(1 << bits_x - 1 - level) * size_y if level < bits_x else 1 << levels - 1 - level for level in range(levels)],
        np.int32,
    )
    flat = moves.reshape(levels, devices)
    every = jnp.arange(devices, dtype=jnp.int32)
    swap = jnp.bitwise_xor(every[None, :, None], level_bit[:, None, None]) == every[None, None, :]
    mate_moves = jnp.sum(jnp.where(swap, flat[:, None, :], 0), axis=2)
    delta = flat - mate_moves
    before = nbd + jnp.sum(delta, axis=0)
    kept = []
    for level in range(levels):
        kept.append(before - flat[level])
        before = before - delta[level]
    kept = jnp.stack(kept, axis=0)
    kept_mate = jnp.sum(jnp.where(swap, kept[:, None, :], 0), axis=2)
    return kept, kept_mate, level_bit


def trace_back(loc, kept, kept_mate, level_bit, nbd):
    levels, devices = kept.shape
    every = jnp.arange(devices, dtype=jnp.int32)
    device = loc.reshape(-1) // nbd
    slot = loc.reshape(-1) % nbd
    for level in reversed(range(levels)):
        pick = device[:, None] == every[None, :]
        here = jnp.sum(jnp.where(pick, kept[level][None, :], 0), axis=1)
        there = jnp.sum(jnp.where(pick, kept_mate[level][None, :], 0), axis=1)
        moved = slot >= here
        slot = jnp.where(moved, slot - here + there, slot)
        device = jnp.where(moved, jnp.bitwise_xor(device, level_bit[level]), device)
    return device.reshape(loc.shape), slot.reshape(loc.shape)


def table_blocks(table, lanes):
    cap, width = table.shape
    pieces = -(-cap // lanes)
    wide = jnp.pad(table.T, ((0, 0), (0, pieces * lanes - cap)))
    return wide.reshape(width, pieces, lanes).transpose(1, 0, 2)


def local(positions, strength, core, moves, owner, near_list, far_list):
    column_index = lax.axis_index("gx")
    row_index = lax.axis_index("gy")
    size_x = lax.axis_size("gx")
    size_y = lax.axis_size("gy")
    bits_x = size_x.bit_length() - 1
    levels = moves.shape[0]
    cap = positions.shape[2]
    nbd = near_list.shape[2]
    lanes = positions.shape[4]
    me = column_index * size_y + row_index
    held = jnp.concatenate([positions[0, 0], strength[0, 0], core[0, 0][:, None, :]], axis=1)
    slot_table = slot_multipoles(held[:, 0:3], held[:, 3:6], held[:, 6])
    width = slot_table.shape[1]
    gathered = table_blocks(slot_table, lanes)
    pieces = gathered.shape[0]
    held = jnp.pad(held, ((0, MOVE), (0, 0), (0, 0)))
    level_bits = []
    for level in range(levels):
        if level < bits_x:
            level_bits.append((1 << bits_x - 1 - level) * size_y)
        else:
            level_bits.append(1 << levels - 1 - level)
    devices = size_x * size_y
    flat_moves = moves.reshape(levels, devices)
    every = jnp.arange(devices, dtype=jnp.int32)
    mates = jnp.bitwise_xor(me, jnp.array(level_bits, jnp.int32))
    own = jnp.sum(jnp.where(every[None, :] == me, flat_moves, 0), axis=1)
    mate_own = jnp.sum(jnp.where(every[None, :] == mates[:, None], flat_moves, 0), axis=1)
    count = nbd + jnp.sum(own - mate_own, keepdims=True)
    slot_ids = jnp.arange(held.shape[0], dtype=jnp.int32)
    move_ids = jnp.arange(MOVE, dtype=jnp.int32)
    exact = lax.Precision.HIGHEST
    for level in range(levels):
        if level < bits_x:
            axis_name, bit_at = "gx", bits_x - 1 - level
        else:
            axis_name, bit_at = "gy", levels - 1 - level
        count = count - own[level : level + 1]
        take = (slot_ids[None, :] == (count + move_ids)[:, None]).astype(jnp.float32)
        leaving = jnp.einsum("ms,scl->mcl", take, held, precision=exact)
        payload = jnp.concatenate([leaving, gathered], axis=0)
        got = from_partner(payload, axis_name, bit_at)
        arriving = got[:MOVE]
        gathered = jnp.concatenate([gathered, got[MOVE:]], axis=0)
        put = slot_ids[:, None] == (count + move_ids)[None, :]
        placed = jnp.einsum("sm,mcl->scl", put.astype(jnp.float32), arriving, precision=exact)
        held = jnp.where(jnp.any(put, axis=1)[:, None, None], placed, held)
        count = count + mate_own[level : level + 1]
        if level == min(1, levels - 1):
            moves_late, near_late, _ = lax.optimization_barrier((moves, near_list[0, 0], held))
            kept, kept_mate, level_bit = level_tables(moves_late, levels, bits_x, nbd)
            near_where = owner[near_late]
        if level == min(2, levels - 1):
            far_late, _ = lax.optimization_barrier((far_list[0, 0], held))
            far_where = owner[far_late]
            far_device, far_slot = trace_back(far_where, kept, kept_mate, level_bit, nbd)
    blocks = held[:nbd]
    relative = jnp.bitwise_xor(far_device, me)
    entry = jnp.zeros_like(relative)
    for level in range(levels):
        entry = entry + ((relative // level_bits[level]) % 2) * (1 << level)
    all_table = gathered.reshape(-1, pieces, width, lanes).transpose(0, 1, 3, 2).reshape(-1, width)
    moments = all_table[entry * (pieces * lanes) + far_slot]
    source_device = near_where // nbd
    source_slot = near_where % nbd
    delta_x = source_device // size_y - column_index
    delta_y = source_device % size_y - row_index
    sign_x = 2 * (column_index % 2) - 1
    sign_y = 2 * (row_index % 2) - 1
    source_pool = swapped(swapped(blocks, "gx"), "gy")
    pool_index = ((1 + delta_y * sign_y) * 3 + (1 + delta_x * sign_x)) * nbd + source_slot
    sources_all = source_pool[pool_index]
    targets = blocks[:, 0:3]
    centre = jnp.mean(targets, axis=2)
    extra = source_terms(sources_all, centre)
    velocity = jax.vmap(evaluate)(targets, centre, sources_all, extra, moments)
    return velocity[None, None]


def solution(mesh):
    placed = (
        P("gx", "gy", None, None, None),
        P("gx", "gy", None, None, None),
        P("gx", "gy", None, None),
        P(),
        P(),
        P("gx", "gy", None, None),
        P("gx", "gy", None, None),
    )
    return jax.shard_map(
        local,
        mesh=mesh,
        in_specs=placed,
        out_specs=P("gx", "gy", None, None, None),
        check_vma=False,
    )
```

```python
import math

import jax
import jax.numpy as jnp
import numpy as np
from jax import lax
from jax.sharding import PartitionSpec as P

MOVE = 8


inv_four_pi = 0.25 / math.pi


def from_partner(shard, axis, apart):
    return lax.ppermute(shard, axis, [(i, i ^ 1 << apart) for i in range(lax.axis_size(axis))])


def swapped(shard, axis):
    size = lax.axis_size(axis)
    first = [(i, i ^ 1) for i in range(size)]
    second = [(i, i + 1 - 2 * (i % 2 == 0)) for i in range(1, size - 1)]
    return jnp.concatenate([lax.ppermute(shard, axis, first), shard, lax.ppermute(shard, axis, second)], axis=0)


def slot_multipoles(pos, stren, core):
    lanes = pos.shape[-1]
    ones = jnp.ones((lanes,), jnp.float32)
    exact = lax.Precision.HIGHEST
    rough = jnp.einsum("scl,l->sc", pos, ones, precision=exact) / lanes
    centre = rough + jnp.einsum("scl,l->sc", pos - rough[:, :, None], ones, precision=exact) / lanes
    total = jnp.einsum("scl,l->sc", stren, ones, precision=exact)
    offset = pos - centre[:, :, None]
    spread = (
        jnp.einsum("sl,l->s", core * core, ones, precision=exact) / lanes
        + jnp.sum(jnp.einsum("scl,l->sc", offset * offset, ones, precision=exact), axis=1) / lanes
    )
    return jnp.concatenate([centre, total, spread[:, None]], axis=1)


def evaluate(target, centre, sources, extra, moments):
    sep_x = target[0][None, :, None] - sources[:, 0][:, None, :]
    sep_y = target[1][None, :, None] - sources[:, 1][:, None, :]
    sep_z = target[2][None, :, None] - sources[:, 2][:, None, :]
    radius_sq = sep_x * sep_x + sep_y * sep_y + sep_z * sep_z + extra[:, 0][:, None, :]
    inverse = lax.rsqrt(radius_sq)
    weight = inverse * inverse * inverse
    sum_x = jnp.sum(sources[:, 3][:, None, :] * weight, axis=(0, 2))
    sum_y = jnp.sum(sources[:, 4][:, None, :] * weight, axis=(0, 2))
    sum_z = jnp.sum(sources[:, 5][:, None, :] * weight, axis=(0, 2))
    arm_x = jnp.sum(extra[:, 1][:, None, :] * weight, axis=(0, 2))
    arm_y = jnp.sum(extra[:, 2][:, None, :] * weight, axis=(0, 2))
    arm_z = jnp.sum(extra[:, 3][:, None, :] * weight, axis=(0, 2))
    rel_x = target[0] - centre[0]
    rel_y = target[1] - centre[1]
    rel_z = target[2] - centre[2]
    near_x = sum_y * rel_z - sum_z * rel_y - arm_x
    near_y = sum_z * rel_x - sum_x * rel_z - arm_y
    near_z = sum_x * rel_y - sum_y * rel_x - arm_z
    off_x = target[0][None, :] - moments[:, 0][:, None]
    off_y = target[1][None, :] - moments[:, 1][:, None]
    off_z = target[2][None, :] - moments[:, 2][:, None]
    far_sq = off_x * off_x + off_y * off_y + off_z * off_z + moments[:, 6][:, None]
    far_inverse = lax.rsqrt(far_sq)
    far_weight = far_inverse * far_inverse * far_inverse
    mom_x = moments[:, 3][:, None] * far_weight
    mom_y = moments[:, 4][:, None] * far_weight
    mom_z = moments[:, 5][:, None] * far_weight
    far_x = jnp.sum(mom_y * off_z - mom_z * off_y, axis=0)
    far_y = jnp.sum(mom_z * off_x - mom_x * off_z, axis=0)
    far_z = jnp.sum(mom_x * off_y - mom_y * off_x, axis=0)
    return jnp.stack([near_x + far_x, near_y + far_y, near_z + far_z], axis=0) * inv_four_pi


def source_terms(sources_all, centre):
    px = sources_all[:, :, 0] - centre[:, 0][:, None, None]
    py = sources_all[:, :, 1] - centre[:, 1][:, None, None]
    pz = sources_all[:, :, 2] - centre[:, 2][:, None, None]
    sx, sy, sz = sources_all[:, :, 3], sources_all[:, :, 4], sources_all[:, :, 5]
    core_sq = sources_all[:, :, 6] * sources_all[:, :, 6]
    extra = jnp.stack([core_sq, sy * pz - sz * py, sz * px - sx * pz, sx * py - sy * px], axis=2)
    return lax.optimization_barrier(extra)


def trace_back(loc, moves, levels, bits_x, nbd):
    size_x, size_y = moves.shape[1], moves.shape[2]
    devices = size_x * size_y
    level_bit = np.array(
        [(1 << bits_x - 1 - level) * size_y if level < bits_x else 1 << levels - 1 - level for level in range(levels)],
        np.int32,
    )
    flat = moves.reshape(levels, devices)
    every = jnp.arange(devices, dtype=jnp.int32)
    swap = jnp.bitwise_xor(every[None, :, None], level_bit[:, None, None]) == every[None, None, :]
    mate_moves = jnp.sum(jnp.where(swap, flat[:, None, :], 0), axis=2)
    delta = flat - mate_moves
    before = nbd + jnp.sum(delta, axis=0)
    kept = []
    for level in range(levels):
        kept.append(before - flat[level])
        before = before - delta[level]
    kept = jnp.stack(kept, axis=0)
    kept_mate = jnp.sum(jnp.where(swap, kept[:, None, :], 0), axis=2)
    device = loc.reshape(-1) // nbd
    slot = loc.reshape(-1) % nbd
    for level in reversed(range(levels)):
        pick = device[:, None] == every[None, :]
        here = jnp.sum(jnp.where(pick, kept[level][None, :], 0), axis=1)
        there = jnp.sum(jnp.where(pick, kept_mate[level][None, :], 0), axis=1)
        moved = slot >= here
        slot = jnp.where(moved, slot - here + there, slot)
        device = jnp.where(moved, jnp.bitwise_xor(device, level_bit[level]), device)
    return device.reshape(loc.shape), slot.reshape(loc.shape)


def table_blocks(table, lanes):
    cap, width = table.shape
    pieces = -(-cap // lanes)
    wide = jnp.pad(table.T, ((0, 0), (0, pieces * lanes - cap)))
    return wide.reshape(width, pieces, lanes).transpose(1, 0, 2)


def local(positions, strength, core, moves, owner, near_list, far_list):
    column_index = lax.axis_index("gx")
    row_index = lax.axis_index("gy")
    size_x = lax.axis_size("gx")
    size_y = lax.axis_size("gy")
    bits_x = size_x.bit_length() - 1
    levels = moves.shape[0]
    cap = positions.shape[2]
    nbd = near_list.shape[2]
    lanes = positions.shape[4]
    me = column_index * size_y + row_index
    held = jnp.concatenate([positions[0, 0], strength[0, 0], core[0, 0][:, None, :]], axis=1)
    held = lax.optimization_barrier(held)
    slot_table = slot_multipoles(held[:, 0:3], held[:, 3:6], held[:, 6])
    width = slot_table.shape[1]
    gathered = table_blocks(slot_table, lanes)
    pieces = gathered.shape[0]
    far_where = owner[far_list[0, 0]]
    far_device, far_slot = trace_back(far_where, moves, levels, bits_x, nbd)
    held = jnp.pad(held, ((0, MOVE), (0, 0), (0, 0)))
    plans = []
    level_bits = []
    for level in range(levels):
        if level < bits_x:
            bit_at = bits_x - 1 - level
            mate_moves = moves[level, jnp.bitwise_xor(column_index, 1 << bit_at), row_index]
            level_bits.append((1 << bit_at) * size_y)
        else:
            bit_at = levels - 1 - level
            mate_moves = moves[level, column_index, jnp.bitwise_xor(row_index, 1 << bit_at)]
            level_bits.append(1 << bit_at)
        plans.append((bit_at, moves[level, column_index, row_index], mate_moves))
    count = jnp.int32(nbd)
    for plan_item in plans:
        count = count + plan_item[1] - plan_item[2]
    for level in range(levels):
        bit_at, own_moves, mate_moves = plans[level]
        leaving = lax.dynamic_slice_in_dim(held, count - own_moves, MOVE, 0)
        payload = jnp.concatenate([leaving, gathered], axis=0)
        if level < bits_x:
            got = from_partner(payload, "gx", bit_at)
        else:
            got = from_partner(payload, "gy", bit_at)
        arriving = got[:MOVE]
        gathered = jnp.concatenate([gathered, got[MOVE:]], axis=0)
        count = count - own_moves
        held = lax.dynamic_update_slice_in_dim(held, arriving, count, 0)
        count = count + mate_moves
    blocks = held[:nbd]
    relative = jnp.bitwise_xor(far_device, me)
    entry = jnp.zeros_like(relative)
    for level in range(levels):
        entry = entry + ((relative // level_bits[level]) % 2) * (1 << level)
    all_table = gathered.reshape(-1, pieces, width, lanes).transpose(0, 1, 3, 2).reshape(-1, width)
    moments = all_table[entry * (pieces * lanes) + far_slot]
    near_where = owner[near_list[0, 0]]
    source_device = near_where // nbd
    source_slot = near_where % nbd
    delta_x = source_device // size_y - column_index
    delta_y = source_device % size_y - row_index
    sign_x = 2 * (column_index % 2) - 1
    sign_y = 2 * (row_index % 2) - 1
    source_pool = swapped(swapped(blocks, "gx"), "gy")
    pool_index = ((1 + delta_y * sign_y) * 3 + (1 + delta_x * sign_x)) * nbd + source_slot
    sources_all = source_pool[pool_index]
    targets = blocks[:, 0:3]
    centre = jnp.mean(targets, axis=2)
    extra = source_terms(sources_all, centre)
    velocity = jax.vmap(evaluate)(targets, centre, sources_all, extra, moments)
    return velocity[None, None]


def solution(mesh):
    placed = (
        P("gx", "gy", None, None, None),
        P("gx", "gy", None, None, None),
        P("gx", "gy", None, None),
        P(),
        P(),
        P("gx", "gy", None, None),
        P("gx", "gy", None, None),
    )
    return jax.shard_map(
        local,
        mesh=mesh,
        in_specs=placed,
        out_specs=P("gx", "gy", None, None, None),
        check_vma=False,
    )
```

```python
import math

import jax
import jax.numpy as jnp
import numpy as np
from jax import lax
from jax.sharding import PartitionSpec as P

MOVE = 8


inv_four_pi = 0.25 / math.pi


def from_partner(shard, axis, apart):
    return lax.ppermute(shard, axis, [(i, i ^ 1 << apart) for i in range(lax.axis_size(axis))])


def swapped(shard, axis):
    size = lax.axis_size(axis)
    first = [(i, i ^ 1) for i in range(size)]
    second = [(i, i + 1 - 2 * (i % 2 == 0)) for i in range(1, size - 1)]
    return jnp.concatenate([lax.ppermute(shard, axis, first), shard, lax.ppermute(shard, axis, second)], axis=0)


def slot_multipoles(pos, stren, core):
    lanes = pos.shape[-1]
    ones = jnp.ones((lanes,), jnp.float32)
    exact = lax.Precision.HIGHEST
    rough = jnp.einsum("scl,l->sc", pos, ones, precision=exact) / lanes
    centre = rough + jnp.einsum("scl,l->sc", pos - rough[:, :, None], ones, precision=exact) / lanes
    total = jnp.einsum("scl,l->sc", stren, ones, precision=exact)
    offset = pos - centre[:, :, None]
    spread = (
        jnp.einsum("sl,l->s", core * core, ones, precision=exact) / lanes
        + jnp.sum(jnp.einsum("scl,l->sc", offset * offset, ones, precision=exact), axis=1) / lanes
    )
    return jnp.concatenate([centre, total, spread[:, None]], axis=1)


def evaluate(target, centre, sources, extra, moments):
    sep_x = target[0][None, :, None] - sources[:, 0][:, None, :]
    sep_y = target[1][None, :, None] - sources[:, 1][:, None, :]
    sep_z = target[2][None, :, None] - sources[:, 2][:, None, :]
    radius_sq = sep_x * sep_x + sep_y * sep_y + sep_z * sep_z + extra[:, 0][:, None, :]
    inverse = lax.rsqrt(radius_sq)
    weight = inverse * inverse * inverse
    sum_x = jnp.sum(sources[:, 3][:, None, :] * weight, axis=(0, 2))
    sum_y = jnp.sum(sources[:, 4][:, None, :] * weight, axis=(0, 2))
    sum_z = jnp.sum(sources[:, 5][:, None, :] * weight, axis=(0, 2))
    arm_x = jnp.sum(extra[:, 1][:, None, :] * weight, axis=(0, 2))
    arm_y = jnp.sum(extra[:, 2][:, None, :] * weight, axis=(0, 2))
    arm_z = jnp.sum(extra[:, 3][:, None, :] * weight, axis=(0, 2))
    rel_x = target[0] - centre[0]
    rel_y = target[1] - centre[1]
    rel_z = target[2] - centre[2]
    near_x = sum_y * rel_z - sum_z * rel_y - arm_x
    near_y = sum_z * rel_x - sum_x * rel_z - arm_y
    near_z = sum_x * rel_y - sum_y * rel_x - arm_z
    off_x = target[0][None, :] - moments[:, 0][:, None]
    off_y = target[1][None, :] - moments[:, 1][:, None]
    off_z = target[2][None, :] - moments[:, 2][:, None]
    far_sq = off_x * off_x + off_y * off_y + off_z * off_z + moments[:, 6][:, None]
    far_inverse = lax.rsqrt(far_sq)
    far_weight = far_inverse * far_inverse * far_inverse
    mom_x = moments[:, 3][:, None] * far_weight
    mom_y = moments[:, 4][:, None] * far_weight
    mom_z = moments[:, 5][:, None] * far_weight
    far_x = jnp.sum(mom_y * off_z - mom_z * off_y, axis=0)
    far_y = jnp.sum(mom_z * off_x - mom_x * off_z, axis=0)
    far_z = jnp.sum(mom_x * off_y - mom_y * off_x, axis=0)
    return jnp.stack([near_x + far_x, near_y + far_y, near_z + far_z], axis=0) * inv_four_pi


def source_terms(sources_all, centre):
    px = sources_all[:, :, 0] - centre[:, 0][:, None, None]
    py = sources_all[:, :, 1] - centre[:, 1][:, None, None]
    pz = sources_all[:, :, 2] - centre[:, 2][:, None, None]
    sx, sy, sz = sources_all[:, :, 3], sources_all[:, :, 4], sources_all[:, :, 5]
    core_sq = sources_all[:, :, 6] * sources_all[:, :, 6]
    extra = jnp.stack([core_sq, sy * pz - sz * py, sz * px - sx * pz, sx * py - sy * px], axis=2)
    return lax.optimization_barrier(extra)


def level_tables(moves, levels, bits_x, nbd):
    size_x, size_y = moves.shape[1], moves.shape[2]
    devices = size_x * size_y
    level_bit = np.array(
        [(1 << bits_x - 1 - level) * size_y if level < bits_x else 1 << levels - 1 - level for level in range(levels)],
        np.int32,
    )
    flat = moves.reshape(levels, devices)
    every = jnp.arange(devices, dtype=jnp.int32)
    swap = jnp.bitwise_xor(every[None, :, None], level_bit[:, None, None]) == every[None, None, :]
    mate_moves = jnp.sum(jnp.where(swap, flat[:, None, :], 0), axis=2)
    delta = flat - mate_moves
    before = nbd + jnp.sum(delta, axis=0)
    kept = []
    for level in range(levels):
        kept.append(before - flat[level])
        before = before - delta[level]
    kept = jnp.stack(kept, axis=0)
    kept_mate = jnp.sum(jnp.where(swap, kept[:, None, :], 0), axis=2)
    return kept, kept_mate, level_bit


def trace_back(loc, kept, kept_mate, level_bit, nbd):
    levels, devices = kept.shape
    every = jnp.arange(devices, dtype=jnp.int32)
    device = loc.reshape(-1) // nbd
    slot = loc.reshape(-1) % nbd
    for level in reversed(range(levels)):
        pick = device[:, None] == every[None, :]
        here = jnp.sum(jnp.where(pick, kept[level][None, :], 0), axis=1)
        there = jnp.sum(jnp.where(pick, kept_mate[level][None, :], 0), axis=1)
        moved = slot >= here
        slot = jnp.where(moved, slot - here + there, slot)
        device = jnp.where(moved, jnp.bitwise_xor(device, level_bit[level]), device)
    return device.reshape(loc.shape), slot.reshape(loc.shape)


def table_blocks(table, lanes):
    cap, width = table.shape
    pieces = -(-cap // lanes)
    wide = jnp.pad(table.T, ((0, 0), (0, pieces * lanes - cap)))
    return wide.reshape(width, pieces, lanes).transpose(1, 0, 2)


def local(positions, strength, core, moves, owner, near_list, far_list):
    column_index = lax.axis_index("gx")
    row_index = lax.axis_index("gy")
    size_x = lax.axis_size("gx")
    size_y = lax.axis_size("gy")
    bits_x = size_x.bit_length() - 1
    levels = moves.shape[0]
    cap = positions.shape[2]
    nbd = near_list.shape[2]
    lanes = positions.shape[4]
    me = column_index * size_y + row_index
    held = jnp.concatenate([positions[0, 0], strength[0, 0], core[0, 0][:, None, :]], axis=1)
    held = lax.optimization_barrier(held)
    slot_table = slot_multipoles(held[:, 0:3], held[:, 3:6], held[:, 6])
    width = slot_table.shape[1]
    gathered = table_blocks(slot_table, lanes)
    pieces = gathered.shape[0]
    held = jnp.pad(held, ((0, MOVE), (0, 0), (0, 0)))
    level_bits = []
    for level in range(levels):
        if level < bits_x:
            level_bits.append((1 << bits_x - 1 - level) * size_y)
        else:
            level_bits.append(1 << levels - 1 - level)
    devices = size_x * size_y
    flat_moves = moves.reshape(levels, devices)
    every = jnp.arange(devices, dtype=jnp.int32)
    mates = jnp.bitwise_xor(me, jnp.array(level_bits, jnp.int32))
    own = jnp.sum(jnp.where(every[None, :] == me, flat_moves, 0), axis=1)
    mate_own = jnp.sum(jnp.where(every[None, :] == mates[:, None], flat_moves, 0), axis=1)
    count = nbd + jnp.sum(own - mate_own, keepdims=True)
    slot_ids = jnp.arange(held.shape[0], dtype=jnp.int32)
    move_ids = jnp.arange(MOVE, dtype=jnp.int32)
    exact = lax.Precision.HIGHEST
    for level in range(levels):
        if level < bits_x:
            axis_name, bit_at = "gx", bits_x - 1 - level
        else:
            axis_name, bit_at = "gy", levels - 1 - level
        count = count - own[level : level + 1]
        take = (slot_ids[None, :] == (count + move_ids)[:, None]).astype(jnp.float32)
        leaving = jnp.einsum("ms,scl->mcl", take, held, precision=exact)
        payload = jnp.concatenate([leaving, gathered], axis=0)
        got = from_partner(payload, axis_name, bit_at)
        arriving = got[:MOVE]
        gathered = jnp.concatenate([gathered, got[MOVE:]], axis=0)
        put = slot_ids[:, None] == (count + move_ids)[None, :]
        placed = jnp.einsum("sm,mcl->scl", put.astype(jnp.float32), arriving, precision=exact)
        held = jnp.where(jnp.any(put, axis=1)[:, None, None], placed, held)
        count = count + mate_own[level : level + 1]
    far_where = owner[far_list[0, 0]]
    kept, kept_mate, level_bit = level_tables(moves, levels, bits_x, nbd)
    far_device, far_slot = trace_back(far_where, kept, kept_mate, level_bit, nbd)
    blocks = held[:nbd]
    relative = jnp.bitwise_xor(far_device, me)
    entry = jnp.zeros_like(relative)
    for level in range(levels):
        entry = entry + ((relative // level_bits[level]) % 2) * (1 << level)
    all_table = gathered.reshape(-1, pieces, width, lanes).transpose(0, 1, 3, 2).reshape(-1, width)
    moments = all_table[entry * (pieces * lanes) + far_slot]
    near_where = owner[near_list[0, 0]]
    source_device = near_where // nbd
    source_slot = near_where % nbd
    delta_x = source_device // size_y - column_index
    delta_y = source_device % size_y - row_index
    sign_x = 2 * (column_index % 2) - 1
    sign_y = 2 * (row_index % 2) - 1
    source_pool = swapped(swapped(blocks, "gx"), "gy")
    pool_index = ((1 + delta_y * sign_y) * 3 + (1 + delta_x * sign_x)) * nbd + source_slot
    sources_all = source_pool[pool_index]
    targets = blocks[:, 0:3]
    centre = jnp.mean(targets, axis=2)
    extra = source_terms(sources_all, centre)
    velocity = jax.vmap(evaluate)(targets, centre, sources_all, extra, moments)
    return velocity[None, None]


def solution(mesh):
    placed = (
        P("gx", "gy", None, None, None),
        P("gx", "gy", None, None, None),
        P("gx", "gy", None, None),
        P(),
        P(),
        P("gx", "gy", None, None),
        P("gx", "gy", None, None),
    )
    return jax.shard_map(
        local,
        mesh=mesh,
        in_specs=placed,
        out_specs=P("gx", "gy", None, None, None),
        check_vma=False,
    )
```

```python
import math

import jax
import jax.numpy as jnp
import numpy as np
from jax import lax
from jax.sharding import PartitionSpec as P

MOVE = 8


inv_four_pi = 0.25 / math.pi


def from_partner(shard, axis, apart):
    return lax.ppermute(shard, axis, [(i, i ^ 1 << apart) for i in range(lax.axis_size(axis))])


def swapped(shard, axis, wrap=False):
    size = lax.axis_size(axis)
    first = [(i, i ^ 1) for i in range(size)]
    second = [(i, i + 1 - 2 * (i % 2 == 0)) for i in range(1, size - 1)]
    if wrap and size > 2:
        second = second + [(0, size - 1), (size - 1, 0)]
    return jnp.concatenate([lax.ppermute(shard, axis, first), shard, lax.ppermute(shard, axis, second)], axis=0)


def slot_multipoles(pos, stren, core):
    lanes = pos.shape[-1]
    ones = jnp.ones((lanes,), jnp.float32)
    exact = lax.Precision.HIGHEST
    rough = jnp.einsum("scl,l->sc", pos, ones, precision=exact) / lanes
    centre = rough + jnp.einsum("scl,l->sc", pos - rough[:, :, None], ones, precision=exact) / lanes
    total = jnp.einsum("scl,l->sc", stren, ones, precision=exact)
    offset = pos - centre[:, :, None]
    spread = (
        jnp.einsum("sl,l->s", core * core, ones, precision=exact) / lanes
        + jnp.sum(jnp.einsum("scl,l->sc", offset * offset, ones, precision=exact), axis=1) / lanes
    )
    return jnp.concatenate([centre, total, spread[:, None]], axis=1)


def evaluate(target, centre, sources, extra, moments):
    sep_x = target[0][None, :, None] - sources[:, 0][:, None, :]
    sep_y = target[1][None, :, None] - sources[:, 1][:, None, :]
    sep_z = target[2][None, :, None] - sources[:, 2][:, None, :]
    radius_sq = sep_x * sep_x + sep_y * sep_y + sep_z * sep_z + extra[:, 0][:, None, :]
    inverse = lax.rsqrt(radius_sq)
    weight = inverse * inverse * inverse
    sum_x = jnp.sum(sources[:, 3][:, None, :] * weight, axis=(0, 2))
    sum_y = jnp.sum(sources[:, 4][:, None, :] * weight, axis=(0, 2))
    sum_z = jnp.sum(sources[:, 5][:, None, :] * weight, axis=(0, 2))
    arm_x = jnp.sum(extra[:, 1][:, None, :] * weight, axis=(0, 2))
    arm_y = jnp.sum(extra[:, 2][:, None, :] * weight, axis=(0, 2))
    arm_z = jnp.sum(extra[:, 3][:, None, :] * weight, axis=(0, 2))
    rel_x = target[0] - centre[0]
    rel_y = target[1] - centre[1]
    rel_z = target[2] - centre[2]
    near_x = sum_y * rel_z - sum_z * rel_y - arm_x
    near_y = sum_z * rel_x - sum_x * rel_z - arm_y
    near_z = sum_x * rel_y - sum_y * rel_x - arm_z
    off_x = target[0][None, :] - moments[:, 0][:, None]
    off_y = target[1][None, :] - moments[:, 1][:, None]
    off_z = target[2][None, :] - moments[:, 2][:, None]
    far_sq = off_x * off_x + off_y * off_y + off_z * off_z + moments[:, 6][:, None]
    far_inverse = lax.rsqrt(far_sq)
    far_weight = far_inverse * far_inverse * far_inverse
    mom_x = moments[:, 3][:, None] * far_weight
    mom_y = moments[:, 4][:, None] * far_weight
    mom_z = moments[:, 5][:, None] * far_weight
    far_x = jnp.sum(mom_y * off_z - mom_z * off_y, axis=0)
    far_y = jnp.sum(mom_z * off_x - mom_x * off_z, axis=0)
    far_z = jnp.sum(mom_x * off_y - mom_y * off_x, axis=0)
    return jnp.stack([near_x + far_x, near_y + far_y, near_z + far_z], axis=0) * inv_four_pi


def source_terms(sources_all, centre):
    px = sources_all[:, :, 0] - centre[:, 0][:, None, None]
    py = sources_all[:, :, 1] - centre[:, 1][:, None, None]
    pz = sources_all[:, :, 2] - centre[:, 2][:, None, None]
    sx, sy, sz = sources_all[:, :, 3], sources_all[:, :, 4], sources_all[:, :, 5]
    core_sq = sources_all[:, :, 6] * sources_all[:, :, 6]
    extra = jnp.stack([core_sq, sy * pz - sz * py, sz * px - sx * pz, sx * py - sy * px], axis=2)
    return lax.optimization_barrier(extra)


def trace_back(loc, moves, levels, bits_x, nbd):
    size_x, size_y = moves.shape[1], moves.shape[2]
    devices = size_x * size_y
    level_bit = np.array(
        [(1 << bits_x - 1 - level) * size_y if level < bits_x else 1 << levels - 1 - level for level in range(levels)],
        np.int32,
    )
    flat = moves.reshape(levels, devices)
    every = jnp.arange(devices, dtype=jnp.int32)
    swap = jnp.bitwise_xor(every[None, :, None], level_bit[:, None, None]) == every[None, None, :]
    mate_moves = jnp.sum(jnp.where(swap, flat[:, None, :], 0), axis=2)
    delta = flat - mate_moves
    before = nbd + jnp.sum(delta, axis=0)
    kept = []
    for level in range(levels):
        kept.append(before - flat[level])
        before = before - delta[level]
    kept = jnp.stack(kept, axis=0)
    kept_mate = jnp.sum(jnp.where(swap, kept[:, None, :], 0), axis=2)
    device = loc.reshape(-1) // nbd
    slot = loc.reshape(-1) % nbd
    for level in reversed(range(levels)):
        pick = device[:, None] == every[None, :]
        here = jnp.sum(jnp.where(pick, kept[level][None, :], 0), axis=1)
        there = jnp.sum(jnp.where(pick, kept_mate[level][None, :], 0), axis=1)
        moved = slot >= here
        slot = jnp.where(moved, slot - here + there, slot)
        device = jnp.where(moved, jnp.bitwise_xor(device, level_bit[level]), device)
    return device.reshape(loc.shape), slot.reshape(loc.shape)


def table_blocks(table, lanes):
    cap, width = table.shape
    pieces = -(-cap // lanes)
    wide = jnp.pad(table.T, ((0, 0), (0, pieces * lanes - cap)))
    return wide.reshape(width, pieces, lanes).transpose(1, 0, 2)


def local(positions, strength, core, moves, owner, near_list, far_list):
    column_index = lax.axis_index("gx")
    row_index = lax.axis_index("gy")
    size_x = lax.axis_size("gx")
    size_y = lax.axis_size("gy")
    bits_x = size_x.bit_length() - 1
    levels = moves.shape[0]
    cap = positions.shape[2]
    nbd = near_list.shape[2]
    lanes = positions.shape[4]
    me = column_index * size_y + row_index
    held = jnp.concatenate([positions[0, 0], strength[0, 0], core[0, 0][:, None, :]], axis=1)
    held = lax.optimization_barrier(held)
    slot_table = slot_multipoles(held[:, 0:3], held[:, 3:6], held[:, 6])
    width = slot_table.shape[1]
    gathered = table_blocks(slot_table, lanes)
    pieces = gathered.shape[0]
    far_where = owner[far_list[0, 0]]
    far_device, far_slot = trace_back(far_where, moves, levels, bits_x, nbd)
    held = jnp.pad(held, ((0, MOVE), (0, 0), (0, 0)))
    plans = []
    level_bits = []
    for level in range(levels):
        if level < bits_x:
            bit_at = bits_x - 1 - level
            mate_moves = moves[level, jnp.bitwise_xor(column_index, 1 << bit_at), row_index]
            level_bits.append((1 << bit_at) * size_y)
        else:
            bit_at = levels - 1 - level
            mate_moves = moves[level, column_index, jnp.bitwise_xor(row_index, 1 << bit_at)]
            level_bits.append(1 << bit_at)
        plans.append((bit_at, moves[level, column_index, row_index], mate_moves))
    count = jnp.int32(nbd)
    for plan_item in plans:
        count = count + plan_item[1] - plan_item[2]
    for level in range(levels):
        bit_at, own_moves, mate_moves = plans[level]
        leaving = lax.dynamic_slice_in_dim(held, count - own_moves, MOVE, 0)
        payload = jnp.concatenate([leaving, gathered], axis=0)
        if level < bits_x:
            got = from_partner(payload, "gx", bit_at)
        else:
            got = from_partner(payload, "gy", bit_at)
        arriving = got[:MOVE]
        gathered = jnp.concatenate([gathered, got[MOVE:]], axis=0)
        count = count - own_moves
        held = lax.dynamic_update_slice_in_dim(held, arriving, count, 0)
        count = count + mate_moves
    blocks = held[:nbd]
    relative = jnp.bitwise_xor(far_device, me)
    entry = jnp.zeros_like(relative)
    for level in range(levels):
        entry = entry + ((relative // level_bits[level]) % 2) * (1 << level)
    all_table = gathered.reshape(-1, pieces, width, lanes).transpose(0, 1, 3, 2).reshape(-1, width)
    moments = all_table[entry * (pieces * lanes) + far_slot]
    near_where = owner[near_list[0, 0]]
    source_device = near_where // nbd
    source_slot = near_where % nbd
    delta_x = source_device // size_y - column_index
    delta_y = source_device % size_y - row_index
    sign_x = 2 * (column_index % 2) - 1
    sign_y = 2 * (row_index % 2) - 1
    source_pool = swapped(swapped(blocks, "gx"), "gy", wrap=True)
    pool_index = ((1 + delta_y * sign_y) * 3 + (1 + delta_x * sign_x)) * nbd + source_slot
    sources_all = source_pool[pool_index]
    targets = blocks[:, 0:3]
    centre = jnp.mean(targets, axis=2)
    extra = source_terms(sources_all, centre)
    velocity = jax.vmap(evaluate)(targets, centre, sources_all, extra, moments)
    return velocity[None, None]


def solution(mesh):
    placed = (
        P("gx", "gy", None, None, None),
        P("gx", "gy", None, None, None),
        P("gx", "gy", None, None),
        P(),
        P(),
        P("gx", "gy", None, None),
        P("gx", "gy", None, None),
    )
    return jax.shard_map(
        local,
        mesh=mesh,
        in_specs=placed,
        out_specs=P("gx", "gy", None, None, None),
        check_vma=False,
    )
```

```python
import math

import jax
import jax.numpy as jnp
import numpy as np
from jax import lax
from jax.sharding import PartitionSpec as P

MOVE = 8


inv_four_pi = 0.25 / math.pi


def from_partner(shard, axis, apart):
    return lax.ppermute(shard, axis, [(i, i ^ 1 << apart) for i in range(lax.axis_size(axis))])


def swapped(shard, axis):
    size = lax.axis_size(axis)
    first = [(i, i ^ 1) for i in range(size)]
    second = [(i, i + 1 - 2 * (i % 2 == 0)) for i in range(1, size - 1)]
    return jnp.concatenate([lax.ppermute(shard, axis, first), shard, lax.ppermute(shard, axis, second)], axis=0)


def slot_multipoles(pos, stren, core):
    lanes = pos.shape[-1]
    ones = jnp.ones((lanes,), jnp.float32)
    exact = lax.Precision.HIGHEST
    rough = jnp.einsum("scl,l->sc", pos, ones, precision=exact) / lanes
    centre = rough + jnp.einsum("scl,l->sc", pos - rough[:, :, None], ones, precision=exact) / lanes
    total = jnp.einsum("scl,l->sc", stren, ones, precision=exact)
    offset = pos - centre[:, :, None]
    spread = (
        jnp.einsum("sl,l->s", core * core, ones, precision=exact) / lanes
        + jnp.sum(jnp.einsum("scl,l->sc", offset * offset, ones, precision=exact), axis=1) / lanes
    )
    return jnp.concatenate([centre, total, spread[:, None]], axis=1)


def evaluate(target, centre, sources, extra, moments):
    sep_x = target[0][None, :, None] - sources[:, 0][:, None, :]
    sep_y = target[1][None, :, None] - sources[:, 1][:, None, :]
    sep_z = target[2][None, :, None] - sources[:, 2][:, None, :]
    radius_sq = sep_x * sep_x + sep_y * sep_y + sep_z * sep_z + extra[:, 0][:, None, :]
    inverse = lax.rsqrt(radius_sq)
    weight = inverse * inverse * inverse
    sum_x = jnp.sum(sources[:, 3][:, None, :] * weight, axis=(0, 2))
    sum_y = jnp.sum(sources[:, 4][:, None, :] * weight, axis=(0, 2))
    sum_z = jnp.sum(sources[:, 5][:, None, :] * weight, axis=(0, 2))
    arm_x = jnp.sum(extra[:, 1][:, None, :] * weight, axis=(0, 2))
    arm_y = jnp.sum(extra[:, 2][:, None, :] * weight, axis=(0, 2))
    arm_z = jnp.sum(extra[:, 3][:, None, :] * weight, axis=(0, 2))
    rel_x = target[0] - centre[0]
    rel_y = target[1] - centre[1]
    rel_z = target[2] - centre[2]
    near_x = sum_y * rel_z - sum_z * rel_y - arm_x
    near_y = sum_z * rel_x - sum_x * rel_z - arm_y
    near_z = sum_x * rel_y - sum_y * rel_x - arm_z
    off_x = target[0][None, :] - moments[:, 0][:, None]
    off_y = target[1][None, :] - moments[:, 1][:, None]
    off_z = target[2][None, :] - moments[:, 2][:, None]
    far_sq = off_x * off_x + off_y * off_y + off_z * off_z + moments[:, 6][:, None]
    far_inverse = lax.rsqrt(far_sq)
    far_weight = far_inverse * far_inverse * far_inverse
    mom_x = moments[:, 3][:, None] * far_weight
    mom_y = moments[:, 4][:, None] * far_weight
    mom_z = moments[:, 5][:, None] * far_weight
    far_x = jnp.sum(mom_y * off_z - mom_z * off_y, axis=0)
    far_y = jnp.sum(mom_z * off_x - mom_x * off_z, axis=0)
    far_z = jnp.sum(mom_x * off_y - mom_y * off_x, axis=0)
    return jnp.stack([near_x + far_x, near_y + far_y, near_z + far_z], axis=0) * inv_four_pi


def source_terms(sources_all, centre):
    px = sources_all[:, :, 0] - centre[:, 0][:, None, None]
    py = sources_all[:, :, 1] - centre[:, 1][:, None, None]
    pz = sources_all[:, :, 2] - centre[:, 2][:, None, None]
    sx, sy, sz = sources_all[:, :, 3], sources_all[:, :, 4], sources_all[:, :, 5]
    core_sq = sources_all[:, :, 6] * sources_all[:, :, 6]
    extra = jnp.stack([core_sq, sy * pz - sz * py, sz * px - sx * pz, sx * py - sy * px], axis=2)
    return lax.optimization_barrier(extra)


def trace_back(loc, moves, levels, bits_x, nbd):
    size_x, size_y = moves.shape[1], moves.shape[2]
    devices = size_x * size_y
    level_bit = np.array(
        [(1 << bits_x - 1 - level) * size_y if level < bits_x else 1 << levels - 1 - level for level in range(levels)],
        np.int32,
    )
    flat = moves.reshape(levels, devices)
    every = jnp.arange(devices, dtype=jnp.int32)
    swap = jnp.bitwise_xor(every[None, :, None], level_bit[:, None, None]) == every[None, None, :]
    mate_moves = jnp.sum(jnp.where(swap, flat[:, None, :], 0), axis=2)
    delta = flat - mate_moves
    before = nbd + jnp.sum(delta, axis=0)
    kept = []
    for level in range(levels):
        kept.append(before - flat[level])
        before = before - delta[level]
    kept = jnp.stack(kept, axis=0)
    kept_mate = jnp.sum(jnp.where(swap, kept[:, None, :], 0), axis=2)
    device = loc.reshape(-1) // nbd
    slot = loc.reshape(-1) % nbd
    for level in reversed(range(levels)):
        pick = device[:, None] == every[None, :]
        here = jnp.sum(jnp.where(pick, kept[level][None, :], 0), axis=1)
        there = jnp.sum(jnp.where(pick, kept_mate[level][None, :], 0), axis=1)
        moved = slot >= here
        slot = jnp.where(moved, slot - here + there, slot)
        device = jnp.where(moved, jnp.bitwise_xor(device, level_bit[level]), device)
    return device.reshape(loc.shape), slot.reshape(loc.shape)


def table_blocks(table, lanes):
    cap, width = table.shape
    pieces = -(-cap // lanes)
    wide = jnp.pad(table.T, ((0, 0), (0, pieces * lanes - cap)))
    return wide.reshape(width, pieces, lanes).transpose(1, 0, 2)


def local(positions, strength, core, moves, owner, near_list, far_list):
    column_index = lax.axis_index("gx")
    row_index = lax.axis_index("gy")
    size_x = lax.axis_size("gx")
    size_y = lax.axis_size("gy")
    bits_x = size_x.bit_length() - 1
    levels = moves.shape[0]
    cap = positions.shape[2]
    nbd = near_list.shape[2]
    lanes = positions.shape[4]
    me = column_index * size_y + row_index
    held = jnp.concatenate([positions[0, 0], strength[0, 0], core[0, 0][:, None, :]], axis=1)
    held = lax.optimization_barrier(held)
    slot_table = slot_multipoles(held[:, 0:3], held[:, 3:6], held[:, 6])
    width = slot_table.shape[1]
    gathered = table_blocks(slot_table, lanes)
    pieces = gathered.shape[0]
    far_where = owner[far_list[0, 0]]
    far_device, far_slot = trace_back(far_where, moves, levels, bits_x, nbd)
    held = jnp.pad(held, ((0, MOVE), (0, 0), (0, 0)))
    plans = []
    level_bits = []
    for level in range(levels):
        if level < bits_x:
            bit_at = bits_x - 1 - level
            mate_moves = moves[level, jnp.bitwise_xor(column_index, 1 << bit_at), row_index]
            level_bits.append((1 << bit_at) * size_y)
        else:
            bit_at = levels - 1 - level
            mate_moves = moves[level, column_index, jnp.bitwise_xor(row_index, 1 << bit_at)]
            level_bits.append(1 << bit_at)
        plans.append((bit_at, moves[level, column_index, row_index], mate_moves))
    count = jnp.int32(nbd)
    for plan_item in plans:
        count = count + plan_item[1] - plan_item[2]
    for level in range(levels):
        bit_at, own_moves, mate_moves = plans[level]
        leaving = lax.dynamic_slice_in_dim(held, count - own_moves, MOVE, 0)
        payload = jnp.concatenate([leaving, gathered], axis=0)
        if level < bits_x:
            got = from_partner(payload, "gx", bit_at)
        else:
            got = from_partner(payload, "gy", bit_at)
        arriving = got[:MOVE]
        gathered = jnp.concatenate([gathered, got[MOVE:]], axis=0)
        count = count - own_moves
        held = lax.dynamic_update_slice_in_dim(held, arriving, count, 0)
        count = count + mate_moves
    blocks = held[:nbd]
    relative = jnp.bitwise_xor(far_device, me)
    entry = jnp.zeros_like(relative)
    for level in range(levels):
        entry = entry + ((relative // level_bits[level]) % 2) * (1 << level)
    all_table = gathered.reshape(-1, pieces, width, lanes).transpose(0, 1, 3, 2).reshape(-1, width)
    moments = all_table[entry * (pieces * lanes) + far_slot]
    near_where = owner[near_list[0, 0]]
    source_device = near_where // nbd
    source_slot = near_where % nbd
    delta_x = source_device // size_y - column_index
    delta_y = source_device % size_y - row_index
    sign_x = 2 * (column_index % 2) - 1
    sign_y = 2 * (row_index % 2) - 1
    row = swapped(blocks, "gx")
    column = swapped(blocks, "gy")
    corners = swapped(jnp.concatenate([row[:nbd], row[2 * nbd :]], axis=0), "gy")
    source_pool = jnp.concatenate([row, column, corners], axis=0)
    pos_x = 1 + delta_x * sign_x
    pos_y = 1 + delta_y * sign_y
    pool_index = jnp.where(
        delta_y == 0,
        pos_x * nbd,
        jnp.where(delta_x == 0, 3 * nbd + pos_y * nbd, 6 * nbd + pos_y * 2 * nbd + (pos_x // 2) * nbd),
    ) + source_slot
    sources_all = source_pool[pool_index]
    targets = blocks[:, 0:3]
    centre = jnp.mean(targets, axis=2)
    extra = source_terms(sources_all, centre)
    velocity = jax.vmap(evaluate)(targets, centre, sources_all, extra, moments)
    return velocity[None, None]


def solution(mesh):
    placed = (
        P("gx", "gy", None, None, None),
        P("gx", "gy", None, None, None),
        P("gx", "gy", None, None),
        P(),
        P(),
        P("gx", "gy", None, None),
        P("gx", "gy", None, None),
    )
    return jax.shard_map(
        local,
        mesh=mesh,
        in_specs=placed,
        out_specs=P("gx", "gy", None, None, None),
        check_vma=False,
    )
```

```python
import math

import jax
import jax.numpy as jnp
import numpy as np
from jax import lax
from jax.sharding import PartitionSpec as P

MOVE = 8


inv_four_pi = 0.25 / math.pi


def from_partner(shard, axis, apart):
    return lax.ppermute(shard, axis, [(i, i ^ 1 << apart) for i in range(lax.axis_size(axis))])


def swapped(shard, axis):
    size = lax.axis_size(axis)
    first = [(i, i ^ 1) for i in range(size)]
    second = [(i, i + 1 - 2 * (i % 2 == 0)) for i in range(1, size - 1)]
    return jnp.concatenate([lax.ppermute(shard, axis, first), shard, lax.ppermute(shard, axis, second)], axis=0)


def slot_multipoles(pos, stren, core):
    lanes = pos.shape[-1]
    ones = jnp.ones((lanes,), jnp.float32)
    exact = lax.Precision.HIGHEST
    rough = jnp.einsum("scl,l->sc", pos, ones, precision=exact) / lanes
    centre = rough + jnp.einsum("scl,l->sc", pos - rough[:, :, None], ones, precision=exact) / lanes
    total = jnp.einsum("scl,l->sc", stren, ones, precision=exact)
    offset = pos - centre[:, :, None]
    spread = (
        jnp.einsum("sl,l->s", core * core, ones, precision=exact) / lanes
        + jnp.sum(jnp.einsum("scl,l->sc", offset * offset, ones, precision=exact), axis=1) / lanes
    )
    return jnp.concatenate([centre, total, spread[:, None]], axis=1)


def evaluate(target, centre, sources, extra, moments):
    sep_x = target[0][None, :, None] - sources[:, 0][:, None, :]
    sep_y = target[1][None, :, None] - sources[:, 1][:, None, :]
    sep_z = target[2][None, :, None] - sources[:, 2][:, None, :]
    radius_sq = sep_x * sep_x + sep_y * sep_y + sep_z * sep_z + extra[:, 0][:, None, :]
    inverse = lax.rsqrt(radius_sq)
    weight = inverse * inverse * inverse
    sum_x = jnp.sum(sources[:, 3][:, None, :] * weight, axis=(0, 2))
    sum_y = jnp.sum(sources[:, 4][:, None, :] * weight, axis=(0, 2))
    sum_z = jnp.sum(sources[:, 5][:, None, :] * weight, axis=(0, 2))
    arm_x = jnp.sum(extra[:, 1][:, None, :] * weight, axis=(0, 2))
    arm_y = jnp.sum(extra[:, 2][:, None, :] * weight, axis=(0, 2))
    arm_z = jnp.sum(extra[:, 3][:, None, :] * weight, axis=(0, 2))
    rel_x = target[0] - centre[0]
    rel_y = target[1] - centre[1]
    rel_z = target[2] - centre[2]
    near_x = sum_y * rel_z - sum_z * rel_y - arm_x
    near_y = sum_z * rel_x - sum_x * rel_z - arm_y
    near_z = sum_x * rel_y - sum_y * rel_x - arm_z
    off_x = target[0][None, :] - moments[:, 0][:, None]
    off_y = target[1][None, :] - moments[:, 1][:, None]
    off_z = target[2][None, :] - moments[:, 2][:, None]
    far_sq = off_x * off_x + off_y * off_y + off_z * off_z + moments[:, 6][:, None]
    far_inverse = lax.rsqrt(far_sq)
    far_weight = far_inverse * far_inverse * far_inverse
    mom_x = moments[:, 3][:, None] * far_weight
    mom_y = moments[:, 4][:, None] * far_weight
    mom_z = moments[:, 5][:, None] * far_weight
    far_x = jnp.sum(mom_y * off_z - mom_z * off_y, axis=0)
    far_y = jnp.sum(mom_z * off_x - mom_x * off_z, axis=0)
    far_z = jnp.sum(mom_x * off_y - mom_y * off_x, axis=0)
    return jnp.stack([near_x + far_x, near_y + far_y, near_z + far_z], axis=0) * inv_four_pi


def source_terms(sources_all, centre):
    px = sources_all[:, :, 0] - centre[:, 0][:, None, None]
    py = sources_all[:, :, 1] - centre[:, 1][:, None, None]
    pz = sources_all[:, :, 2] - centre[:, 2][:, None, None]
    sx, sy, sz = sources_all[:, :, 3], sources_all[:, :, 4], sources_all[:, :, 5]
    core_sq = sources_all[:, :, 6] * sources_all[:, :, 6]
    extra = jnp.stack([core_sq, sy * pz - sz * py, sz * px - sx * pz, sx * py - sy * px], axis=2)
    return lax.optimization_barrier(extra)


def trace_back(loc, moves, levels, bits_x, nbd):
    size_x, size_y = moves.shape[1], moves.shape[2]
    devices = size_x * size_y
    level_bit = np.array(
        [(1 << bits_x - 1 - level) * size_y if level < bits_x else 1 << levels - 1 - level for level in range(levels)],
        np.int32,
    )
    flat = moves.reshape(levels, devices)
    every = jnp.arange(devices, dtype=jnp.int32)
    swap = jnp.bitwise_xor(every[None, :, None], level_bit[:, None, None]) == every[None, None, :]
    mate_moves = jnp.sum(jnp.where(swap, flat[:, None, :], 0), axis=2)
    delta = flat - mate_moves
    before = nbd + jnp.sum(delta, axis=0)
    kept = []
    for level in range(levels):
        kept.append(before - flat[level])
        before = before - delta[level]
    kept = jnp.stack(kept, axis=0)
    kept_mate = jnp.sum(jnp.where(swap, kept[:, None, :], 0), axis=2)
    device = loc.reshape(-1) // nbd
    slot = loc.reshape(-1) % nbd
    for level in reversed(range(levels)):
        pick = device[:, None] == every[None, :]
        here = jnp.sum(jnp.where(pick, kept[level][None, :], 0), axis=1)
        there = jnp.sum(jnp.where(pick, kept_mate[level][None, :], 0), axis=1)
        moved = slot >= here
        slot = jnp.where(moved, slot - here + there, slot)
        device = jnp.where(moved, jnp.bitwise_xor(device, level_bit[level]), device)
    return device.reshape(loc.shape), slot.reshape(loc.shape)


def table_blocks(table, lanes):
    cap, width = table.shape
    pieces = -(-cap // lanes)
    wide = jnp.pad(table.T, ((0, 0), (0, pieces * lanes - cap)))
    return wide.reshape(width, pieces, lanes).transpose(1, 0, 2)


def local(positions, strength, core, moves, owner, near_list, far_list):
    column_index = lax.axis_index("gx")
    row_index = lax.axis_index("gy")
    size_x = lax.axis_size("gx")
    size_y = lax.axis_size("gy")
    bits_x = size_x.bit_length() - 1
    levels = moves.shape[0]
    cap = positions.shape[2]
    nbd = near_list.shape[2]
    lanes = positions.shape[4]
    me = column_index * size_y + row_index
    held = jnp.concatenate([positions[0, 0], strength[0, 0], core[0, 0][:, None, :]], axis=1)
    held = lax.optimization_barrier(held)
    slot_table = slot_multipoles(held[:, 0:3], held[:, 3:6], held[:, 6])
    width = slot_table.shape[1]
    gathered = table_blocks(slot_table, lanes)
    pieces = gathered.shape[0]
    far_where = owner[far_list[0, 0]]
    far_device, far_slot = trace_back(far_where, moves, levels, bits_x, nbd)
    held = jnp.pad(held, ((0, MOVE), (0, 0), (0, 0)))
    plans = []
    level_bits = []
    for level in range(levels):
        if level < bits_x:
            bit_at = bits_x - 1 - level
            mate_moves = moves[level, jnp.bitwise_xor(column_index, 1 << bit_at), row_index]
            level_bits.append((1 << bit_at) * size_y)
        else:
            bit_at = levels - 1 - level
            mate_moves = moves[level, column_index, jnp.bitwise_xor(row_index, 1 << bit_at)]
            level_bits.append(1 << bit_at)
        plans.append((bit_at, moves[level, column_index, row_index], mate_moves))
    count = jnp.int32(nbd)
    for plan_item in plans:
        count = count + plan_item[1] - plan_item[2]
    for level in range(levels):
        bit_at, own_moves, mate_moves = plans[level]
        leaving = lax.dynamic_slice_in_dim(held, count - own_moves, MOVE, 0)
        payload = jnp.concatenate([leaving, gathered], axis=0)
        if level < bits_x:
            got = from_partner(payload, "gx", bit_at)
        else:
            got = from_partner(payload, "gy", bit_at)
        arriving = got[:MOVE]
        gathered = jnp.concatenate([gathered, got[MOVE:]], axis=0)
        count = count - own_moves
        held = lax.dynamic_update_slice_in_dim(held, arriving, count, 0)
        count = count + mate_moves
    blocks = held[:nbd]
    relative = jnp.bitwise_xor(far_device, me)
    entry = jnp.zeros_like(relative)
    for level in range(levels):
        entry = entry + ((relative // level_bits[level]) % 2) * (1 << level)
    all_table = gathered.reshape(-1, pieces, width, lanes).transpose(0, 1, 3, 2).reshape(-1, width)
    moments = all_table[entry * (pieces * lanes) + far_slot]
    near_where = owner[near_list[0, 0]]
    source_device = near_where // nbd
    source_slot = near_where % nbd
    delta_x = source_device // size_y - column_index
    delta_y = source_device % size_y - row_index
    sign_x = 2 * (column_index % 2) - 1
    row = swapped(blocks, "gx")
    size_y_axis = lax.axis_size("gy")
    from_below = lax.ppermute(row, "gy", [(i, i + 1) for i in range(size_y_axis - 1)])
    from_above = lax.ppermute(row, "gy", [(i + 1, i) for i in range(size_y_axis - 1)])
    source_pool = jnp.concatenate([from_below, row, from_above], axis=0)
    pool_index = ((1 + delta_y) * 3 + (1 + delta_x * sign_x)) * nbd + source_slot
    sources_all = source_pool[pool_index]
    targets = blocks[:, 0:3]
    centre = jnp.mean(targets, axis=2)
    extra = source_terms(sources_all, centre)
    velocity = jax.vmap(evaluate)(targets, centre, sources_all, extra, moments)
    return velocity[None, None]


def solution(mesh):
    placed = (
        P("gx", "gy", None, None, None),
        P("gx", "gy", None, None, None),
        P("gx", "gy", None, None),
        P(),
        P(),
        P("gx", "gy", None, None),
        P("gx", "gy", None, None),
    )
    return jax.shard_map(
        local,
        mesh=mesh,
        in_specs=placed,
        out_specs=P("gx", "gy", None, None, None),
        check_vma=False,
    )
```

```python
import math

import jax
import jax.numpy as jnp
import numpy as np
from jax import lax
from jax.experimental.layout import Layout, with_layout_constraint
from jax.sharding import PartitionSpec as P

MOVE = 8


inv_four_pi = 0.25 / math.pi


def from_partner(shard, axis, apart):
    return lax.ppermute(shard, axis, [(i, i ^ 1 << apart) for i in range(lax.axis_size(axis))])


def swapped(shard, axis, dim=0):
    size = lax.axis_size(axis)
    first = [(i, i ^ 1) for i in range(size)]
    second = [(i, i + 1 - 2 * (i % 2 == 0)) for i in range(1, size - 1)]
    return jnp.concatenate([lax.ppermute(shard, axis, first), shard, lax.ppermute(shard, axis, second)], axis=dim)


def slot_multipoles(pos, stren, core):
    lanes = pos.shape[-1]
    ones = jnp.ones((lanes,), jnp.float32)
    exact = lax.Precision.HIGHEST
    rough = jnp.einsum("scl,l->sc", pos, ones, precision=exact) / lanes
    centre = rough + jnp.einsum("scl,l->sc", pos - rough[:, :, None], ones, precision=exact) / lanes
    total = jnp.einsum("scl,l->sc", stren, ones, precision=exact)
    offset = pos - centre[:, :, None]
    spread = (
        jnp.einsum("sl,l->s", core * core, ones, precision=exact) / lanes
        + jnp.sum(jnp.einsum("scl,l->sc", offset * offset, ones, precision=exact), axis=1) / lanes
    )
    return jnp.concatenate([centre, total, spread[:, None]], axis=1)


def evaluate(target, centre, sources, extra, moments):
    sep_x = target[0][None, :, None] - sources[:, 0][:, None, :]
    sep_y = target[1][None, :, None] - sources[:, 1][:, None, :]
    sep_z = target[2][None, :, None] - sources[:, 2][:, None, :]
    radius_sq = sep_x * sep_x + sep_y * sep_y + sep_z * sep_z + extra[:, 0][:, None, :]
    inverse = lax.rsqrt(radius_sq)
    weight = inverse * inverse * inverse
    sum_x = jnp.sum(sources[:, 3][:, None, :] * weight, axis=(0, 2))
    sum_y = jnp.sum(sources[:, 4][:, None, :] * weight, axis=(0, 2))
    sum_z = jnp.sum(sources[:, 5][:, None, :] * weight, axis=(0, 2))
    arm_x = jnp.sum(extra[:, 1][:, None, :] * weight, axis=(0, 2))
    arm_y = jnp.sum(extra[:, 2][:, None, :] * weight, axis=(0, 2))
    arm_z = jnp.sum(extra[:, 3][:, None, :] * weight, axis=(0, 2))
    rel_x = target[0] - centre[0]
    rel_y = target[1] - centre[1]
    rel_z = target[2] - centre[2]
    near_x = sum_y * rel_z - sum_z * rel_y - arm_x
    near_y = sum_z * rel_x - sum_x * rel_z - arm_y
    near_z = sum_x * rel_y - sum_y * rel_x - arm_z
    off_x = target[0][None, :] - moments[:, 0][:, None]
    off_y = target[1][None, :] - moments[:, 1][:, None]
    off_z = target[2][None, :] - moments[:, 2][:, None]
    far_sq = off_x * off_x + off_y * off_y + off_z * off_z + moments[:, 6][:, None]
    far_inverse = lax.rsqrt(far_sq)
    far_weight = far_inverse * far_inverse * far_inverse
    mom_x = moments[:, 3][:, None] * far_weight
    mom_y = moments[:, 4][:, None] * far_weight
    mom_z = moments[:, 5][:, None] * far_weight
    far_x = jnp.sum(mom_y * off_z - mom_z * off_y, axis=0)
    far_y = jnp.sum(mom_z * off_x - mom_x * off_z, axis=0)
    far_z = jnp.sum(mom_x * off_y - mom_y * off_x, axis=0)
    return jnp.stack([near_x + far_x, near_y + far_y, near_z + far_z], axis=0) * inv_four_pi


def source_terms(sources_all, centre):
    px = sources_all[:, :, 0] - centre[:, 0][:, None, None]
    py = sources_all[:, :, 1] - centre[:, 1][:, None, None]
    pz = sources_all[:, :, 2] - centre[:, 2][:, None, None]
    sx, sy, sz = sources_all[:, :, 3], sources_all[:, :, 4], sources_all[:, :, 5]
    core_sq = sources_all[:, :, 6] * sources_all[:, :, 6]
    extra = jnp.stack([core_sq, sy * pz - sz * py, sz * px - sx * pz, sx * py - sy * px], axis=2)
    return lax.optimization_barrier(extra)


def trace_back(loc, moves, levels, bits_x, nbd):
    size_x, size_y = moves.shape[1], moves.shape[2]
    devices = size_x * size_y
    level_bit = np.array(
        [(1 << bits_x - 1 - level) * size_y if level < bits_x else 1 << levels - 1 - level for level in range(levels)],
        np.int32,
    )
    flat = moves.reshape(levels, devices)
    every = jnp.arange(devices, dtype=jnp.int32)
    swap = jnp.bitwise_xor(every[None, :, None], level_bit[:, None, None]) == every[None, None, :]
    mate_moves = jnp.sum(jnp.where(swap, flat[:, None, :], 0), axis=2)
    delta = flat - mate_moves
    before = nbd + jnp.sum(delta, axis=0)
    kept = []
    for level in range(levels):
        kept.append(before - flat[level])
        before = before - delta[level]
    kept = jnp.stack(kept, axis=0)
    kept_mate = jnp.sum(jnp.where(swap, kept[:, None, :], 0), axis=2)
    device = loc.reshape(-1) // nbd
    slot = loc.reshape(-1) % nbd
    for level in reversed(range(levels)):
        pick = device[:, None] == every[None, :]
        here = jnp.sum(jnp.where(pick, kept[level][None, :], 0), axis=1)
        there = jnp.sum(jnp.where(pick, kept_mate[level][None, :], 0), axis=1)
        moved = slot >= here
        slot = jnp.where(moved, slot - here + there, slot)
        device = jnp.where(moved, jnp.bitwise_xor(device, level_bit[level]), device)
    return device.reshape(loc.shape), slot.reshape(loc.shape)


def table_blocks(table, lanes):
    cap, width = table.shape
    pieces = -(-cap // lanes)
    wide = jnp.pad(table.T, ((0, 0), (0, pieces * lanes - cap)))
    return wide.reshape(width, pieces, lanes).transpose(1, 0, 2)


def local(positions, strength, core, moves, owner, near_list, far_list):
    column_index = lax.axis_index("gx")
    row_index = lax.axis_index("gy")
    size_x = lax.axis_size("gx")
    size_y = lax.axis_size("gy")
    bits_x = size_x.bit_length() - 1
    levels = moves.shape[0]
    cap = positions.shape[2]
    nbd = near_list.shape[2]
    lanes = positions.shape[4]
    me = column_index * size_y + row_index
    held = jnp.concatenate([positions[0, 0], strength[0, 0], core[0, 0][:, None, :]], axis=1)
    held = lax.optimization_barrier(held)
    slot_table = slot_multipoles(held[:, 0:3], held[:, 3:6], held[:, 6])
    width = slot_table.shape[1]
    gathered = table_blocks(slot_table, lanes)
    pieces = gathered.shape[0]
    far_where = owner[far_list[0, 0]]
    far_device, far_slot = trace_back(far_where, moves, levels, bits_x, nbd)
    held = jnp.pad(held, ((0, MOVE), (0, 0), (0, 0)))
    plans = []
    level_bits = []
    for level in range(levels):
        if level < bits_x:
            bit_at = bits_x - 1 - level
            mate_moves = moves[level, jnp.bitwise_xor(column_index, 1 << bit_at), row_index]
            level_bits.append((1 << bit_at) * size_y)
        else:
            bit_at = levels - 1 - level
            mate_moves = moves[level, column_index, jnp.bitwise_xor(row_index, 1 << bit_at)]
            level_bits.append(1 << bit_at)
        plans.append((bit_at, moves[level, column_index, row_index], mate_moves))
    count = jnp.int32(nbd)
    for plan_item in plans:
        count = count + plan_item[1] - plan_item[2]
    for level in range(levels):
        bit_at, own_moves, mate_moves = plans[level]
        leaving = lax.dynamic_slice_in_dim(held, count - own_moves, MOVE, 0)
        payload = jnp.concatenate([leaving, gathered], axis=0)
        if level < bits_x:
            got = from_partner(payload, "gx", bit_at)
        else:
            got = from_partner(payload, "gy", bit_at)
        arriving = got[:MOVE]
        gathered = jnp.concatenate([gathered, got[MOVE:]], axis=0)
        count = count - own_moves
        held = lax.dynamic_update_slice_in_dim(held, arriving, count, 0)
        count = count + mate_moves
    blocks = held[:nbd]
    relative = jnp.bitwise_xor(far_device, me)
    entry = jnp.zeros_like(relative)
    for level in range(levels):
        entry = entry + ((relative // level_bits[level]) % 2) * (1 << level)
    all_table = gathered.reshape(-1, pieces, width, lanes).transpose(0, 1, 3, 2).reshape(-1, width)
    moments = all_table[entry * (pieces * lanes) + far_slot]
    near_where = owner[near_list[0, 0]]
    source_device = near_where // nbd
    source_slot = near_where % nbd
    delta_x = source_device // size_y - column_index
    delta_y = source_device % size_y - row_index
    sign_x = 2 * (column_index % 2) - 1
    sign_y = 2 * (row_index % 2) - 1
    dense = with_layout_constraint(jnp.transpose(blocks, (1, 0, 2)), Layout(major_to_minor=(0, 1, 2)))
    source_pool = swapped(swapped(dense, "gx", 1), "gy", 1)
    pool_index = ((1 + delta_y * sign_y) * 3 + (1 + delta_x * sign_x)) * nbd + source_slot
    sources_all = jnp.transpose(source_pool[:, pool_index], (1, 2, 0, 3))
    targets = blocks[:, 0:3]
    centre = jnp.mean(targets, axis=2)
    extra = source_terms(sources_all, centre)
    velocity = jax.vmap(evaluate)(targets, centre, sources_all, extra, moments)
    return velocity[None, None]


def solution(mesh):
    placed = (
        P("gx", "gy", None, None, None),
        P("gx", "gy", None, None, None),
        P("gx", "gy", None, None),
        P(),
        P(),
        P("gx", "gy", None, None),
        P("gx", "gy", None, None),
    )
    return jax.shard_map(
        local,
        mesh=mesh,
        in_specs=placed,
        out_specs=P("gx", "gy", None, None, None),
        check_vma=False,
    )
```

```python
import math

import jax
import jax.numpy as jnp
import numpy as np
from jax import lax
from jax.experimental.layout import Layout, with_layout_constraint
from jax.sharding import PartitionSpec as P

MOVE = 8


inv_four_pi = 0.25 / math.pi


def from_partner(shard, axis, apart):
    return lax.ppermute(shard, axis, [(i, i ^ 1 << apart) for i in range(lax.axis_size(axis))])


def swapped(shard, axis, dim=0):
    size = lax.axis_size(axis)
    first = [(i, i ^ 1) for i in range(size)]
    second = [(i, i + 1 - 2 * (i % 2 == 0)) for i in range(1, size - 1)]
    return jnp.concatenate([lax.ppermute(shard, axis, first), shard, lax.ppermute(shard, axis, second)], axis=dim)


def slot_multipoles(pos, stren, core):
    lanes = pos.shape[-1]
    ones = jnp.ones((lanes,), jnp.float32)
    exact = lax.Precision.HIGHEST
    rough = jnp.einsum("scl,l->sc", pos, ones, precision=exact) / lanes
    centre = rough + jnp.einsum("scl,l->sc", pos - rough[:, :, None], ones, precision=exact) / lanes
    total = jnp.einsum("scl,l->sc", stren, ones, precision=exact)
    offset = pos - centre[:, :, None]
    spread = (
        jnp.einsum("sl,l->s", core * core, ones, precision=exact) / lanes
        + jnp.sum(jnp.einsum("scl,l->sc", offset * offset, ones, precision=exact), axis=1) / lanes
    )
    return jnp.concatenate([centre, total, spread[:, None]], axis=1)


def evaluate(target, centre, sources, extra, moments):
    sep_x = target[0][None, :, None] - sources[:, 0][:, None, :]
    sep_y = target[1][None, :, None] - sources[:, 1][:, None, :]
    sep_z = target[2][None, :, None] - sources[:, 2][:, None, :]
    radius_sq = sep_x * sep_x + sep_y * sep_y + sep_z * sep_z + extra[:, 0][:, None, :]
    inverse = lax.rsqrt(radius_sq)
    weight = inverse * inverse * inverse
    sum_x = jnp.sum(sources[:, 3][:, None, :] * weight, axis=(0, 2))
    sum_y = jnp.sum(sources[:, 4][:, None, :] * weight, axis=(0, 2))
    sum_z = jnp.sum(sources[:, 5][:, None, :] * weight, axis=(0, 2))
    arm_x = jnp.sum(extra[:, 1][:, None, :] * weight, axis=(0, 2))
    arm_y = jnp.sum(extra[:, 2][:, None, :] * weight, axis=(0, 2))
    arm_z = jnp.sum(extra[:, 3][:, None, :] * weight, axis=(0, 2))
    rel_x = target[0] - centre[0]
    rel_y = target[1] - centre[1]
    rel_z = target[2] - centre[2]
    near_x = sum_y * rel_z - sum_z * rel_y - arm_x
    near_y = sum_z * rel_x - sum_x * rel_z - arm_y
    near_z = sum_x * rel_y - sum_y * rel_x - arm_z
    off_x = target[0][None, :] - moments[:, 0][:, None]
    off_y = target[1][None, :] - moments[:, 1][:, None]
    off_z = target[2][None, :] - moments[:, 2][:, None]
    far_sq = off_x * off_x + off_y * off_y + off_z * off_z + moments[:, 6][:, None]
    far_inverse = lax.rsqrt(far_sq)
    far_weight = far_inverse * far_inverse * far_inverse
    mom_x = moments[:, 3][:, None] * far_weight
    mom_y = moments[:, 4][:, None] * far_weight
    mom_z = moments[:, 5][:, None] * far_weight
    far_x = jnp.sum(mom_y * off_z - mom_z * off_y, axis=0)
    far_y = jnp.sum(mom_z * off_x - mom_x * off_z, axis=0)
    far_z = jnp.sum(mom_x * off_y - mom_y * off_x, axis=0)
    return jnp.stack([near_x + far_x, near_y + far_y, near_z + far_z], axis=0) * inv_four_pi


def source_terms(sources_all, centre):
    px = sources_all[:, :, 0] - centre[:, 0][:, None, None]
    py = sources_all[:, :, 1] - centre[:, 1][:, None, None]
    pz = sources_all[:, :, 2] - centre[:, 2][:, None, None]
    sx, sy, sz = sources_all[:, :, 3], sources_all[:, :, 4], sources_all[:, :, 5]
    core_sq = sources_all[:, :, 6] * sources_all[:, :, 6]
    extra = jnp.stack([core_sq, sy * pz - sz * py, sz * px - sx * pz, sx * py - sy * px], axis=2)
    return lax.optimization_barrier(extra)


def trace_back(loc, moves, levels, bits_x, nbd):
    size_x, size_y = moves.shape[1], moves.shape[2]
    devices = size_x * size_y
    level_bit = np.array(
        [(1 << bits_x - 1 - level) * size_y if level < bits_x else 1 << levels - 1 - level for level in range(levels)],
        np.int32,
    )
    flat = moves.reshape(levels, devices)
    every = jnp.arange(devices, dtype=jnp.int32)
    swap = jnp.bitwise_xor(every[None, :, None], level_bit[:, None, None]) == every[None, None, :]
    mate_moves = jnp.sum(jnp.where(swap, flat[:, None, :], 0), axis=2)
    delta = flat - mate_moves
    before = nbd + jnp.sum(delta, axis=0)
    kept = []
    for level in range(levels):
        kept.append(before - flat[level])
        before = before - delta[level]
    kept = jnp.stack(kept, axis=0)
    kept_mate = jnp.sum(jnp.where(swap, kept[:, None, :], 0), axis=2)
    device = loc.reshape(-1) // nbd
    slot = loc.reshape(-1) % nbd
    for level in reversed(range(levels)):
        pick = device[:, None] == every[None, :]
        here = jnp.sum(jnp.where(pick, kept[level][None, :], 0), axis=1)
        there = jnp.sum(jnp.where(pick, kept_mate[level][None, :], 0), axis=1)
        moved = slot >= here
        slot = jnp.where(moved, slot - here + there, slot)
        device = jnp.where(moved, jnp.bitwise_xor(device, level_bit[level]), device)
    return device.reshape(loc.shape), slot.reshape(loc.shape)


def table_blocks(table, lanes):
    cap, width = table.shape
    pieces = -(-cap // lanes)
    wide = jnp.pad(table.T, ((0, 0), (0, pieces * lanes - cap)))
    return wide.reshape(width, pieces, lanes).transpose(1, 0, 2)


def local(positions, strength, core, moves, owner, near_list, far_list):
    column_index = lax.axis_index("gx")
    row_index = lax.axis_index("gy")
    size_x = lax.axis_size("gx")
    size_y = lax.axis_size("gy")
    bits_x = size_x.bit_length() - 1
    levels = moves.shape[0]
    cap = positions.shape[2]
    nbd = near_list.shape[2]
    lanes = positions.shape[4]
    me = column_index * size_y + row_index
    held = jnp.concatenate([positions[0, 0], strength[0, 0], core[0, 0][:, None, :]], axis=1)
    held = lax.optimization_barrier(held)
    slot_table = slot_multipoles(held[:, 0:3], held[:, 3:6], held[:, 6])
    width = slot_table.shape[1]
    gathered = table_blocks(slot_table, lanes)
    pieces = gathered.shape[0]
    far_where = owner[far_list[0, 0]]
    far_device, far_slot = trace_back(far_where, moves, levels, bits_x, nbd)
    held = jnp.pad(held, ((0, MOVE), (0, 0), (0, 0)))
    plans = []
    level_bits = []
    for level in range(levels):
        if level < bits_x:
            bit_at = bits_x - 1 - level
            mate_moves = moves[level, jnp.bitwise_xor(column_index, 1 << bit_at), row_index]
            level_bits.append((1 << bit_at) * size_y)
        else:
            bit_at = levels - 1 - level
            mate_moves = moves[level, column_index, jnp.bitwise_xor(row_index, 1 << bit_at)]
            level_bits.append(1 << bit_at)
        plans.append((bit_at, moves[level, column_index, row_index], mate_moves))
    count = jnp.int32(nbd)
    for plan_item in plans:
        count = count + plan_item[1] - plan_item[2]
    for level in range(levels):
        bit_at, own_moves, mate_moves = plans[level]
        leaving = lax.dynamic_slice_in_dim(held, count - own_moves, MOVE, 0)
        payload = jnp.concatenate([leaving, gathered], axis=0)
        payload = with_layout_constraint(jnp.transpose(payload, (1, 0, 2)), Layout(major_to_minor=(0, 1, 2)))
        if level < bits_x:
            got = from_partner(payload, "gx", bit_at)
        else:
            got = from_partner(payload, "gy", bit_at)
        got = jnp.transpose(got, (1, 0, 2))
        arriving = got[:MOVE]
        gathered = jnp.concatenate([gathered, got[MOVE:]], axis=0)
        count = count - own_moves
        held = lax.dynamic_update_slice_in_dim(held, arriving, count, 0)
        count = count + mate_moves
    blocks = held[:nbd]
    relative = jnp.bitwise_xor(far_device, me)
    entry = jnp.zeros_like(relative)
    for level in range(levels):
        entry = entry + ((relative // level_bits[level]) % 2) * (1 << level)
    all_table = gathered.reshape(-1, pieces, width, lanes).transpose(0, 1, 3, 2).reshape(-1, width)
    moments = all_table[entry * (pieces * lanes) + far_slot]
    near_where = owner[near_list[0, 0]]
    source_device = near_where // nbd
    source_slot = near_where % nbd
    delta_x = source_device // size_y - column_index
    delta_y = source_device % size_y - row_index
    sign_x = 2 * (column_index % 2) - 1
    sign_y = 2 * (row_index % 2) - 1
    dense = with_layout_constraint(jnp.transpose(blocks, (1, 0, 2)), Layout(major_to_minor=(0, 1, 2)))
    source_pool = swapped(swapped(dense, "gx", 1), "gy", 1)
    pool_index = ((1 + delta_y * sign_y) * 3 + (1 + delta_x * sign_x)) * nbd + source_slot
    sources_all = jnp.transpose(source_pool[:, pool_index], (1, 2, 0, 3))
    targets = blocks[:, 0:3]
    centre = jnp.mean(targets, axis=2)
    extra = source_terms(sources_all, centre)
    velocity = jax.vmap(evaluate)(targets, centre, sources_all, extra, moments)
    return velocity[None, None]


def solution(mesh):
    placed = (
        P("gx", "gy", None, None, None),
        P("gx", "gy", None, None, None),
        P("gx", "gy", None, None),
        P(),
        P(),
        P("gx", "gy", None, None),
        P("gx", "gy", None, None),
    )
    return jax.shard_map(
        local,
        mesh=mesh,
        in_specs=placed,
        out_specs=P("gx", "gy", None, None, None),
        check_vma=False,
    )
```

```python
import math

import jax
import jax.numpy as jnp
import numpy as np
from jax import lax
from jax.experimental.layout import Layout, with_layout_constraint
from jax.sharding import PartitionSpec as P

MOVE = 8


inv_four_pi = 0.25 / math.pi


def from_partner(shard, axis, apart):
    return lax.ppermute(shard, axis, [(i, i ^ 1 << apart) for i in range(lax.axis_size(axis))])


def swapped(shard, axis, dim=0):
    size = lax.axis_size(axis)
    first = [(i, i ^ 1) for i in range(size)]
    second = [(i, i + 1 - 2 * (i % 2 == 0)) for i in range(1, size - 1)]
    return jnp.concatenate([lax.ppermute(shard, axis, first), shard, lax.ppermute(shard, axis, second)], axis=dim)


def slot_multipoles(pos, stren, core):
    lanes = pos.shape[-1]
    ones = jnp.ones((lanes,), jnp.float32)
    exact = lax.Precision.HIGHEST
    rough = jnp.einsum("scl,l->sc", pos, ones, precision=exact) / lanes
    centre = rough + jnp.einsum("scl,l->sc", pos - rough[:, :, None], ones, precision=exact) / lanes
    total = jnp.einsum("scl,l->sc", stren, ones, precision=exact)
    offset = pos - centre[:, :, None]
    spread = (
        jnp.einsum("sl,l->s", core * core, ones, precision=exact) / lanes
        + jnp.sum(jnp.einsum("scl,l->sc", offset * offset, ones, precision=exact), axis=1) / lanes
    )
    return jnp.concatenate([centre, total, spread[:, None]], axis=1)


def evaluate(target, centre, sources, extra, moments):
    sep_x = target[0][None, :, None] - sources[0][:, None, :]
    sep_y = target[1][None, :, None] - sources[1][:, None, :]
    sep_z = target[2][None, :, None] - sources[2][:, None, :]
    radius_sq = sep_x * sep_x + sep_y * sep_y + sep_z * sep_z + extra[0][:, None, :]
    inverse = lax.rsqrt(radius_sq)
    weight = inverse * inverse * inverse
    sum_x = jnp.sum(sources[3][:, None, :] * weight, axis=(0, 2))
    sum_y = jnp.sum(sources[4][:, None, :] * weight, axis=(0, 2))
    sum_z = jnp.sum(sources[5][:, None, :] * weight, axis=(0, 2))
    arm_x = jnp.sum(extra[1][:, None, :] * weight, axis=(0, 2))
    arm_y = jnp.sum(extra[2][:, None, :] * weight, axis=(0, 2))
    arm_z = jnp.sum(extra[3][:, None, :] * weight, axis=(0, 2))
    rel_x = target[0] - centre[0]
    rel_y = target[1] - centre[1]
    rel_z = target[2] - centre[2]
    near_x = sum_y * rel_z - sum_z * rel_y - arm_x
    near_y = sum_z * rel_x - sum_x * rel_z - arm_y
    near_z = sum_x * rel_y - sum_y * rel_x - arm_z
    off_x = target[0][None, :] - moments[:, 0][:, None]
    off_y = target[1][None, :] - moments[:, 1][:, None]
    off_z = target[2][None, :] - moments[:, 2][:, None]
    far_sq = off_x * off_x + off_y * off_y + off_z * off_z + moments[:, 6][:, None]
    far_inverse = lax.rsqrt(far_sq)
    far_weight = far_inverse * far_inverse * far_inverse
    mom_x = moments[:, 3][:, None] * far_weight
    mom_y = moments[:, 4][:, None] * far_weight
    mom_z = moments[:, 5][:, None] * far_weight
    far_x = jnp.sum(mom_y * off_z - mom_z * off_y, axis=0)
    far_y = jnp.sum(mom_z * off_x - mom_x * off_z, axis=0)
    far_z = jnp.sum(mom_x * off_y - mom_y * off_x, axis=0)
    return jnp.stack([near_x + far_x, near_y + far_y, near_z + far_z], axis=0) * inv_four_pi


def source_terms(sources_all, centre):
    px = sources_all[0] - centre[:, 0][:, None, None]
    py = sources_all[1] - centre[:, 1][:, None, None]
    pz = sources_all[2] - centre[:, 2][:, None, None]
    sx, sy, sz = sources_all[3], sources_all[4], sources_all[5]
    core_sq = sources_all[6] * sources_all[6]
    extra = jnp.stack([core_sq, sy * pz - sz * py, sz * px - sx * pz, sx * py - sy * px], axis=0)
    return lax.optimization_barrier(extra)


def trace_back(loc, moves, levels, bits_x, nbd):
    size_x, size_y = moves.shape[1], moves.shape[2]
    devices = size_x * size_y
    level_bit = np.array(
        [(1 << bits_x - 1 - level) * size_y if level < bits_x else 1 << levels - 1 - level for level in range(levels)],
        np.int32,
    )
    flat = moves.reshape(levels, devices)
    every = jnp.arange(devices, dtype=jnp.int32)
    swap = jnp.bitwise_xor(every[None, :, None], level_bit[:, None, None]) == every[None, None, :]
    mate_moves = jnp.sum(jnp.where(swap, flat[:, None, :], 0), axis=2)
    delta = flat - mate_moves
    before = nbd + jnp.sum(delta, axis=0)
    kept = []
    for level in range(levels):
        kept.append(before - flat[level])
        before = before - delta[level]
    kept = jnp.stack(kept, axis=0)
    kept_mate = jnp.sum(jnp.where(swap, kept[:, None, :], 0), axis=2)
    device = loc.reshape(-1) // nbd
    slot = loc.reshape(-1) % nbd
    for level in reversed(range(levels)):
        pick = device[:, None] == every[None, :]
        here = jnp.sum(jnp.where(pick, kept[level][None, :], 0), axis=1)
        there = jnp.sum(jnp.where(pick, kept_mate[level][None, :], 0), axis=1)
        moved = slot >= here
        slot = jnp.where(moved, slot - here + there, slot)
        device = jnp.where(moved, jnp.bitwise_xor(device, level_bit[level]), device)
    return device.reshape(loc.shape), slot.reshape(loc.shape)


def table_blocks(table, lanes):
    cap, width = table.shape
    pieces = -(-cap // lanes)
    wide = jnp.pad(table.T, ((0, 0), (0, pieces * lanes - cap)))
    return wide.reshape(width, pieces, lanes).transpose(1, 0, 2)


def local(positions, strength, core, moves, owner, near_list, far_list):
    column_index = lax.axis_index("gx")
    row_index = lax.axis_index("gy")
    size_x = lax.axis_size("gx")
    size_y = lax.axis_size("gy")
    bits_x = size_x.bit_length() - 1
    levels = moves.shape[0]
    cap = positions.shape[2]
    nbd = near_list.shape[2]
    lanes = positions.shape[4]
    me = column_index * size_y + row_index
    held = jnp.concatenate([positions[0, 0], strength[0, 0], core[0, 0][:, None, :]], axis=1)
    held = lax.optimization_barrier(held)
    slot_table = slot_multipoles(held[:, 0:3], held[:, 3:6], held[:, 6])
    width = slot_table.shape[1]
    gathered = table_blocks(slot_table, lanes)
    pieces = gathered.shape[0]
    far_where = owner[far_list[0, 0]]
    far_device, far_slot = trace_back(far_where, moves, levels, bits_x, nbd)
    held = jnp.pad(held, ((0, MOVE), (0, 0), (0, 0)))
    plans = []
    level_bits = []
    for level in range(levels):
        if level < bits_x:
            bit_at = bits_x - 1 - level
            mate_moves = moves[level, jnp.bitwise_xor(column_index, 1 << bit_at), row_index]
            level_bits.append((1 << bit_at) * size_y)
        else:
            bit_at = levels - 1 - level
            mate_moves = moves[level, column_index, jnp.bitwise_xor(row_index, 1 << bit_at)]
            level_bits.append(1 << bit_at)
        plans.append((bit_at, moves[level, column_index, row_index], mate_moves))
    count = jnp.int32(nbd)
    for plan_item in plans:
        count = count + plan_item[1] - plan_item[2]
    for level in range(levels):
        bit_at, own_moves, mate_moves = plans[level]
        leaving = lax.dynamic_slice_in_dim(held, count - own_moves, MOVE, 0)
        payload = jnp.concatenate([leaving, gathered], axis=0)
        if level < bits_x:
            got = from_partner(payload, "gx", bit_at)
        else:
            got = from_partner(payload, "gy", bit_at)
        arriving = got[:MOVE]
        gathered = jnp.concatenate([gathered, got[MOVE:]], axis=0)
        count = count - own_moves
        held = lax.dynamic_update_slice_in_dim(held, arriving, count, 0)
        count = count + mate_moves
    blocks = held[:nbd]
    relative = jnp.bitwise_xor(far_device, me)
    entry = jnp.zeros_like(relative)
    for level in range(levels):
        entry = entry + ((relative // level_bits[level]) % 2) * (1 << level)
    all_table = gathered.reshape(-1, pieces, width, lanes).transpose(0, 1, 3, 2).reshape(-1, width)
    moments = all_table[entry * (pieces * lanes) + far_slot]
    near_where = owner[near_list[0, 0]]
    source_device = near_where // nbd
    source_slot = near_where % nbd
    delta_x = source_device // size_y - column_index
    delta_y = source_device % size_y - row_index
    sign_x = 2 * (column_index % 2) - 1
    sign_y = 2 * (row_index % 2) - 1
    dense = with_layout_constraint(jnp.transpose(blocks, (1, 0, 2)), Layout(major_to_minor=(0, 1, 2)))
    source_pool = swapped(swapped(dense, "gx", 1), "gy", 1)
    pool_index = ((1 + delta_y * sign_y) * 3 + (1 + delta_x * sign_x)) * nbd + source_slot
    sources_all = source_pool[:, pool_index]
    targets = blocks[:, 0:3]
    centre = jnp.mean(targets, axis=2)
    extra = source_terms(sources_all, centre)
    velocity = jax.vmap(evaluate, in_axes=(0, 0, 1, 1, 0))(targets, centre, sources_all, extra, moments)
    return velocity[None, None]


def solution(mesh):
    placed = (
        P("gx", "gy", None, None, None),
        P("gx", "gy", None, None, None),
        P("gx", "gy", None, None),
        P(),
        P(),
        P("gx", "gy", None, None),
        P("gx", "gy", None, None),
    )
    return jax.shard_map(
        local,
        mesh=mesh,
        in_specs=placed,
        out_specs=P("gx", "gy", None, None, None),
        check_vma=False,
    )
```
